256 devices in a mesh: req: 4 (over x), seq: 8 (over z_lo, y), tp: 8 (over z_hi, core).
Axes of the slice: x: 4, y: 4, z: 8 (z_hi: 4, z_lo: 2; z = z_hi * 2 + z_lo), core: 2. Of those that a mesh axis runs over, the one named last changes fastest.
Arguments:
- img_hidden: bfloat16 [16384, 3072], P(('req', 'seq'), 'tp'), parts along dimension 0, may hold values from -6 to 6
- txt_hidden: bfloat16 [2048, 3072], P(('req', 'seq'), 'tp'), parts along dimension 0, may hold values from -6 to 6
- img_mod: bfloat16 [12, 3072], P('req'), parts along dimension 0, may hold values from -3 to 3
- txt_mod: bfloat16 [12, 3072], P('req'), parts along dimension 0, may hold values from -3 to 3
- img_qkv: bfloat16 [3072, 3, 3072], P('seq', None, 'tp')
- txt_qkv: bfloat16 [3072, 3, 3072], P('seq', None, 'tp'), may hold values from -0.109375 to 0.109375
- qk_gains: float32 [4, 128], replicated, may hold values from 0.5 to 4.5, as said below
- img_out_w: bfloat16 [3072, 3072], P('tp', 'seq'), may hold values from -0.109375 to 0.109375
- txt_out_w: bfloat16 [3072, 3072], P('tp', 'seq'), may hold values from -0.109375 to 0.109375
- final_mod: bfloat16 [8, 3072], P('req'), parts along dimension 0, may hold values from -3 to 3
- final_w: bfloat16 [3072, 64], P('tp'), may hold values from -0.109375 to 0.109375
- conv_w: bfloat16 [3, 3, 64, 64], replicated, may hold values from -0.25 to 0.25
- latent: float32 [256, 4096], P(('req', 'seq'), 'tp'), parts along dimension 0, may hold values from -6 to 6
- text_len: int32 [4], P('req'), parts along dimension 0, may hold values from 1 to 512
- step_index: int32 [4], P('req'), parts along dimension 0, may hold values from 0 to 27
Outputs:
- img_next: bfloat16 [16384, 3072], P(('req', 'seq'), 'tp'), parts along dimension 0
- txt_next: bfloat16 [2048, 3072], P(('req', 'seq'), 'tp'), parts along dimension 0
- velocity: float32 [256, 4096], P(('req', 'seq'), 'tp'), parts along dimension 0
- latent_next: float32 [256, 4096], P(('req', 'seq'), 'tp'), parts along dimension 0
- denoised: float32 [256, 4096], P(('req', 'seq'), 'tp'), parts along dimension 0
The draws below stay inside these ranges and needn't reach their ends.
There are 4 independent parts, one for each index of `req`. The reference program is written for one: setup_inputs(seed, part) draws one part's arguments, and reference() takes and returns one part's arrays. A program takes and returns all parts, laid end to end along the dimension named above; an argument that names none is the same for every part. Nothing has to cross between parts.
Inputs may be any that keep to these rules, and one draw needn't show every extreme that they name: `qk_gains`: positive gains.
All inputs are finite; a program needn't handle non-finite values.
Results may differ from the reference program's by a relative error of at most 0.014.
Values may be sent and summed in bfloat16 or wider, within the bound.
No kernel may reach another device: no remote copies, remote signals or barrier semaphores. Data moves between devices by JAX's collectives and lax.ppermute only.
A program may use at most 128 MiB of HBM per device.

```python
import math
import jax
import jax.numpy as jnp
from jax import lax

D = 3072
HD = 128
CH = 64
STEPS = 28
GRID = 64
IMG = 4096
TXT = 512
N_TP = 8


def draw_img_hidden(key, part):
    position = jnp.arange(D, dtype=jnp.float32) / (D - 1)
    col_scale = jnp.exp(math.log(0.4) + position * math.log(5.0))
    picked = jnp.clip(jax.random.normal(key, (IMG, D), jnp.float32), -3.0, 3.0)
    return (picked * col_scale[None, :]).astype(jnp.bfloat16)


def draw_img_qkv(key, part):
    base = jax.random.normal(key, (D, 3, D), jnp.float32) * D ** (-0.5)
    return base.astype(jnp.bfloat16)


def draw_qk_gains(key, part):
    lower = math.log(0.5)
    upper = math.log(2.0)
    picked = jax.random.uniform(key, (4, HD), jnp.float32)
    return jnp.exp(lower + picked * (upper - lower))


def block_scale(own_key, dims, cuts, low, largest):
    def one(dim, parts):
        steps = jax.random.uniform(jax.random.fold_in(jax.random.fold_in(own_key, 6), dim), (parts,), jnp.float32, low / len(cuts), largest / len(cuts))
        return jnp.repeat(jnp.exp(steps), dims[dim] // parts).reshape((-1,) + (1,) * (len(dims) - dim - 1))

    gain = one(*cuts[0])
    for cut in cuts[1:]:
        gain = gain * one(*cut)
    return gain


def centred(stream_key, dims, deviation, most, pieces=(), held_as=jnp.bfloat16):
    drawn = jax.random.normal(stream_key, dims, jnp.float32) * deviation
    if len(pieces) > 0:
        drawn = block_scale(stream_key, dims, pieces, -0.22, 0.18) * drawn
    return jnp.clip(drawn, min=-most, max=most).astype(held_as)


def setup_inputs(seed: int = 0, part: int = 0) -> dict:
    streams_of = jax.random.split(jax.random.key(seed), 16)
    own_keys = jax.random.split(jax.random.fold_in(streams_of[15], part), 16)
    return {
        "img_hidden": draw_img_hidden(jax.random.fold_in(jax.random.fold_in(streams_of[15], part), 71), part),
        "txt_hidden": centred(own_keys[1], (TXT, D), 1.0, 6.0, ((0, 8), (1, 8))),
        "img_mod": centred(own_keys[2], (3, D), 0.5, 3.0),
        "txt_mod": centred(own_keys[3], (3, D), 0.5, 3.0),
        "img_qkv": draw_img_qkv(jax.random.fold_in(streams_of[15], 71), part),
        "txt_qkv": centred(streams_of[5], (D, 3, D), D ** -0.5, 0.109375, ((0, 8), (2, 8))),
        "qk_gains": draw_qk_gains(jax.random.fold_in(streams_of[15], 71), part),
        "img_out_w": centred(streams_of[7], (D, D), D ** -0.5, 0.109375, ((0, 8), (1, 8))),
        "txt_out_w": centred(streams_of[8], (D, D), D ** -0.5, 0.109375, ((0, 8), (1, 8))),
        "final_mod": centred(own_keys[9], (2, D), 0.5, 3.0),
        "final_w": centred(streams_of[10], (D, CH), D ** -0.5, 0.109375, ((0, 8),)),
        "conv_w": centred(streams_of[11], (3, 3, CH, CH), (9 * CH) ** -0.5, 0.25),
        "latent": centred(own_keys[12], (GRID, GRID * CH), 1.0, 6.0, ((0, 8), (1, 8)), jnp.float32),
        "text_len": jax.random.randint(own_keys[13], (1,), 1, TXT + 1).astype(jnp.int32),
        "step_index": jax.random.randint(own_keys[14], (1,), 0, STEPS).astype(jnp.int32),
    }


EPS = 1e-06
SHIFT_MU = 1.15
THETA = 10000.0

def modulate(hidden, mod_rows):
    values = hidden.astype(jnp.float32)
    mod_f = mod_rows.astype(jnp.float32)
    row_mean = lax.optimization_barrier(jnp.mean(values, -1, keepdims=True))
    row_var = lax.optimization_barrier(jnp.mean((values - row_mean) ** 2, -1, keepdims=True))
    normed = (values - row_mean) * lax.rsqrt(row_var + EPS)
    return (normed * (1.0 + mod_f[1]) + mod_f[0]).astype(jnp.bfloat16)

def rms_gain(values, gain_row):
    return values * lax.rsqrt(lax.optimization_barrier(jnp.mean(values * values, -1, keepdims=True)) + EPS) * gain_row

def rope_angles(row_pos, col_pos, head_dim):
    lead = head_dim // 16
    span = 7 * head_dim // 32
    freq = THETA ** (-jnp.arange(span, dtype=jnp.float32) / span)
    zero_part = jnp.zeros((row_pos.shape[0], lead), jnp.float32)
    return jnp.concatenate([zero_part, row_pos[:, None] * freq[None], col_pos[:, None] * freq[None]], 1)

def apply_rope(values, angles):
    count, heads_n, head_dim = values.shape
    pairs = values.reshape(count, heads_n, head_dim // 2, 2)
    first = pairs[..., 0]
    second = pairs[..., 1]
    cosine = jnp.cos(angles)[:, None, :]
    sine = jnp.sin(angles)[:, None, :]
    turned = jnp.stack([first * cosine - second * sine, first * sine + second * cosine], -1)
    return turned.reshape(values.shape)

def split_heads(mixed, gain_q, gain_k, angles):
    head_dim = gain_q.shape[0]
    shaped = mixed.reshape(mixed.shape[0], 3, -1, head_dim)
    query = rms_gain(shaped[:, 0], gain_q)
    keyed = rms_gain(shaped[:, 1], gain_k)
    if angles is not None:
        query = apply_rope(query, angles)
        keyed = apply_rope(keyed, angles)
    return (query.astype(jnp.bfloat16), keyed.astype(jnp.bfloat16), shaped[:, 2].astype(jnp.bfloat16))

def noise_level(tval):
    factor = math.exp(SHIFT_MU)
    return factor * tval / (factor * tval + 1.0 - tval)

def project_out(attn, weight):
    group = D // N_TP
    summed = jnp.zeros((attn.shape[0], weight.shape[1]), jnp.float32)
    for index in range(N_TP):
        partial_term = jnp.dot(attn[:, index * group:(index + 1) * group], weight[index * group:(index + 1) * group], preferred_element_type=jnp.float32)
        rounded = lax.optimization_barrier(partial_term.astype(jnp.bfloat16))
        summed = summed + rounded.astype(jnp.float32)
    return summed

def reference(img_hidden, txt_hidden, img_mod, txt_mod, img_qkv, txt_qkv, qk_gains, img_out_w, txt_out_w, final_mod, final_w, conv_w, latent, text_len, step_index):
    gains = qk_gains.astype(jnp.float32)
    img_norm = modulate(img_hidden, img_mod)
    txt_norm = modulate(txt_hidden, txt_mod)
    img_mixed = jnp.dot(img_norm, img_qkv.reshape(D, 3 * D), preferred_element_type=jnp.float32)
    txt_mixed = jnp.dot(txt_norm, txt_qkv.reshape(D, 3 * D), preferred_element_type=jnp.float32)
    token_ids = jnp.arange(IMG, dtype=jnp.int32)
    row_pos = (token_ids // GRID).astype(jnp.float32)
    col_pos = (token_ids % GRID).astype(jnp.float32)
    angles = rope_angles(row_pos, col_pos, HD)
    img_query, img_key, img_value = split_heads(img_mixed, gains[0], gains[1], angles)
    txt_query, txt_key, txt_value = split_heads(txt_mixed, gains[2], gains[3], None)
    queries = jnp.concatenate([txt_query, img_query], 0).transpose(1, 0, 2)
    keys_all = jnp.concatenate([txt_key, img_key], 0).transpose(1, 0, 2)
    values_all = jnp.concatenate([txt_value, img_value], 0).transpose(1, 0, 2)
    positions = jnp.arange(TXT + IMG, dtype=jnp.int32)
    usable = (positions >= TXT) | (positions < text_len[0])
    score_scale = HD ** (-0.5)

    def one_head(operands):
        head_q, head_k, head_v = operands
        scores = jnp.dot(head_q, head_k.T, preferred_element_type=jnp.float32) * score_scale
        scores = jnp.where(usable[None, :], scores, -1e+30)
        peak = lax.optimization_barrier(jnp.max(scores, -1, keepdims=True))
        weights = jnp.exp(scores - peak)
        summed = lax.optimization_barrier(jnp.sum(weights, -1, keepdims=True))
        mixed_v = jnp.dot(weights.astype(jnp.bfloat16), head_v, preferred_element_type=jnp.float32)
        return (mixed_v / summed).astype(jnp.bfloat16)
    heads_out = lax.map(one_head, (queries, keys_all, values_all))
    attn = heads_out.transpose(1, 0, 2).reshape(TXT + IMG, D)
    txt_out = project_out(attn[:TXT], txt_out_w)
    img_out = project_out(attn[TXT:], img_out_w)
    img_next = (img_hidden.astype(jnp.float32) + img_mod.astype(jnp.float32)[2] * img_out).astype(jnp.bfloat16)
    text_valid = jnp.arange(TXT, dtype=jnp.int32) < text_len[0]
    txt_base = txt_hidden.astype(jnp.float32)
    txt_next = jnp.where(text_valid[:, None], txt_base + txt_mod.astype(jnp.float32)[2] * txt_out, txt_base).astype(jnp.bfloat16)
    final_f = final_mod.astype(jnp.float32)
    values = img_next.astype(jnp.float32)
    row_mean = lax.optimization_barrier(jnp.mean(values, -1, keepdims=True))
    row_sq = lax.optimization_barrier(jnp.mean(values * values, -1, keepdims=True))
    row_var = row_sq - row_mean * row_mean
    normed = (values - row_mean) * lax.rsqrt(row_var + EPS) * (1.0 + final_f[1]) + final_f[0]
    patch = jnp.dot(normed, final_w.astype(jnp.float32), precision=lax.Precision.HIGHEST).astype(jnp.bfloat16)
    framed = jnp.pad(patch.reshape(GRID, GRID, CH), ((1, 1), (1, 1), (0, 0)))
    velocity = jnp.zeros((GRID, GRID, CH), jnp.float32)
    for row_shift in range(3):
        for col_shift in range(3):
            window = framed[row_shift:row_shift + GRID, col_shift:col_shift + GRID].astype(jnp.float32)
            velocity = velocity + jnp.einsum('rci,io->rco', window, conv_w[row_shift, col_shift].astype(jnp.float32), precision=lax.Precision.HIGHEST)
    velocity_flat = velocity.reshape(GRID, GRID * CH)
    step_f = step_index[0].astype(jnp.float32)
    t_now = 1.0 - step_f / STEPS
    t_after = 1.0 - (step_f + 1.0) / STEPS
    delta = noise_level(t_after) - noise_level(t_now)
    latent_next = latent + delta * velocity_flat
    denoised = latent - noise_level(t_now) * velocity_flat
    return (img_next, txt_next, velocity_flat, latent_next, denoised)
```

```python
import math

import jax
import jax.numpy as jnp
from jax import lax
from jax.sharding import PartitionSpec as P

STEPS = 28


EPS = 1e-06
SHIFT_MU = 1.15
THETA = 10000.0


def extended(block, sides, width):
    for axis, dim in sides:
        count = lax.axis_size(axis)
        forward = [(i, i + 1) for i in range(count - 1)]
        backward = [(target, source) for source, target in forward]
        low = lax.ppermute(
            lax.slice_in_dim(block, block.shape[dim] - width, None, axis=dim), axis, forward
        )
        high = lax.ppermute(lax.slice_in_dim(block, 0, width, axis=dim), axis, backward)
        block = jnp.concatenate([low, block, high], axis=dim)
    return block


def modulate(hidden, mod_rows):
    values = hidden.astype(jnp.float32)
    mod_f = mod_rows.astype(jnp.float32)
    row_mean = jnp.mean(values, -1, keepdims=True)
    row_var = jnp.mean((values - row_mean) ** 2, -1, keepdims=True)
    normed = (values - row_mean) * lax.rsqrt(row_var + EPS)
    return (normed * (1.0 + mod_f[1]) + mod_f[0]).astype(jnp.bfloat16)


def rms_gain(values, gain_row):
    return values * lax.rsqrt(jnp.mean(values * values, -1, keepdims=True) + EPS) * gain_row


def rope_angles(row_pos, col_pos, head_dim):
    lead = head_dim // 16
    span = 7 * head_dim // 32
    freq = THETA ** (-jnp.arange(span, dtype=jnp.float32) / span)
    zero_part = jnp.zeros((row_pos.shape[0], lead), jnp.float32)
    return jnp.concatenate(
        [zero_part, row_pos[:, None] * freq[None], col_pos[:, None] * freq[None]], 1
    )


def apply_rope(values, angles):
    count, heads_n, head_dim = values.shape
    pairs = values.reshape(count, heads_n, head_dim // 2, 2)
    first = pairs[..., 0]
    second = pairs[..., 1]
    cosine = jnp.cos(angles)[:, None, :]
    sine = jnp.sin(angles)[:, None, :]
    turned = jnp.stack([first * cosine - second * sine, first * sine + second * cosine], -1)
    return turned.reshape(values.shape)


def split_heads(mixed, gain_q, gain_k, angles):
    head_dim = gain_q.shape[0]
    shaped = mixed.reshape(mixed.shape[0], 3, -1, head_dim)
    query = rms_gain(shaped[:, 0], gain_q)
    keyed = rms_gain(shaped[:, 1], gain_k)
    if angles is not None:
        query = apply_rope(query, angles)
        keyed = apply_rope(keyed, angles)
    return (
        query.astype(jnp.bfloat16),
        keyed.astype(jnp.bfloat16),
        shaped[:, 2].astype(jnp.bfloat16),
    )


def noise_level(tval):
    factor = math.exp(SHIFT_MU)
    return factor * tval / (factor * tval + 1.0 - tval)


def add_rows(normed, piece):
    flat_piece = piece.reshape(piece.shape[0], piece.shape[1] * piece.shape[2])
    return jnp.dot(normed, flat_piece, preferred_element_type=jnp.float32)


def per_device(
    img_hidden,
    txt_hidden,
    img_mod,
    txt_mod,
    img_qkv,
    txt_qkv,
    qk_gains,
    img_out_w,
    txt_out_w,
    final_mod,
    final_w,
    conv_w,
    latent,
    text_len,
    step_index,
):
    seq_count = lax.axis_size("seq")
    seq_at = lax.axis_index("seq")
    tp_at = lax.axis_index("tp")
    img_rows = img_hidden.shape[0]
    txt_rows = txt_hidden.shape[0]
    local_width = img_hidden.shape[1]
    img_full, txt_full = (
        lax.all_gather(img_hidden, "tp", axis=1, tiled=True),
        lax.all_gather(txt_hidden, "tp", axis=1, tiled=True),
    )
    full_width = img_full.shape[1]
    img_norm = modulate(img_full, img_mod)
    txt_norm = modulate(txt_full, txt_mod)
    img_mixed = add_rows(img_norm, lax.all_gather(img_qkv, "seq", axis=0, tiled=True))
    txt_norm_rows = lax.all_to_all(txt_norm, "seq", 1, 0, tiled=True)
    txt_mixed = lax.psum_scatter(
        add_rows(txt_norm_rows, txt_qkv), "seq", scatter_dimension=0, tiled=True
    )
    head_dim = qk_gains.shape[1]
    grid_side = latent.shape[0] * seq_count
    token_ids = seq_at * img_rows + jnp.arange(img_rows, dtype=jnp.int32)
    row_pos = (token_ids // grid_side).astype(jnp.float32)
    col_pos = (token_ids % grid_side).astype(jnp.float32)
    angles = rope_angles(row_pos, col_pos, head_dim)
    img_query, img_key, img_value = split_heads(img_mixed, qk_gains[0], qk_gains[1], angles)
    txt_query, txt_key, txt_value = split_heads(txt_mixed, qk_gains[2], qk_gains[3], None)
    local_len = txt_rows + img_rows
    heads_local = img_query.shape[1]
    queries = jnp.concatenate([txt_query, img_query], 0)
    keys_local = jnp.concatenate([txt_key, img_key], 0).reshape(local_len, heads_local * head_dim)
    values_local = jnp.concatenate([txt_value, img_value], 0).reshape(
        local_len, heads_local * head_dim
    )
    limit = text_len[0]
    score_scale = head_dim ** (-0.5)
    start_state = (
        jnp.full((heads_local, local_len), -1e30, jnp.float32),
        jnp.zeros((heads_local, local_len), jnp.float32),
        jnp.zeros((heads_local, local_len, head_dim), jnp.float32),
    )
    key_piece = lax.all_gather(keys_local, "seq", axis=0, tiled=True)
    value_piece = lax.all_gather(values_local, "seq", axis=0, tiled=True)
    blocks = key_piece.shape[0] // local_len

    def advance(block, state):
        peak, running, accum = state
        key_block = lax.dynamic_slice_in_dim(key_piece, block * local_len, local_len, 0).reshape(
            local_len, heads_local, head_dim
        )
        value_block = lax.dynamic_slice_in_dim(
            value_piece, block * local_len, local_len, 0
        ).reshape(local_len, heads_local, head_dim)
        within = jnp.arange(local_len, dtype=jnp.int32)
        text_pos = block * txt_rows + within
        usable = (within >= txt_rows) | (text_pos < limit)
        scores = (
            jnp.einsum("qhd,khd->hqk", queries, key_block, preferred_element_type=jnp.float32)
            * score_scale
        )
        scores = jnp.where(usable[None, None, :], scores, -1e30)
        new_peak = jnp.maximum(peak, jnp.max(scores, -1))
        rescale = jnp.exp(peak - new_peak)
        weights = jnp.exp(scores - new_peak[..., None])
        running = running * rescale + jnp.sum(weights, -1)
        accum = accum * rescale[..., None] + jnp.einsum(
            "hqk,khd->hqd",
            weights.astype(jnp.bfloat16),
            value_block,
            preferred_element_type=jnp.float32,
        )
        return (new_peak, running, accum)

    peak, running, accum = lax.fori_loop(0, blocks, advance, start_state)
    attn = (
        (accum / running[..., None])
        .astype(jnp.bfloat16)
        .transpose(1, 0, 2)
        .reshape(local_len, heads_local * head_dim)
    )
    txt_attn = attn[:txt_rows]
    img_attn = attn[txt_rows:]
    img_term = jnp.dot(
        img_attn,
        lax.all_gather(img_out_w, "seq", axis=1, tiled=True),
        preferred_element_type=jnp.float32,
    )
    txt_term = jnp.dot(
        lax.all_gather(txt_attn, "seq", axis=0, tiled=True),
        txt_out_w,
        preferred_element_type=jnp.float32,
    )
    txt_part = lax.psum_scatter(
        txt_term.astype(jnp.bfloat16).astype(jnp.float32), "tp", scatter_dimension=0, tiled=True
    )
    side = lax.axis_size("tp")
    swap = [(a * side + b, b * side + a) for a in range(side) for b in range(side)]
    txt_out = lax.ppermute(txt_part, ("seq", "tp"), swap)
    img_out = lax.psum_scatter(
        img_term.astype(jnp.bfloat16), "tp", scatter_dimension=1, tiled=True
    ).astype(jnp.float32)
    img_gate = lax.dynamic_slice_in_dim(
        img_mod.astype(jnp.float32)[2], tp_at * local_width, local_width
    )
    txt_gate = lax.dynamic_slice_in_dim(
        txt_mod.astype(jnp.float32)[2], tp_at * local_width, local_width
    )
    img_next = (img_hidden.astype(jnp.float32) + img_gate * img_out).astype(jnp.bfloat16)
    text_valid = seq_at * txt_rows + jnp.arange(txt_rows, dtype=jnp.int32) < limit
    txt_base = txt_hidden.astype(jnp.float32)
    txt_next = jnp.where(text_valid[:, None], txt_base + txt_gate * txt_out, txt_base).astype(
        jnp.bfloat16
    )
    shift_row = lax.dynamic_slice_in_dim(final_mod[0], tp_at * local_width, local_width)
    scale_row = lax.dynamic_slice_in_dim(final_mod[1], tp_at * local_width, local_width)
    final_shift = shift_row.astype(jnp.float32)
    final_scale = scale_row.astype(jnp.float32)
    weight_final = final_w.astype(jnp.float32)
    values = img_next.astype(jnp.float32)
    channels = final_w.shape[1]
    final_gain = 1.0 + final_scale
    high = lax.Precision.HIGHEST
    lifted = jnp.dot(values * final_gain, weight_final, precision=high)
    consts = jnp.stack(
        [jnp.dot(final_gain, weight_final, precision=high), jnp.dot(final_shift, weight_final, precision=high)]
    )
    packed = jnp.concatenate(
        [
            jnp.concatenate([lifted, jnp.sum(values, -1)[:, None], jnp.sum(values * values, -1)[:, None]], 1),
            jnp.pad(consts, ((0, 0), (0, 2))),
        ],
        0,
    )
    packed = lax.psum(packed, "tp")
    lifted = packed[:img_rows, :channels]
    row_mean = packed[:img_rows, channels] / full_width
    row_var = packed[:img_rows, channels + 1] / full_width - row_mean * row_mean
    row_scale = lax.rsqrt(row_var + EPS)[:, None]
    patch = row_scale * (lifted - row_mean[:, None] * packed[img_rows, :channels]) + packed[
        img_rows + 1, :channels
    ]
    band_rows = latent.shape[0]
    patch_band = patch.astype(jnp.bfloat16).reshape(band_rows, grid_side * channels)
    rimmed = extended(patch_band, (("seq", 0),), 1)
    col_width = latent.shape[1] // channels
    framed = jnp.pad(rimmed.reshape(band_rows + 2, grid_side, channels), ((0, 0), (1, 1), (0, 0)))
    window = lax.dynamic_slice_in_dim(framed, tp_at * col_width, col_width + 2, 1)
    velocity = jnp.zeros((band_rows, col_width, channels), jnp.float32)
    for row_shift in range(3):
        for col_shift in range(3):
            velocity = velocity + jnp.einsum(
                "rci,io->rco",
                window[row_shift : row_shift + band_rows, col_shift : col_shift + col_width],
                conv_w[row_shift, col_shift],
                preferred_element_type=jnp.float32,
            )
    velocity_flat = velocity.reshape(band_rows, col_width * channels)
    step_f = step_index[0].astype(jnp.float32)
    t_now = 1.0 - step_f / STEPS
    t_after = 1.0 - (step_f + 1.0) / STEPS
    delta = noise_level(t_after) - noise_level(t_now)
    latent_next = latent + delta * velocity_flat
    denoised = latent - noise_level(t_now) * velocity_flat
    return (img_next, txt_next, velocity_flat, latent_next, denoised)


def solution(mesh):
    placed = (
        P(("req", "seq"), "tp"),
        P(("req", "seq"), "tp"),
        P("req", None),
        P("req", None),
        P("seq", None, "tp"),
        P("seq", None, "tp"),
        P(),
        P("tp", "seq"),
        P("tp", "seq"),
        P("req", None),
        P("tp", None),
        P(),
        P(("req", "seq"), "tp"),
        P("req"),
        P("req"),
    )
    return jax.shard_map(
        per_device,
        mesh=mesh,
        in_specs=placed,
        out_specs=(
            P(("req", "seq"), "tp"),
            P(("req", "seq"), "tp"),
            P(("req", "seq"), "tp"),
            P(("req", "seq"), "tp"),
            P(("req", "seq"), "tp"),
        ),
        check_vma=False,
    )
```

```python
import math

import jax
import jax.numpy as jnp
from jax import lax
from jax.sharding import PartitionSpec as P

STEPS = 28


EPS = 1e-06
SHIFT_MU = 1.15
THETA = 10000.0


def extended(block, sides, width):
    for axis, dim in sides:
        count = lax.axis_size(axis)
        forward = [(i, i + 1) for i in range(count - 1)]
        backward = [(target, source) for source, target in forward]
        low = lax.ppermute(
            lax.slice_in_dim(block, block.shape[dim] - width, None, axis=dim), axis, forward
        )
        high = lax.ppermute(lax.slice_in_dim(block, 0, width, axis=dim), axis, backward)
        block = jnp.concatenate([low, block, high], axis=dim)
    return block


def tree_sum(block, axis):
    count = lax.axis_size(axis)
    step = 1
    while step < count:
        block = block + lax.ppermute(block, axis, [(i, i ^ step) for i in range(count)])
        step *= 2
    return block


def halving_sum(block, axis, dim):
    count = lax.axis_size(axis)
    at = lax.axis_index(axis)
    step = count // 2
    while step >= 1:
        half = block.shape[dim] // 2
        low = lax.slice_in_dim(block, 0, half, axis=dim)
        high = lax.slice_in_dim(block, half, None, axis=dim)
        upper = (at // step) % 2 == 1
        kept = jnp.where(upper, high, low)
        sent = jnp.where(upper, low, high)
        block = kept + lax.ppermute(sent, axis, [(i, i ^ step) for i in range(count)])
        step //= 2
    return block


def modulate(hidden, mod_rows):
    values = hidden.astype(jnp.float32)
    mod_f = mod_rows.astype(jnp.float32)
    row_mean = jnp.mean(values, -1, keepdims=True)
    row_var = jnp.mean((values - row_mean) ** 2, -1, keepdims=True)
    normed = (values - row_mean) * lax.rsqrt(row_var + EPS)
    return (normed * (1.0 + mod_f[1]) + mod_f[0]).astype(jnp.bfloat16)


def rms_gain(values, gain_row):
    return values * lax.rsqrt(jnp.mean(values * values, -1, keepdims=True) + EPS) * gain_row


def rope_angles(row_pos, col_pos, head_dim):
    lead = head_dim // 16
    span = 7 * head_dim // 32
    freq = THETA ** (-jnp.arange(span, dtype=jnp.float32) / span)
    zero_part = jnp.zeros((row_pos.shape[0], lead), jnp.float32)
    return jnp.concatenate(
        [zero_part, row_pos[:, None] * freq[None], col_pos[:, None] * freq[None]], 1
    )


def apply_rope(values, angles):
    count, heads_n, head_dim = values.shape
    pairs = values.reshape(count, heads_n, head_dim // 2, 2)
    first = pairs[..., 0]
    second = pairs[..., 1]
    cosine = jnp.cos(angles)[:, None, :]
    sine = jnp.sin(angles)[:, None, :]
    turned = jnp.stack([first * cosine - second * sine, first * sine + second * cosine], -1)
    return turned.reshape(values.shape)


def split_heads(mixed, gain_q, gain_k, angles):
    head_dim = gain_q.shape[0]
    shaped = mixed.reshape(mixed.shape[0], 3, -1, head_dim)
    query = rms_gain(shaped[:, 0], gain_q)
    keyed = rms_gain(shaped[:, 1], gain_k)
    if angles is not None:
        query = apply_rope(query, angles)
        keyed = apply_rope(keyed, angles)
    return (
        query.astype(jnp.bfloat16),
        keyed.astype(jnp.bfloat16),
        shaped[:, 2].astype(jnp.bfloat16),
    )


def noise_level(tval):
    factor = math.exp(SHIFT_MU)
    return factor * tval / (factor * tval + 1.0 - tval)


def add_rows(normed, piece):
    flat_piece = piece.reshape(piece.shape[0], piece.shape[1] * piece.shape[2])
    return jnp.dot(normed, flat_piece, preferred_element_type=jnp.float32)


def per_device(
    img_hidden,
    txt_hidden,
    img_mod,
    txt_mod,
    img_qkv,
    txt_qkv,
    qk_gains,
    img_out_w,
    txt_out_w,
    final_mod,
    final_w,
    conv_w,
    latent,
    text_len,
    step_index,
):
    seq_count = lax.axis_size("seq")
    seq_at = lax.axis_index("seq")
    tp_at = lax.axis_index("tp")
    img_rows = img_hidden.shape[0]
    txt_rows = txt_hidden.shape[0]
    local_width = img_hidden.shape[1]
    img_full, txt_full = (
        lax.all_gather(img_hidden, "tp", axis=1, tiled=True),
        lax.all_gather(txt_hidden, "tp", axis=1, tiled=True),
    )
    full_width = img_full.shape[1]
    img_norm = modulate(img_full, img_mod)
    txt_norm = modulate(txt_full, txt_mod)
    img_mixed = add_rows(img_norm, lax.all_gather(img_qkv, "seq", axis=0, tiled=True))
    txt_norm_rows = lax.all_to_all(txt_norm, "seq", 1, 0, tiled=True)
    txt_mixed = lax.psum_scatter(
        add_rows(txt_norm_rows, txt_qkv), "seq", scatter_dimension=0, tiled=True
    )
    head_dim = qk_gains.shape[1]
    grid_side = latent.shape[0] * seq_count
    token_ids = seq_at * img_rows + jnp.arange(img_rows, dtype=jnp.int32)
    row_pos = (token_ids // grid_side).astype(jnp.float32)
    col_pos = (token_ids % grid_side).astype(jnp.float32)
    angles = rope_angles(row_pos, col_pos, head_dim)
    img_query, img_key, img_value = split_heads(img_mixed, qk_gains[0], qk_gains[1], angles)
    txt_query, txt_key, txt_value = split_heads(txt_mixed, qk_gains[2], qk_gains[3], None)
    local_len = txt_rows + img_rows
    heads_local = img_query.shape[1]
    queries = jnp.concatenate([txt_query, img_query], 0)
    keys_local = jnp.concatenate([txt_key, img_key], 0).reshape(local_len, heads_local * head_dim)
    values_local = jnp.concatenate([txt_value, img_value], 0).reshape(
        local_len, heads_local * head_dim
    )
    limit = text_len[0]
    score_scale = head_dim ** (-0.5)
    start_state = (
        jnp.full((heads_local, local_len), -1e30, jnp.float32),
        jnp.zeros((heads_local, local_len), jnp.float32),
        jnp.zeros((heads_local, local_len, head_dim), jnp.float32),
    )
    kv_width = heads_local * head_dim
    kv_piece = lax.all_gather(
        jnp.concatenate([keys_local, values_local], 1), "seq", axis=0, tiled=True
    )
    key_piece = kv_piece[:, :kv_width]
    value_piece = kv_piece[:, kv_width:]
    blocks = key_piece.shape[0] // local_len

    def advance(block, state):
        peak, running, accum = state
        key_block = lax.dynamic_slice_in_dim(key_piece, block * local_len, local_len, 0).reshape(
            local_len, heads_local, head_dim
        )
        value_block = lax.dynamic_slice_in_dim(
            value_piece, block * local_len, local_len, 0
        ).reshape(local_len, heads_local, head_dim)
        within = jnp.arange(local_len, dtype=jnp.int32)
        text_pos = block * txt_rows + within
        usable = (within >= txt_rows) | (text_pos < limit)
        scores = (
            jnp.einsum("qhd,khd->hqk", queries, key_block, preferred_element_type=jnp.float32)
            * score_scale
        )
        scores = jnp.where(usable[None, None, :], scores, -1e30)
        new_peak = jnp.maximum(peak, jnp.max(scores, -1))
        rescale = jnp.exp(peak - new_peak)
        weights = jnp.exp(scores - new_peak[..., None])
        running = running * rescale + jnp.sum(weights, -1)
        accum = accum * rescale[..., None] + jnp.einsum(
            "hqk,khd->hqd",
            weights.astype(jnp.bfloat16),
            value_block,
            preferred_element_type=jnp.float32,
        )
        return (new_peak, running, accum)

    peak, running, accum = lax.fori_loop(0, blocks, advance, start_state)
    attn = (
        (accum / running[..., None])
        .astype(jnp.bfloat16)
        .transpose(1, 0, 2)
        .reshape(local_len, heads_local * head_dim)
    )
    txt_attn = attn[:txt_rows]
    img_attn = attn[txt_rows:]
    img_term = jnp.dot(
        img_attn,
        lax.all_gather(img_out_w, "seq", axis=1, tiled=True),
        preferred_element_type=jnp.float32,
    )
    txt_term = jnp.dot(
        txt_attn,
        lax.all_gather(txt_out_w, "seq", axis=1, tiled=True),
        preferred_element_type=jnp.float32,
    )
    txt_out = halving_sum(txt_term.astype(jnp.bfloat16).astype(jnp.float32), "tp", 1)
    img_out = lax.psum_scatter(
        img_term.astype(jnp.bfloat16), "tp", scatter_dimension=1, tiled=True
    ).astype(jnp.float32)
    img_gate = lax.dynamic_slice_in_dim(
        img_mod.astype(jnp.float32)[2], tp_at * local_width, local_width
    )
    txt_gate = lax.dynamic_slice_in_dim(
        txt_mod.astype(jnp.float32)[2], tp_at * local_width, local_width
    )
    img_next = (img_hidden.astype(jnp.float32) + img_gate * img_out).astype(jnp.bfloat16)
    text_valid = seq_at * txt_rows + jnp.arange(txt_rows, dtype=jnp.int32) < limit
    txt_base = txt_hidden.astype(jnp.float32)
    txt_next = jnp.where(text_valid[:, None], txt_base + txt_gate * txt_out, txt_base).astype(
        jnp.bfloat16
    )
    shift_row = lax.dynamic_slice_in_dim(final_mod[0], tp_at * local_width, local_width)
    scale_row = lax.dynamic_slice_in_dim(final_mod[1], tp_at * local_width, local_width)
    final_shift = shift_row.astype(jnp.float32)
    final_scale = scale_row.astype(jnp.float32)
    weight_final = final_w.astype(jnp.float32)
    values = img_next.astype(jnp.float32)
    channels = final_w.shape[1]
    final_gain = 1.0 + final_scale
    high = lax.Precision.HIGHEST
    lifted = jnp.dot(values * final_gain, weight_final, precision=high)
    consts = jnp.stack(
        [jnp.dot(final_gain, weight_final, precision=high), jnp.dot(final_shift, weight_final, precision=high)]
    )
    packed = jnp.concatenate(
        [
            jnp.concatenate([lifted, jnp.sum(values, -1)[:, None], jnp.sum(values * values, -1)[:, None]], 1),
            jnp.pad(consts, ((0, 0), (0, 2))),
        ],
        0,
    )
    packed = tree_sum(packed, "tp")
    lifted = packed[:img_rows, :channels]
    row_mean = packed[:img_rows, channels] / full_width
    row_var = packed[:img_rows, channels + 1] / full_width - row_mean * row_mean
    row_scale = lax.rsqrt(row_var + EPS)[:, None]
    patch = row_scale * (lifted - row_mean[:, None] * packed[img_rows, :channels]) + packed[
        img_rows + 1, :channels
    ]
    band_rows = latent.shape[0]
    patch_band = patch.astype(jnp.bfloat16).reshape(band_rows, grid_side * channels)
    rimmed = extended(patch_band, (("seq", 0),), 1)
    col_width = latent.shape[1] // channels
    framed = jnp.pad(rimmed.reshape(band_rows + 2, grid_side, channels), ((0, 0), (1, 1), (0, 0)))
    window = lax.dynamic_slice_in_dim(framed, tp_at * col_width, col_width + 2, 1)
    velocity = jnp.zeros((band_rows, col_width, channels), jnp.float32)
    for row_shift in range(3):
        for col_shift in range(3):
            velocity = velocity + jnp.einsum(
                "rci,io->rco",
                window[row_shift : row_shift + band_rows, col_shift : col_shift + col_width],
                conv_w[row_shift, col_shift],
                preferred_element_type=jnp.float32,
            )
    velocity_flat = velocity.reshape(band_rows, col_width * channels)
    step_f = step_index[0].astype(jnp.float32)
    t_now = 1.0 - step_f / STEPS
    t_after = 1.0 - (step_f + 1.0) / STEPS
    delta = noise_level(t_after) - noise_level(t_now)
    latent_next = latent + delta * velocity_flat
    denoised = latent - noise_level(t_now) * velocity_flat
    return (img_next, txt_next, velocity_flat, latent_next, denoised)


def solution(mesh):
    placed = (
        P(("req", "seq"), "tp"),
        P(("req", "seq"), "tp"),
        P("req", None),
        P("req", None),
        P("seq", None, "tp"),
        P("seq", None, "tp"),
        P(),
        P("tp", "seq"),
        P("tp", "seq"),
        P("req", None),
        P("tp", None),
        P(),
        P(("req", "seq"), "tp"),
        P("req"),
        P("req"),
    )
    return jax.shard_map(
        per_device,
        mesh=mesh,
        in_specs=placed,
        out_specs=(
            P(("req", "seq"), "tp"),
            P(("req", "seq"), "tp"),
            P(("req", "seq"), "tp"),
            P(("req", "seq"), "tp"),
            P(("req", "seq"), "tp"),
        ),
        check_vma=False,
    )
```

```python
import functools
import math

import jax
import jax.numpy as jnp
from jax import lax
from jax.experimental import pallas as pl
from jax.sharding import PartitionSpec as P

STEPS = 28


EPS = 1e-06
SHIFT_MU = 1.15
THETA = 10000.0


def extended(block, sides, width):
    for axis, dim in sides:
        count = lax.axis_size(axis)
        forward = [(i, i + 1) for i in range(count - 1)]
        backward = [(target, source) for source, target in forward]
        low = lax.ppermute(
            lax.slice_in_dim(block, block.shape[dim] - width, None, axis=dim), axis, forward
        )
        high = lax.ppermute(lax.slice_in_dim(block, 0, width, axis=dim), axis, backward)
        block = jnp.concatenate([low, block, high], axis=dim)
    return block


def tree_sum(block, axis):
    count = lax.axis_size(axis)
    step = 1
    while step < count:
        block = block + lax.ppermute(block, axis, [(i, i ^ step) for i in range(count)])
        step *= 2
    return block


def halving_sum(block, axis, dim):
    count = lax.axis_size(axis)
    at = lax.axis_index(axis)
    step = count // 2
    while step >= 1:
        half = block.shape[dim] // 2
        low = lax.slice_in_dim(block, 0, half, axis=dim)
        high = lax.slice_in_dim(block, half, None, axis=dim)
        upper = (at // step) % 2 == 1
        kept = jnp.where(upper, high, low)
        sent = jnp.where(upper, low, high)
        block = kept + lax.ppermute(sent, axis, [(i, i ^ step) for i in range(count)])
        step //= 2
    return block


def attend_block(keep_ref, query_ref, key_ref, value_ref, out_ref, *, scale):
    scores = (
        lax.dot_general(
            query_ref[...],
            key_ref[...],
            (((1,), (1,)), ((), ())),
            preferred_element_type=jnp.float32,
        )
        * scale
    )
    scores = jnp.where(keep_ref[...] > 0.5, scores, -1e30)
    peak = jnp.max(scores, -1, keepdims=True)
    weights = jnp.exp(scores - peak)
    summed = jnp.sum(weights, -1, keepdims=True)
    mixed_v = jnp.dot(
        weights.astype(jnp.bfloat16), value_ref[...], preferred_element_type=jnp.float32
    )
    out_ref[...] = (mixed_v / summed).astype(out_ref.dtype)


def attention(keep, queries, keys, values, head_dim, q_tile):
    rows = queries.shape[0]
    total = keys.shape[0]
    heads = queries.shape[1] // head_dim
    return pl.pallas_call(
        functools.partial(attend_block, scale=head_dim ** (-0.5)),
        grid=(heads, rows // q_tile),
        in_specs=[
            pl.BlockSpec((1, total), lambda h, i: (0, 0)),
            pl.BlockSpec((q_tile, head_dim), lambda h, i: (i, h)),
            pl.BlockSpec((total, head_dim), lambda h, i: (0, h)),
            pl.BlockSpec((total, head_dim), lambda h, i: (0, h)),
        ],
        out_specs=pl.BlockSpec((q_tile, head_dim), lambda h, i: (i, h)),
        out_shape=jax.ShapeDtypeStruct(queries.shape, jnp.bfloat16),
    )(keep, queries, keys, values)


def modulate(hidden, mod_rows):
    values = hidden.astype(jnp.float32)
    mod_f = mod_rows.astype(jnp.float32)
    row_mean = jnp.mean(values, -1, keepdims=True)
    row_var = jnp.mean((values - row_mean) ** 2, -1, keepdims=True)
    normed = (values - row_mean) * lax.rsqrt(row_var + EPS)
    return (normed * (1.0 + mod_f[1]) + mod_f[0]).astype(jnp.bfloat16)


def rms_gain(values, gain_row):
    return values * lax.rsqrt(jnp.mean(values * values, -1, keepdims=True) + EPS) * gain_row


def rope_angles(row_pos, col_pos, head_dim):
    lead = head_dim // 16
    span = 7 * head_dim // 32
    freq = THETA ** (-jnp.arange(span, dtype=jnp.float32) / span)
    zero_part = jnp.zeros((row_pos.shape[0], lead), jnp.float32)
    return jnp.concatenate(
        [zero_part, row_pos[:, None] * freq[None], col_pos[:, None] * freq[None]], 1
    )


def apply_rope(values, angles):
    count, heads_n, head_dim = values.shape
    pairs = values.reshape(count, heads_n, head_dim // 2, 2)
    first = pairs[..., 0]
    second = pairs[..., 1]
    cosine = jnp.cos(angles)[:, None, :]
    sine = jnp.sin(angles)[:, None, :]
    turned = jnp.stack([first * cosine - second * sine, first * sine + second * cosine], -1)
    return turned.reshape(values.shape)


def split_heads(mixed, gain_q, gain_k, angles):
    head_dim = gain_q.shape[0]
    shaped = mixed.reshape(mixed.shape[0], 3, -1, head_dim)
    query = rms_gain(shaped[:, 0], gain_q)
    keyed = rms_gain(shaped[:, 1], gain_k)
    if angles is not None:
        query = apply_rope(query, angles)
        keyed = apply_rope(keyed, angles)
    return (
        query.astype(jnp.bfloat16),
        keyed.astype(jnp.bfloat16),
        shaped[:, 2].astype(jnp.bfloat16),
    )


def noise_level(tval):
    factor = math.exp(SHIFT_MU)
    return factor * tval / (factor * tval + 1.0 - tval)


def add_rows(normed, piece):
    flat_piece = piece.reshape(piece.shape[0], piece.shape[1] * piece.shape[2])
    return jnp.dot(normed, flat_piece, preferred_element_type=jnp.float32)


def per_device(
    img_hidden,
    txt_hidden,
    img_mod,
    txt_mod,
    img_qkv,
    txt_qkv,
    qk_gains,
    img_out_w,
    txt_out_w,
    final_mod,
    final_w,
    conv_w,
    latent,
    text_len,
    step_index,
):
    seq_count = lax.axis_size("seq")
    seq_at = lax.axis_index("seq")
    tp_at = lax.axis_index("tp")
    img_rows = img_hidden.shape[0]
    txt_rows = txt_hidden.shape[0]
    local_width = img_hidden.shape[1]
    img_full, txt_full = (
        lax.all_gather(img_hidden, "tp", axis=1, tiled=True),
        lax.all_gather(txt_hidden, "tp", axis=1, tiled=True),
    )
    full_width = img_full.shape[1]
    img_norm = modulate(img_full, img_mod)
    txt_norm = modulate(txt_full, txt_mod)
    img_mixed = add_rows(img_norm, lax.all_gather(img_qkv, "seq", axis=0, tiled=True))
    txt_norm_rows = lax.all_to_all(txt_norm, "seq", 1, 0, tiled=True)
    txt_mixed = lax.psum_scatter(
        add_rows(txt_norm_rows, txt_qkv), "seq", scatter_dimension=0, tiled=True
    )
    head_dim = qk_gains.shape[1]
    grid_side = latent.shape[0] * seq_count
    token_ids = seq_at * img_rows + jnp.arange(img_rows, dtype=jnp.int32)
    row_pos = (token_ids // grid_side).astype(jnp.float32)
    col_pos = (token_ids % grid_side).astype(jnp.float32)
    angles = rope_angles(row_pos, col_pos, head_dim)
    img_query, img_key, img_value = split_heads(img_mixed, qk_gains[0], qk_gains[1], angles)
    txt_query, txt_key, txt_value = split_heads(txt_mixed, qk_gains[2], qk_gains[3], None)
    local_len = txt_rows + img_rows
    heads_local = img_query.shape[1]
    queries = jnp.concatenate([txt_query, img_query], 0)
    keys_local = jnp.concatenate([txt_key, img_key], 0).reshape(local_len, heads_local * head_dim)
    values_local = jnp.concatenate([txt_value, img_value], 0).reshape(
        local_len, heads_local * head_dim
    )
    limit = text_len[0]
    kv_width = heads_local * head_dim
    kv_piece = lax.all_gather(
        jnp.concatenate([keys_local, values_local], 1), "seq", axis=0, tiled=True
    )
    key_piece = kv_piece[:, :kv_width]
    value_piece = kv_piece[:, kv_width:]
    slot = jnp.arange(key_piece.shape[0], dtype=jnp.int32)
    within = slot % local_len
    text_pos = (slot // local_len) * txt_rows + within
    keep = ((within >= txt_rows) | (text_pos < limit)).astype(jnp.float32)[None, :]
    attn = attention(
        keep,
        queries.reshape(local_len, kv_width),
        key_piece,
        value_piece,
        head_dim,
        local_len // 3,
    )
    txt_attn = attn[:txt_rows]
    img_attn = attn[txt_rows:]
    img_term = jnp.dot(
        img_attn,
        lax.all_gather(img_out_w, "seq", axis=1, tiled=True),
        preferred_element_type=jnp.float32,
    )
    txt_term = jnp.dot(
        txt_attn,
        lax.all_gather(txt_out_w, "seq", axis=1, tiled=True),
        preferred_element_type=jnp.float32,
    )
    txt_out = halving_sum(txt_term.astype(jnp.bfloat16).astype(jnp.float32), "tp", 1)
    img_out = lax.psum_scatter(
        img_term.astype(jnp.bfloat16), "tp", scatter_dimension=1, tiled=True
    ).astype(jnp.float32)
    img_gate = lax.dynamic_slice_in_dim(
        img_mod.astype(jnp.float32)[2], tp_at * local_width, local_width
    )
    txt_gate = lax.dynamic_slice_in_dim(
        txt_mod.astype(jnp.float32)[2], tp_at * local_width, local_width
    )
    img_next = (img_hidden.astype(jnp.float32) + img_gate * img_out).astype(jnp.bfloat16)
    text_valid = seq_at * txt_rows + jnp.arange(txt_rows, dtype=jnp.int32) < limit
    txt_base = txt_hidden.astype(jnp.float32)
    txt_next = jnp.where(text_valid[:, None], txt_base + txt_gate * txt_out, txt_base).astype(
        jnp.bfloat16
    )
    shift_row = lax.dynamic_slice_in_dim(final_mod[0], tp_at * local_width, local_width)
    scale_row = lax.dynamic_slice_in_dim(final_mod[1], tp_at * local_width, local_width)
    final_shift = shift_row.astype(jnp.float32)
    final_scale = scale_row.astype(jnp.float32)
    weight_final = final_w.astype(jnp.float32)
    values = img_next.astype(jnp.float32)
    channels = final_w.shape[1]
    final_gain = 1.0 + final_scale
    high = lax.Precision.HIGHEST
    lifted = jnp.dot(values * final_gain, weight_final, precision=high)
    consts = jnp.stack(
        [jnp.dot(final_gain, weight_final, precision=high), jnp.dot(final_shift, weight_final, precision=high)]
    )
    packed = jnp.concatenate(
        [
            jnp.concatenate([lifted, jnp.sum(values, -1)[:, None], jnp.sum(values * values, -1)[:, None]], 1),
            jnp.pad(consts, ((0, 0), (0, 2))),
        ],
        0,
    )
    packed = tree_sum(packed, "tp")
    lifted = packed[:img_rows, :channels]
    row_mean = packed[:img_rows, channels] / full_width
    row_var = packed[:img_rows, channels + 1] / full_width - row_mean * row_mean
    row_scale = lax.rsqrt(row_var + EPS)[:, None]
    patch = row_scale * (lifted - row_mean[:, None] * packed[img_rows, :channels]) + packed[
        img_rows + 1, :channels
    ]
    band_rows = latent.shape[0]
    patch_band = patch.astype(jnp.bfloat16).reshape(band_rows, grid_side * channels)
    rimmed = extended(patch_band, (("seq", 0),), 1)
    col_width = latent.shape[1] // channels
    framed = jnp.pad(rimmed.reshape(band_rows + 2, grid_side, channels), ((0, 0), (1, 1), (0, 0)))
    window = lax.dynamic_slice_in_dim(framed, tp_at * col_width, col_width + 2, 1)
    velocity = jnp.zeros((band_rows, col_width, channels), jnp.float32)
    for row_shift in range(3):
        for col_shift in range(3):
            velocity = velocity + jnp.einsum(
                "rci,io->rco",
                window[row_shift : row_shift + band_rows, col_shift : col_shift + col_width],
                conv_w[row_shift, col_shift],
                preferred_element_type=jnp.float32,
            )
    velocity_flat = velocity.reshape(band_rows, col_width * channels)
    step_f = step_index[0].astype(jnp.float32)
    t_now = 1.0 - step_f / STEPS
    t_after = 1.0 - (step_f + 1.0) / STEPS
    delta = noise_level(t_after) - noise_level(t_now)
    latent_next = latent + delta * velocity_flat
    denoised = latent - noise_level(t_now) * velocity_flat
    return (img_next, txt_next, velocity_flat, latent_next, denoised)


def solution(mesh):
    placed = (
        P(("req", "seq"), "tp"),
        P(("req", "seq"), "tp"),
        P("req", None),
        P("req", None),
        P("seq", None, "tp"),
        P("seq", None, "tp"),
        P(),
        P("tp", "seq"),
        P("tp", "seq"),
        P("req", None),
        P("tp", None),
        P(),
        P(("req", "seq"), "tp"),
        P("req"),
        P("req"),
    )
    return jax.shard_map(
        per_device,
        mesh=mesh,
        in_specs=placed,
        out_specs=(
            P(("req", "seq"), "tp"),
            P(("req", "seq"), "tp"),
            P(("req", "seq"), "tp"),
            P(("req", "seq"), "tp"),
            P(("req", "seq"), "tp"),
        ),
        check_vma=False,
    )
```

```python
import functools
import math

import jax
import jax.numpy as jnp
from jax import lax
from jax.experimental import pallas as pl
from jax.sharding import PartitionSpec as P

STEPS = 28


EPS = 1e-06
SHIFT_MU = 1.15
THETA = 10000.0


def extended(block, sides, width):
    for axis, dim in sides:
        count = lax.axis_size(axis)
        forward = [(i, i + 1) for i in range(count - 1)]
        backward = [(target, source) for source, target in forward]
        low = lax.ppermute(
            lax.slice_in_dim(block, block.shape[dim] - width, None, axis=dim), axis, forward
        )
        high = lax.ppermute(lax.slice_in_dim(block, 0, width, axis=dim), axis, backward)
        block = jnp.concatenate([low, block, high], axis=dim)
    return block


def tree_sum(block, axis):
    count = lax.axis_size(axis)
    step = 1
    while step < count:
        block = block + lax.ppermute(block, axis, [(i, i ^ step) for i in range(count)])
        step *= 2
    return block


def halving_sum(block, axis, dim):
    count = lax.axis_size(axis)
    at = lax.axis_index(axis)
    step = count // 2
    while step >= 1:
        half = block.shape[dim] // 2
        low = lax.slice_in_dim(block, 0, half, axis=dim)
        high = lax.slice_in_dim(block, half, None, axis=dim)
        upper = (at // step) % 2 == 1
        kept = jnp.where(upper, high, low)
        sent = jnp.where(upper, low, high)
        block = kept + lax.ppermute(sent, axis, [(i, i ^ step) for i in range(count)])
        step //= 2
    return block


def attend_block(keep_ref, query_ref, key_ref, value_ref, out_ref, *, scale):
    scores = (
        lax.dot_general(
            query_ref[...],
            key_ref[...],
            (((1,), (1,)), ((), ())),
            preferred_element_type=jnp.float32,
        )
        * scale
    )
    scores = jnp.where(keep_ref[...] > 0.5, scores, -1e30)
    peak = jnp.max(scores, -1, keepdims=True)
    weights = jnp.exp(scores - peak)
    summed = jnp.sum(weights, -1, keepdims=True)
    mixed_v = jnp.dot(
        weights.astype(jnp.bfloat16), value_ref[...], preferred_element_type=jnp.float32
    )
    out_ref[...] = (mixed_v / summed).astype(out_ref.dtype)


def attention(keep, queries, keys, values, head_dim, q_tile):
    rows = queries.shape[0]
    total = keys.shape[0]
    heads = queries.shape[1] // head_dim
    return pl.pallas_call(
        functools.partial(attend_block, scale=head_dim ** (-0.5)),
        grid=(heads, rows // q_tile),
        in_specs=[
            pl.BlockSpec((1, total), lambda h, i: (0, 0)),
            pl.BlockSpec((q_tile, head_dim), lambda h, i: (i, h)),
            pl.BlockSpec((total, head_dim), lambda h, i: (0, h)),
            pl.BlockSpec((total, head_dim), lambda h, i: (0, h)),
        ],
        out_specs=pl.BlockSpec((q_tile, head_dim), lambda h, i: (i, h)),
        out_shape=jax.ShapeDtypeStruct(queries.shape, jnp.bfloat16),
    )(keep, queries, keys, values)


def bit_of(value, step):
    return (value // step) % 2


def doubling_gather(block, axis, dim, order):
    count = lax.axis_size(axis)
    at = lax.axis_index(axis)
    stacked = block[None]
    for step in order:
        other = lax.ppermute(stacked, axis, [(i, i ^ step) for i in range(count)])
        upper = bit_of(at, step) == 1
        stacked = jnp.stack([jnp.where(upper, other, stacked), jnp.where(upper, stacked, other)])
        stacked = stacked.reshape((-1,) + block.shape)
    rank = len(order)
    source = [sum(((p >> k) & 1) * order[k] for k in range(rank)) for p in range(count)]
    place = [source.index(d) for d in range(count)]
    picked = jnp.stack([stacked[p] for p in place], 0)
    moved = jnp.moveaxis(picked, 0, dim)
    shape = list(block.shape)
    shape[dim] *= count
    return moved.reshape(shape)


def halving_scatter(block, axis, dim, order):
    count = lax.axis_size(axis)
    at = lax.axis_index(axis)
    rank = len(order)
    width = block.shape[dim] // count
    pieces = [lax.slice_in_dim(block, d * width, (d + 1) * width, axis=dim) for d in range(count)]
    slots = [sum(((d // order[k]) % 2) << (rank - 1 - k) for k in range(rank)) for d in range(count)]
    arranged = [None] * count
    for d in range(count):
        arranged[slots[d]] = pieces[d]
    block = jnp.concatenate(arranged, dim)
    for step in order:
        half = block.shape[dim] // 2
        low = lax.slice_in_dim(block, 0, half, axis=dim)
        high = lax.slice_in_dim(block, half, None, axis=dim)
        upper = bit_of(at, step) == 1
        kept = jnp.where(upper, high, low)
        sent = jnp.where(upper, low, high)
        block = kept + lax.ppermute(sent, axis, [(i, i ^ step) for i in range(count)])
    return block


def transpose_devices(block):
    side = lax.axis_size("tp")
    swap = [(a * side + b, b * side + a) for a in range(side) for b in range(side)]
    return lax.ppermute(block, ("seq", "tp"), swap)


def modulate(hidden, mod_rows):
    values = hidden.astype(jnp.float32)
    mod_f = mod_rows.astype(jnp.float32)
    row_mean = jnp.mean(values, -1, keepdims=True)
    row_var = jnp.mean((values - row_mean) ** 2, -1, keepdims=True)
    normed = (values - row_mean) * lax.rsqrt(row_var + EPS)
    return (normed * (1.0 + mod_f[1]) + mod_f[0]).astype(jnp.bfloat16)


def rms_gain(values, gain_row):
    return values * lax.rsqrt(jnp.mean(values * values, -1, keepdims=True) + EPS) * gain_row


def rope_angles(row_pos, col_pos, head_dim):
    lead = head_dim // 16
    span = 7 * head_dim // 32
    freq = THETA ** (-jnp.arange(span, dtype=jnp.float32) / span)
    zero_part = jnp.zeros((row_pos.shape[0], lead), jnp.float32)
    return jnp.concatenate(
        [zero_part, row_pos[:, None] * freq[None], col_pos[:, None] * freq[None]], 1
    )


def apply_rope(values, angles):
    count, heads_n, head_dim = values.shape
    pairs = values.reshape(count, heads_n, head_dim // 2, 2)
    first = pairs[..., 0]
    second = pairs[..., 1]
    cosine = jnp.cos(angles)[:, None, :]
    sine = jnp.sin(angles)[:, None, :]
    turned = jnp.stack([first * cosine - second * sine, first * sine + second * cosine], -1)
    return turned.reshape(values.shape)


def split_heads(mixed, gain_q, gain_k, angles):
    head_dim = gain_q.shape[0]
    shaped = mixed.reshape(mixed.shape[0], 3, -1, head_dim)
    query = rms_gain(shaped[:, 0], gain_q)
    keyed = rms_gain(shaped[:, 1], gain_k)
    if angles is not None:
        query = apply_rope(query, angles)
        keyed = apply_rope(keyed, angles)
    return (
        query.astype(jnp.bfloat16),
        keyed.astype(jnp.bfloat16),
        shaped[:, 2].astype(jnp.bfloat16),
    )


def noise_level(tval):
    factor = math.exp(SHIFT_MU)
    return factor * tval / (factor * tval + 1.0 - tval)


def add_rows(normed, piece):
    flat_piece = piece.reshape(piece.shape[0], piece.shape[1] * piece.shape[2])
    return jnp.dot(normed, flat_piece, preferred_element_type=jnp.float32)


def per_device(
    img_hidden,
    txt_hidden,
    img_mod,
    txt_mod,
    img_qkv,
    txt_qkv,
    qk_gains,
    img_out_w,
    txt_out_w,
    final_mod,
    final_w,
    conv_w,
    latent,
    text_len,
    step_index,
):
    seq_count = lax.axis_size("seq")
    seq_at = lax.axis_index("seq")
    tp_at = lax.axis_index("tp")
    img_rows = img_hidden.shape[0]
    txt_rows = txt_hidden.shape[0]
    local_width = img_hidden.shape[1]
    tp_order = (4, 2, 1)
    seq_order = (2, 1, 4)
    img_full = doubling_gather(img_hidden, "tp", 1, tp_order)
    txt_full = doubling_gather(txt_hidden, "tp", 1, tp_order)
    img_out_full = doubling_gather(img_out_w, "seq", 1, seq_order)
    full_width = img_full.shape[1]
    img_norm = modulate(img_full, img_mod)
    txt_norm = modulate(txt_full, txt_mod)
    img_mixed = add_rows(img_norm, lax.all_gather(img_qkv, "seq", axis=0, tiled=True))
    txt_norm_rows = lax.all_to_all(txt_norm, "seq", 1, 0, tiled=True)
    txt_mixed = halving_scatter(add_rows(txt_norm_rows, txt_qkv), "seq", 0, (4, 1, 2))
    head_dim = qk_gains.shape[1]
    grid_side = latent.shape[0] * seq_count
    token_ids = seq_at * img_rows + jnp.arange(img_rows, dtype=jnp.int32)
    row_pos = (token_ids // grid_side).astype(jnp.float32)
    col_pos = (token_ids % grid_side).astype(jnp.float32)
    angles = rope_angles(row_pos, col_pos, head_dim)
    img_query, img_key, img_value = split_heads(img_mixed, qk_gains[0], qk_gains[1], angles)
    txt_query, txt_key, txt_value = split_heads(txt_mixed, qk_gains[2], qk_gains[3], None)
    local_len = txt_rows + img_rows
    heads_local = img_query.shape[1]
    queries = jnp.concatenate([txt_query, img_query], 0)
    keys_local = jnp.concatenate([txt_key, img_key], 0).reshape(local_len, heads_local * head_dim)
    values_local = jnp.concatenate([txt_value, img_value], 0).reshape(
        local_len, heads_local * head_dim
    )
    limit = text_len[0]
    kv_width = heads_local * head_dim
    kv_piece = lax.all_gather(
        jnp.concatenate([keys_local, values_local], 1), "seq", axis=0, tiled=True
    )
    key_piece = kv_piece[:, :kv_width]
    value_piece = kv_piece[:, kv_width:]
    slot = jnp.arange(key_piece.shape[0], dtype=jnp.int32)
    within = slot % local_len
    text_pos = (slot // local_len) * txt_rows + within
    keep = ((within >= txt_rows) | (text_pos < limit)).astype(jnp.float32)[None, :]
    attn = attention(
        keep,
        queries.reshape(local_len, kv_width),
        key_piece,
        value_piece,
        head_dim,
        local_len // 3,
    )
    txt_attn = attn[:txt_rows]
    img_attn = attn[txt_rows:]
    img_term = jnp.dot(
        img_attn,
        img_out_full,
        preferred_element_type=jnp.float32,
    )
    txt_term = jnp.dot(
        doubling_gather(txt_attn, "seq", 0, seq_order),
        txt_out_w,
        preferred_element_type=jnp.float32,
    )
    txt_out = transpose_devices(
        halving_scatter(txt_term.astype(jnp.bfloat16).astype(jnp.float32), "tp", 0, (1, 2, 4))
    )
    img_out = lax.psum_scatter(
        img_term.astype(jnp.bfloat16), "tp", scatter_dimension=1, tiled=True
    ).astype(jnp.float32)
    img_gate = lax.dynamic_slice_in_dim(
        img_mod.astype(jnp.float32)[2], tp_at * local_width, local_width
    )
    txt_gate = lax.dynamic_slice_in_dim(
        txt_mod.astype(jnp.float32)[2], tp_at * local_width, local_width
    )
    img_next = (img_hidden.astype(jnp.float32) + img_gate * img_out).astype(jnp.bfloat16)
    text_valid = seq_at * txt_rows + jnp.arange(txt_rows, dtype=jnp.int32) < limit
    txt_base = txt_hidden.astype(jnp.float32)
    txt_next = jnp.where(text_valid[:, None], txt_base + txt_gate * txt_out, txt_base).astype(
        jnp.bfloat16
    )
    shift_row = lax.dynamic_slice_in_dim(final_mod[0], tp_at * local_width, local_width)
    scale_row = lax.dynamic_slice_in_dim(final_mod[1], tp_at * local_width, local_width)
    final_shift = shift_row.astype(jnp.float32)
    final_scale = scale_row.astype(jnp.float32)
    weight_final = final_w.astype(jnp.float32)
    values = img_next.astype(jnp.float32)
    channels = final_w.shape[1]
    final_gain = 1.0 + final_scale
    high = lax.Precision.HIGHEST
    lifted = jnp.dot(values * final_gain, weight_final, precision=high)
    consts = jnp.stack(
        [jnp.dot(final_gain, weight_final, precision=high), jnp.dot(final_shift, weight_final, precision=high)]
    )
    packed = jnp.concatenate(
        [
            jnp.concatenate([lifted, jnp.sum(values, -1)[:, None], jnp.sum(values * values, -1)[:, None]], 1),
            jnp.pad(consts, ((0, 0), (0, 2))),
        ],
        0,
    )
    packed = tree_sum(packed, "tp")
    lifted = packed[:img_rows, :channels]
    row_mean = packed[:img_rows, channels] / full_width
    row_var = packed[:img_rows, channels + 1] / full_width - row_mean * row_mean
    row_scale = lax.rsqrt(row_var + EPS)[:, None]
    patch = row_scale * (lifted - row_mean[:, None] * packed[img_rows, :channels]) + packed[
        img_rows + 1, :channels
    ]
    band_rows = latent.shape[0]
    patch_band = patch.astype(jnp.bfloat16).reshape(band_rows, grid_side * channels)
    rimmed = extended(patch_band, (("seq", 0),), 1)
    col_width = latent.shape[1] // channels
    framed = jnp.pad(rimmed.reshape(band_rows + 2, grid_side, channels), ((0, 0), (1, 1), (0, 0)))
    window = lax.dynamic_slice_in_dim(framed, tp_at * col_width, col_width + 2, 1)
    velocity = jnp.zeros((band_rows, col_width, channels), jnp.float32)
    for row_shift in range(3):
        for col_shift in range(3):
            velocity = velocity + jnp.einsum(
                "rci,io->rco",
                window[row_shift : row_shift + band_rows, col_shift : col_shift + col_width],
                conv_w[row_shift, col_shift],
                preferred_element_type=jnp.float32,
            )
    velocity_flat = velocity.reshape(band_rows, col_width * channels)
    step_f = step_index[0].astype(jnp.float32)
    t_now = 1.0 - step_f / STEPS
    t_after = 1.0 - (step_f + 1.0) / STEPS
    delta = noise_level(t_after) - noise_level(t_now)
    latent_next = latent + delta * velocity_flat
    denoised = latent - noise_level(t_now) * velocity_flat
    return (img_next, txt_next, velocity_flat, latent_next, denoised)


def solution(mesh):
    placed = (
        P(("req", "seq"), "tp"),
        P(("req", "seq"), "tp"),
        P("req", None),
        P("req", None),
        P("seq", None, "tp"),
        P("seq", None, "tp"),
        P(),
        P("tp", "seq"),
        P("tp", "seq"),
        P("req", None),
        P("tp", None),
        P(),
        P(("req", "seq"), "tp"),
        P("req"),
        P("req"),
    )
    return jax.shard_map(
        per_device,
        mesh=mesh,
        in_specs=placed,
        out_specs=(
            P(("req", "seq"), "tp"),
            P(("req", "seq"), "tp"),
            P(("req", "seq"), "tp"),
            P(("req", "seq"), "tp"),
            P(("req", "seq"), "tp"),
        ),
        check_vma=False,
    )
```

```python
import functools
import math

import jax
import jax.numpy as jnp
from jax import lax
from jax.experimental import pallas as pl
from jax.sharding import PartitionSpec as P

STEPS = 28


EPS = 1e-06
SHIFT_MU = 1.15
THETA = 10000.0


def extended(block, sides, width):
    for axis, dim in sides:
        count = lax.axis_size(axis)
        forward = [(i, i + 1) for i in range(count - 1)]
        backward = [(target, source) for source, target in forward]
        low = lax.ppermute(
            lax.slice_in_dim(block, block.shape[dim] - width, None, axis=dim), axis, forward
        )
        high = lax.ppermute(lax.slice_in_dim(block, 0, width, axis=dim), axis, backward)
        block = jnp.concatenate([low, block, high], axis=dim)
    return block


def tree_sum(block, axis):
    count = lax.axis_size(axis)
    step = 1
    while step < count:
        block = block + lax.ppermute(block, axis, [(i, i ^ step) for i in range(count)])
        step *= 2
    return block


def halving_sum(block, axis, dim):
    count = lax.axis_size(axis)
    at = lax.axis_index(axis)
    step = count // 2
    while step >= 1:
        half = block.shape[dim] // 2
        low = lax.slice_in_dim(block, 0, half, axis=dim)
        high = lax.slice_in_dim(block, half, None, axis=dim)
        upper = (at // step) % 2 == 1
        kept = jnp.where(upper, high, low)
        sent = jnp.where(upper, low, high)
        block = kept + lax.ppermute(sent, axis, [(i, i ^ step) for i in range(count)])
        step //= 2
    return block


def attend_block(keep_ref, query_ref, key_ref, value_ref, out_ref, *, scale):
    scores = (
        lax.dot_general(
            query_ref[...],
            key_ref[...],
            (((1,), (1,)), ((), ())),
            preferred_element_type=jnp.float32,
        )
        * scale
    )
    scores = jnp.where(keep_ref[...] > 0.5, scores, -1e30)
    peak = jnp.max(scores, -1, keepdims=True)
    weights = jnp.exp(scores - peak)
    summed = jnp.sum(weights, -1, keepdims=True)
    mixed_v = jnp.dot(
        weights.astype(jnp.bfloat16), value_ref[...], preferred_element_type=jnp.float32
    )
    out_ref[...] = (mixed_v / summed).astype(out_ref.dtype)


def attention(keep, queries, keys, values, head_dim, q_tile):
    rows = queries.shape[0]
    total = keys.shape[0]
    heads = queries.shape[1] // head_dim
    return pl.pallas_call(
        functools.partial(attend_block, scale=head_dim ** (-0.5)),
        grid=(heads, rows // q_tile),
        in_specs=[
            pl.BlockSpec((1, total), lambda h, i: (0, 0)),
            pl.BlockSpec((q_tile, head_dim), lambda h, i: (i, h)),
            pl.BlockSpec((total, head_dim), lambda h, i: (0, h)),
            pl.BlockSpec((total, head_dim), lambda h, i: (0, h)),
        ],
        out_specs=pl.BlockSpec((q_tile, head_dim), lambda h, i: (i, h)),
        out_shape=jax.ShapeDtypeStruct(queries.shape, jnp.bfloat16),
    )(keep, queries, keys, values)


def bit_of(value, step):
    return (value // step) % 2


def doubling_gather(block, axis, dim, order):
    count = lax.axis_size(axis)
    at = lax.axis_index(axis)
    stacked = block[None]
    for step in order:
        other = lax.ppermute(stacked, axis, [(i, i ^ step) for i in range(count)])
        upper = bit_of(at, step) == 1
        stacked = jnp.stack([jnp.where(upper, other, stacked), jnp.where(upper, stacked, other)])
        stacked = stacked.reshape((-1,) + block.shape)
    rank = len(order)
    source = [sum(((p >> k) & 1) * order[k] for k in range(rank)) for p in range(count)]
    place = [source.index(d) for d in range(count)]
    picked = jnp.stack([stacked[p] for p in place], 0)
    moved = jnp.moveaxis(picked, 0, dim)
    shape = list(block.shape)
    shape[dim] *= count
    return moved.reshape(shape)


def halving_scatter(block, axis, dim, order):
    count = lax.axis_size(axis)
    at = lax.axis_index(axis)
    rank = len(order)
    width = block.shape[dim] // count
    pieces = [lax.slice_in_dim(block, d * width, (d + 1) * width, axis=dim) for d in range(count)]
    slots = [sum(((d // order[k]) % 2) << (rank - 1 - k) for k in range(rank)) for d in range(count)]
    arranged = [None] * count
    for d in range(count):
        arranged[slots[d]] = pieces[d]
    block = jnp.concatenate(arranged, dim)
    for step in order:
        half = block.shape[dim] // 2
        low = lax.slice_in_dim(block, 0, half, axis=dim)
        high = lax.slice_in_dim(block, half, None, axis=dim)
        upper = bit_of(at, step) == 1
        kept = jnp.where(upper, high, low)
        sent = jnp.where(upper, low, high)
        block = kept + lax.ppermute(sent, axis, [(i, i ^ step) for i in range(count)])
    return block


def transpose_devices(block):
    side = lax.axis_size("tp")
    swap = [(a * side + b, b * side + a) for a in range(side) for b in range(side)]
    return lax.ppermute(block, ("seq", "tp"), swap)


def modulate(hidden, mod_rows):
    values = hidden.astype(jnp.float32)
    mod_f = mod_rows.astype(jnp.float32)
    row_mean = jnp.mean(values, -1, keepdims=True)
    row_var = jnp.mean((values - row_mean) ** 2, -1, keepdims=True)
    normed = (values - row_mean) * lax.rsqrt(row_var + EPS)
    return (normed * (1.0 + mod_f[1]) + mod_f[0]).astype(jnp.bfloat16)


def rms_gain(values, gain_row):
    return values * lax.rsqrt(jnp.mean(values * values, -1, keepdims=True) + EPS) * gain_row


def rope_angles(row_pos, col_pos, head_dim):
    lead = head_dim // 16
    span = 7 * head_dim // 32
    freq = THETA ** (-jnp.arange(span, dtype=jnp.float32) / span)
    zero_part = jnp.zeros((row_pos.shape[0], lead), jnp.float32)
    return jnp.concatenate(
        [zero_part, row_pos[:, None] * freq[None], col_pos[:, None] * freq[None]], 1
    )


def apply_rope(values, angles):
    count, heads_n, head_dim = values.shape
    pairs = values.reshape(count, heads_n, head_dim // 2, 2)
    first = pairs[..., 0]
    second = pairs[..., 1]
    cosine = jnp.cos(angles)[:, None, :]
    sine = jnp.sin(angles)[:, None, :]
    turned = jnp.stack([first * cosine - second * sine, first * sine + second * cosine], -1)
    return turned.reshape(values.shape)


def split_heads(mixed, gain_q, gain_k, angles):
    head_dim = gain_q.shape[0]
    shaped = mixed.reshape(mixed.shape[0], 3, -1, head_dim)
    query = rms_gain(shaped[:, 0], gain_q)
    keyed = rms_gain(shaped[:, 1], gain_k)
    if angles is not None:
        query = apply_rope(query, angles)
        keyed = apply_rope(keyed, angles)
    return (
        query.astype(jnp.bfloat16),
        keyed.astype(jnp.bfloat16),
        shaped[:, 2].astype(jnp.bfloat16),
    )


def noise_level(tval):
    factor = math.exp(SHIFT_MU)
    return factor * tval / (factor * tval + 1.0 - tval)


def add_rows(normed, piece):
    flat_piece = piece.reshape(piece.shape[0], piece.shape[1] * piece.shape[2])
    return jnp.dot(normed, flat_piece, preferred_element_type=jnp.float32)


def per_device(
    img_hidden,
    txt_hidden,
    img_mod,
    txt_mod,
    img_qkv,
    txt_qkv,
    qk_gains,
    img_out_w,
    txt_out_w,
    final_mod,
    final_w,
    conv_w,
    latent,
    text_len,
    step_index,
):
    seq_count = lax.axis_size("seq")
    seq_at = lax.axis_index("seq")
    tp_at = lax.axis_index("tp")
    img_rows = img_hidden.shape[0]
    txt_rows = txt_hidden.shape[0]
    local_width = img_hidden.shape[1]
    img_full, txt_full = (
        lax.all_gather(img_hidden, "tp", axis=1, tiled=True),
        lax.all_gather(txt_hidden, "tp", axis=1, tiled=True),
    )
    full_width = img_full.shape[1]
    img_norm = modulate(img_full, img_mod)
    txt_norm = modulate(txt_full, txt_mod)
    img_weights = lax.all_gather(img_qkv, "seq", axis=0, tiled=True)
    img_weights, img_out_w = lax.optimization_barrier((img_weights, img_out_w))
    img_out_full = lax.all_gather(img_out_w, "seq", axis=1, tiled=True)
    img_mixed = add_rows(img_norm, img_weights)
    txt_norm_rows = lax.all_to_all(txt_norm, "seq", 1, 0, tiled=True)
    txt_mixed = lax.psum_scatter(
        add_rows(txt_norm_rows, txt_qkv), "seq", scatter_dimension=0, tiled=True
    )
    head_dim = qk_gains.shape[1]
    grid_side = latent.shape[0] * seq_count
    token_ids = seq_at * img_rows + jnp.arange(img_rows, dtype=jnp.int32)
    row_pos = (token_ids // grid_side).astype(jnp.float32)
    col_pos = (token_ids % grid_side).astype(jnp.float32)
    angles = rope_angles(row_pos, col_pos, head_dim)
    img_query, img_key, img_value = split_heads(img_mixed, qk_gains[0], qk_gains[1], angles)
    txt_query, txt_key, txt_value = split_heads(txt_mixed, qk_gains[2], qk_gains[3], None)
    local_len = txt_rows + img_rows
    heads_local = img_query.shape[1]
    queries = jnp.concatenate([txt_query, img_query], 0)
    keys_local = jnp.concatenate([txt_key, img_key], 0).reshape(local_len, heads_local * head_dim)
    values_local = jnp.concatenate([txt_value, img_value], 0).reshape(
        local_len, heads_local * head_dim
    )
    limit = text_len[0]
    kv_width = heads_local * head_dim
    kv_piece = lax.all_gather(
        jnp.concatenate([keys_local, values_local], 1), "seq", axis=0, tiled=True
    )
    key_piece = kv_piece[:, :kv_width]
    value_piece = kv_piece[:, kv_width:]
    slot = jnp.arange(key_piece.shape[0], dtype=jnp.int32)
    within = slot % local_len
    text_pos = (slot // local_len) * txt_rows + within
    keep = ((within >= txt_rows) | (text_pos < limit)).astype(jnp.float32)[None, :]
    attn = attention(
        keep,
        queries.reshape(local_len, kv_width),
        key_piece,
        value_piece,
        head_dim,
        local_len // 3,
    )
    txt_attn = attn[:txt_rows]
    img_attn = attn[txt_rows:]
    img_term = jnp.dot(
        img_attn,
        img_out_full,
        preferred_element_type=jnp.float32,
    )
    txt_term = jnp.dot(
        doubling_gather(txt_attn, "seq", 0, (2, 1, 4)),
        txt_out_w,
        preferred_element_type=jnp.float32,
    )
    txt_out = transpose_devices(
        halving_scatter(txt_term.astype(jnp.bfloat16).astype(jnp.float32), "tp", 0, (1, 2, 4))
    )
    img_out = lax.psum_scatter(
        img_term.astype(jnp.bfloat16), "tp", scatter_dimension=1, tiled=True
    ).astype(jnp.float32)
    img_gate = lax.dynamic_slice_in_dim(
        img_mod.astype(jnp.float32)[2], tp_at * local_width, local_width
    )
    txt_gate = lax.dynamic_slice_in_dim(
        txt_mod.astype(jnp.float32)[2], tp_at * local_width, local_width
    )
    img_next = (img_hidden.astype(jnp.float32) + img_gate * img_out).astype(jnp.bfloat16)
    text_valid = seq_at * txt_rows + jnp.arange(txt_rows, dtype=jnp.int32) < limit
    txt_base = txt_hidden.astype(jnp.float32)
    txt_next = jnp.where(text_valid[:, None], txt_base + txt_gate * txt_out, txt_base).astype(
        jnp.bfloat16
    )
    shift_row = lax.dynamic_slice_in_dim(final_mod[0], tp_at * local_width, local_width)
    scale_row = lax.dynamic_slice_in_dim(final_mod[1], tp_at * local_width, local_width)
    final_shift = shift_row.astype(jnp.float32)
    final_scale = scale_row.astype(jnp.float32)
    weight_final = final_w.astype(jnp.float32)
    values = img_next.astype(jnp.float32)
    channels = final_w.shape[1]
    final_gain = 1.0 + final_scale
    high = lax.Precision.HIGHEST
    lifted = jnp.dot(values * final_gain, weight_final, precision=high)
    consts = jnp.stack(
        [jnp.dot(final_gain, weight_final, precision=high), jnp.dot(final_shift, weight_final, precision=high)]
    )
    packed = jnp.concatenate(
        [
            jnp.concatenate([lifted, jnp.sum(values, -1)[:, None], jnp.sum(values * values, -1)[:, None]], 1),
            jnp.pad(consts, ((0, 0), (0, 2))),
        ],
        0,
    )
    packed = tree_sum(packed, "tp")
    lifted = packed[:img_rows, :channels]
    row_mean = packed[:img_rows, channels] / full_width
    row_var = packed[:img_rows, channels + 1] / full_width - row_mean * row_mean
    row_scale = lax.rsqrt(row_var + EPS)[:, None]
    patch = row_scale * (lifted - row_mean[:, None] * packed[img_rows, :channels]) + packed[
        img_rows + 1, :channels
    ]
    band_rows = latent.shape[0]
    patch_band = patch.astype(jnp.bfloat16).reshape(band_rows, grid_side * channels)
    rimmed = extended(patch_band, (("seq", 0),), 1)
    col_width = latent.shape[1] // channels
    framed = jnp.pad(rimmed.reshape(band_rows + 2, grid_side, channels), ((0, 0), (1, 1), (0, 0)))
    window = lax.dynamic_slice_in_dim(framed, tp_at * col_width, col_width + 2, 1)
    velocity = jnp.zeros((band_rows, col_width, channels), jnp.float32)
    for row_shift in range(3):
        for col_shift in range(3):
            velocity = velocity + jnp.einsum(
                "rci,io->rco",
                window[row_shift : row_shift + band_rows, col_shift : col_shift + col_width],
                conv_w[row_shift, col_shift],
                preferred_element_type=jnp.float32,
            )
    velocity_flat = velocity.reshape(band_rows, col_width * channels)
    step_f = step_index[0].astype(jnp.float32)
    t_now = 1.0 - step_f / STEPS
    t_after = 1.0 - (step_f + 1.0) / STEPS
    delta = noise_level(t_after) - noise_level(t_now)
    latent_next = latent + delta * velocity_flat
    denoised = latent - noise_level(t_now) * velocity_flat
    return (img_next, txt_next, velocity_flat, latent_next, denoised)


def solution(mesh):
    placed = (
        P(("req", "seq"), "tp"),
        P(("req", "seq"), "tp"),
        P("req", None),
        P("req", None),
        P("seq", None, "tp"),
        P("seq", None, "tp"),
        P(),
        P("tp", "seq"),
        P("tp", "seq"),
        P("req", None),
        P("tp", None),
        P(),
        P(("req", "seq"), "tp"),
        P("req"),
        P("req"),
    )
    return jax.shard_map(
        per_device,
        mesh=mesh,
        in_specs=placed,
        out_specs=(
            P(("req", "seq"), "tp"),
            P(("req", "seq"), "tp"),
            P(("req", "seq"), "tp"),
            P(("req", "seq"), "tp"),
            P(("req", "seq"), "tp"),
        ),
        check_vma=False,
    )
```

```python
import functools
import math

import jax
import jax.numpy as jnp
from jax import lax
from jax.experimental import pallas as pl
from jax.sharding import PartitionSpec as P

STEPS = 28


EPS = 1e-06
SHIFT_MU = 1.15
THETA = 10000.0


def extended(block, sides, width):
    for axis, dim in sides:
        count = lax.axis_size(axis)
        forward = [(i, i + 1) for i in range(count - 1)]
        backward = [(target, source) for source, target in forward]
        low = lax.ppermute(
            lax.slice_in_dim(block, block.shape[dim] - width, None, axis=dim), axis, forward
        )
        high = lax.ppermute(lax.slice_in_dim(block, 0, width, axis=dim), axis, backward)
        block = jnp.concatenate([low, block, high], axis=dim)
    return block


def tree_sum(block, axis):
    count = lax.axis_size(axis)
    step = 1
    while step < count:
        block = block + lax.ppermute(block, axis, [(i, i ^ step) for i in range(count)])
        step *= 2
    return block


def halving_sum(block, axis, dim):
    count = lax.axis_size(axis)
    at = lax.axis_index(axis)
    step = count // 2
    while step >= 1:
        half = block.shape[dim] // 2
        low = lax.slice_in_dim(block, 0, half, axis=dim)
        high = lax.slice_in_dim(block, half, None, axis=dim)
        upper = (at // step) % 2 == 1
        kept = jnp.where(upper, high, low)
        sent = jnp.where(upper, low, high)
        block = kept + lax.ppermute(sent, axis, [(i, i ^ step) for i in range(count)])
        step //= 2
    return block


def attend_block(keep_ref, query_ref, tkey_ref, tvalue_ref, ikey_ref, ivalue_ref, out_ref, *, scale):
    query = query_ref[...]
    contract = (((1,), (1,)), ((), ()))
    text_scores = (
        lax.dot_general(query, tkey_ref[...], contract, preferred_element_type=jnp.float32) * scale
    )
    text_scores = jnp.where(keep_ref[...] > 0.5, text_scores, -1e30)
    img_scores = (
        lax.dot_general(query, ikey_ref[...], contract, preferred_element_type=jnp.float32) * scale
    )
    peak = jnp.maximum(
        jnp.max(text_scores, -1, keepdims=True), jnp.max(img_scores, -1, keepdims=True)
    )
    text_weights = jnp.exp(text_scores - peak)
    img_weights = jnp.exp(img_scores - peak)
    summed = jnp.sum(text_weights, -1, keepdims=True) + jnp.sum(img_weights, -1, keepdims=True)
    mixed_v = jnp.dot(
        text_weights.astype(jnp.bfloat16), tvalue_ref[...], preferred_element_type=jnp.float32
    ) + jnp.dot(img_weights.astype(jnp.bfloat16), ivalue_ref[...], preferred_element_type=jnp.float32)
    out_ref[...] = (mixed_v / summed).astype(out_ref.dtype)


def attention(keep, queries, text_kv, img_kv, head_dim, q_tile):
    rows = queries.shape[0]
    text_total = text_kv.shape[0]
    img_total = img_kv.shape[0]
    heads = queries.shape[1] // head_dim
    return pl.pallas_call(
        functools.partial(attend_block, scale=head_dim ** (-0.5)),
        grid=(heads, rows // q_tile),
        in_specs=[
            pl.BlockSpec((1, text_total), lambda h, i: (0, 0)),
            pl.BlockSpec((q_tile, head_dim), lambda h, i: (i, h)),
            pl.BlockSpec((text_total, head_dim), lambda h, i: (0, h)),
            pl.BlockSpec((text_total, head_dim), lambda h, i: (0, h + heads)),
            pl.BlockSpec((img_total, head_dim), lambda h, i: (0, h)),
            pl.BlockSpec((img_total, head_dim), lambda h, i: (0, h + heads)),
        ],
        out_specs=pl.BlockSpec((q_tile, head_dim), lambda h, i: (i, h)),
        out_shape=jax.ShapeDtypeStruct(queries.shape, jnp.bfloat16),
    )(keep, queries, text_kv, text_kv, img_kv, img_kv)


def bit_of(value, step):
    return (value // step) % 2


def doubling_gather(block, axis, dim, order):
    count = lax.axis_size(axis)
    at = lax.axis_index(axis)
    stacked = block[None]
    for step in order:
        other = lax.ppermute(stacked, axis, [(i, i ^ step) for i in range(count)])
        upper = bit_of(at, step) == 1
        stacked = jnp.stack([jnp.where(upper, other, stacked), jnp.where(upper, stacked, other)])
        stacked = stacked.reshape((-1,) + block.shape)
    rank = len(order)
    source = [sum(((p >> k) & 1) * order[k] for k in range(rank)) for p in range(count)]
    place = [source.index(d) for d in range(count)]
    picked = jnp.stack([stacked[p] for p in place], 0)
    moved = jnp.moveaxis(picked, 0, dim)
    shape = list(block.shape)
    shape[dim] *= count
    return moved.reshape(shape)


def halving_scatter(block, axis, dim, order):
    count = lax.axis_size(axis)
    at = lax.axis_index(axis)
    rank = len(order)
    width = block.shape[dim] // count
    pieces = [lax.slice_in_dim(block, d * width, (d + 1) * width, axis=dim) for d in range(count)]
    slots = [sum(((d // order[k]) % 2) << (rank - 1 - k) for k in range(rank)) for d in range(count)]
    arranged = [None] * count
    for d in range(count):
        arranged[slots[d]] = pieces[d]
    block = jnp.concatenate(arranged, dim)
    for step in order:
        half = block.shape[dim] // 2
        low = lax.slice_in_dim(block, 0, half, axis=dim)
        high = lax.slice_in_dim(block, half, None, axis=dim)
        upper = bit_of(at, step) == 1
        kept = jnp.where(upper, high, low)
        sent = jnp.where(upper, low, high)
        block = kept + lax.ppermute(sent, axis, [(i, i ^ step) for i in range(count)])
    return block


def transpose_devices(block):
    side = lax.axis_size("tp")
    swap = [(a * side + b, b * side + a) for a in range(side) for b in range(side)]
    return lax.ppermute(block, ("seq", "tp"), swap)


def modulate(hidden, mod_rows):
    values = hidden.astype(jnp.float32)
    mod_f = mod_rows.astype(jnp.float32)
    row_mean = jnp.mean(values, -1, keepdims=True)
    row_var = jnp.mean((values - row_mean) ** 2, -1, keepdims=True)
    normed = (values - row_mean) * lax.rsqrt(row_var + EPS)
    return (normed * (1.0 + mod_f[1]) + mod_f[0]).astype(jnp.bfloat16)


def rms_gain(values, gain_row):
    return values * lax.rsqrt(jnp.mean(values * values, -1, keepdims=True) + EPS) * gain_row


def rope_angles(row_pos, col_pos, head_dim):
    lead = head_dim // 16
    span = 7 * head_dim // 32
    freq = THETA ** (-jnp.arange(span, dtype=jnp.float32) / span)
    zero_part = jnp.zeros((row_pos.shape[0], lead), jnp.float32)
    return jnp.concatenate(
        [zero_part, row_pos[:, None] * freq[None], col_pos[:, None] * freq[None]], 1
    )


def apply_rope(values, angles):
    count, heads_n, head_dim = values.shape
    pairs = values.reshape(count, heads_n, head_dim // 2, 2)
    first = pairs[..., 0]
    second = pairs[..., 1]
    cosine = jnp.cos(angles)[:, None, :]
    sine = jnp.sin(angles)[:, None, :]
    turned = jnp.stack([first * cosine - second * sine, first * sine + second * cosine], -1)
    return turned.reshape(values.shape)


def split_heads(mixed, gain_q, gain_k, angles):
    head_dim = gain_q.shape[0]
    shaped = mixed.reshape(mixed.shape[0], 3, -1, head_dim)
    query = rms_gain(shaped[:, 0], gain_q)
    keyed = rms_gain(shaped[:, 1], gain_k)
    if angles is not None:
        query = apply_rope(query, angles)
        keyed = apply_rope(keyed, angles)
    return (
        query.astype(jnp.bfloat16),
        keyed.astype(jnp.bfloat16),
        shaped[:, 2].astype(jnp.bfloat16),
    )


def noise_level(tval):
    factor = math.exp(SHIFT_MU)
    return factor * tval / (factor * tval + 1.0 - tval)


def add_rows(normed, piece):
    flat_piece = piece.reshape(piece.shape[0], piece.shape[1] * piece.shape[2])
    return jnp.dot(normed, flat_piece, preferred_element_type=jnp.float32)


def per_device(
    img_hidden,
    txt_hidden,
    img_mod,
    txt_mod,
    img_qkv,
    txt_qkv,
    qk_gains,
    img_out_w,
    txt_out_w,
    final_mod,
    final_w,
    conv_w,
    latent,
    text_len,
    step_index,
):
    seq_count = lax.axis_size("seq")
    seq_at = lax.axis_index("seq")
    tp_at = lax.axis_index("tp")
    img_rows = img_hidden.shape[0]
    txt_rows = txt_hidden.shape[0]
    local_width = img_hidden.shape[1]
    img_full, txt_full = (
        lax.all_gather(img_hidden, "tp", axis=1, tiled=True),
        lax.all_gather(txt_hidden, "tp", axis=1, tiled=True),
    )
    full_width = img_full.shape[1]
    img_norm = modulate(img_full, img_mod)
    txt_norm = modulate(txt_full, txt_mod)
    img_weights = lax.all_gather(img_qkv, "seq", axis=0, tiled=True)
    img_weights, img_out_w = lax.optimization_barrier((img_weights, img_out_w))
    img_out_full = lax.all_gather(img_out_w, "seq", axis=1, tiled=True)
    img_mixed = add_rows(img_norm, img_weights)
    txt_norm, img_norm = lax.optimization_barrier((txt_norm, img_norm))
    txt_norm_rows = lax.all_to_all(txt_norm, "seq", 1, 0, tiled=True)
    txt_mixed = lax.psum_scatter(
        add_rows(txt_norm_rows, txt_qkv), "seq", scatter_dimension=0, tiled=True
    )
    head_dim = qk_gains.shape[1]
    grid_side = latent.shape[0] * seq_count
    token_ids = seq_at * img_rows + jnp.arange(img_rows, dtype=jnp.int32)
    row_pos = (token_ids // grid_side).astype(jnp.float32)
    col_pos = (token_ids % grid_side).astype(jnp.float32)
    angles = rope_angles(row_pos, col_pos, head_dim)
    img_query, img_key, img_value = split_heads(img_mixed, qk_gains[0], qk_gains[1], angles)
    txt_query, txt_key, txt_value = split_heads(txt_mixed, qk_gains[2], qk_gains[3], None)
    local_len = txt_rows + img_rows
    heads_local = img_query.shape[1]
    kv_width = heads_local * head_dim
    queries = jnp.concatenate([txt_query, img_query], 0).reshape(local_len, kv_width)
    img_kv = lax.all_gather(
        jnp.concatenate(
            [img_key.reshape(img_rows, kv_width), img_value.reshape(img_rows, kv_width)], 1
        ),
        "seq",
        axis=0,
        tiled=True,
    )
    text_kv = lax.all_gather(
        jnp.concatenate(
            [txt_key.reshape(txt_rows, kv_width), txt_value.reshape(txt_rows, kv_width)], 1
        ),
        "seq",
        axis=0,
        tiled=True,
    )
    limit = text_len[0]
    keep = (jnp.arange(text_kv.shape[0], dtype=jnp.int32) < limit).astype(jnp.float32)[None, :]
    attn = attention(keep, queries, text_kv, img_kv, head_dim, local_len // 3)
    txt_attn = attn[:txt_rows]
    img_attn = attn[txt_rows:]
    img_term = jnp.dot(
        img_attn,
        img_out_full,
        preferred_element_type=jnp.float32,
    )
    txt_term = jnp.dot(
        doubling_gather(txt_attn, "seq", 0, (2, 1, 4)),
        txt_out_w,
        preferred_element_type=jnp.float32,
    )
    txt_out = transpose_devices(
        halving_scatter(txt_term.astype(jnp.bfloat16).astype(jnp.float32), "tp", 0, (1, 2, 4))
    )
    img_out = lax.psum_scatter(
        img_term.astype(jnp.bfloat16), "tp", scatter_dimension=1, tiled=True
    ).astype(jnp.float32)
    img_gate = lax.dynamic_slice_in_dim(
        img_mod.astype(jnp.float32)[2], tp_at * local_width, local_width
    )
    txt_gate = lax.dynamic_slice_in_dim(
        txt_mod.astype(jnp.float32)[2], tp_at * local_width, local_width
    )
    img_next = (img_hidden.astype(jnp.float32) + img_gate * img_out).astype(jnp.bfloat16)
    text_valid = seq_at * txt_rows + jnp.arange(txt_rows, dtype=jnp.int32) < limit
    txt_base = txt_hidden.astype(jnp.float32)
    txt_next = jnp.where(text_valid[:, None], txt_base + txt_gate * txt_out, txt_base).astype(
        jnp.bfloat16
    )
    shift_row = lax.dynamic_slice_in_dim(final_mod[0], tp_at * local_width, local_width)
    scale_row = lax.dynamic_slice_in_dim(final_mod[1], tp_at * local_width, local_width)
    final_shift = shift_row.astype(jnp.float32)
    final_scale = scale_row.astype(jnp.float32)
    weight_final = final_w.astype(jnp.float32)
    values = img_next.astype(jnp.float32)
    channels = final_w.shape[1]
    final_gain = 1.0 + final_scale
    high = lax.Precision.HIGHEST
    lifted = jnp.dot(values * final_gain, weight_final, precision=high)
    consts = jnp.stack(
        [jnp.dot(final_gain, weight_final, precision=high), jnp.dot(final_shift, weight_final, precision=high)]
    )
    packed = jnp.concatenate(
        [
            jnp.concatenate([lifted, jnp.sum(values, -1)[:, None], jnp.sum(values * values, -1)[:, None]], 1),
            jnp.pad(consts, ((0, 0), (0, 2))),
        ],
        0,
    )
    packed = tree_sum(packed, "tp")
    lifted = packed[:img_rows, :channels]
    row_mean = packed[:img_rows, channels] / full_width
    row_var = packed[:img_rows, channels + 1] / full_width - row_mean * row_mean
    row_scale = lax.rsqrt(row_var + EPS)[:, None]
    patch = row_scale * (lifted - row_mean[:, None] * packed[img_rows, :channels]) + packed[
        img_rows + 1, :channels
    ]
    band_rows = latent.shape[0]
    patch_band = patch.astype(jnp.bfloat16).reshape(band_rows, grid_side * channels)
    rimmed = extended(patch_band, (("seq", 0),), 1)
    col_width = latent.shape[1] // channels
    framed = jnp.pad(rimmed.reshape(band_rows + 2, grid_side, channels), ((0, 0), (1, 1), (0, 0)))
    window = lax.dynamic_slice_in_dim(framed, tp_at * col_width, col_width + 2, 1)
    velocity = jnp.zeros((band_rows, col_width, channels), jnp.float32)
    for row_shift in range(3):
        for col_shift in range(3):
            velocity = velocity + jnp.einsum(
                "rci,io->rco",
                window[row_shift : row_shift + band_rows, col_shift : col_shift + col_width],
                conv_w[row_shift, col_shift],
                preferred_element_type=jnp.float32,
            )
    velocity_flat = velocity.reshape(band_rows, col_width * channels)
    step_f = step_index[0].astype(jnp.float32)
    t_now = 1.0 - step_f / STEPS
    t_after = 1.0 - (step_f + 1.0) / STEPS
    delta = noise_level(t_after) - noise_level(t_now)
    latent_next = latent + delta * velocity_flat
    denoised = latent - noise_level(t_now) * velocity_flat
    return (img_next, txt_next, velocity_flat, latent_next, denoised)


def solution(mesh):
    placed = (
        P(("req", "seq"), "tp"),
        P(("req", "seq"), "tp"),
        P("req", None),
        P("req", None),
        P("seq", None, "tp"),
        P("seq", None, "tp"),
        P(),
        P("tp", "seq"),
        P("tp", "seq"),
        P("req", None),
        P("tp", None),
        P(),
        P(("req", "seq"), "tp"),
        P("req"),
        P("req"),
    )
    return jax.shard_map(
        per_device,
        mesh=mesh,
        in_specs=placed,
        out_specs=(
            P(("req", "seq"), "tp"),
            P(("req", "seq"), "tp"),
            P(("req", "seq"), "tp"),
            P(("req", "seq"), "tp"),
            P(("req", "seq"), "tp"),
        ),
        check_vma=False,
    )
```

```python
import functools
import math

import jax
import jax.numpy as jnp
from jax import lax
from jax.experimental import pallas as pl
from jax.sharding import PartitionSpec as P

STEPS = 28


EPS = 1e-06
SHIFT_MU = 1.15
THETA = 10000.0


def extended(block, sides, width):
    for axis, dim in sides:
        count = lax.axis_size(axis)
        forward = [(i, i + 1) for i in range(count - 1)]
        backward = [(target, source) for source, target in forward]
        low = lax.ppermute(
            lax.slice_in_dim(block, block.shape[dim] - width, None, axis=dim), axis, forward
        )
        high = lax.ppermute(lax.slice_in_dim(block, 0, width, axis=dim), axis, backward)
        block = jnp.concatenate([low, block, high], axis=dim)
    return block


def tree_sum(block, axis):
    count = lax.axis_size(axis)
    step = 1
    while step < count:
        block = block + lax.ppermute(block, axis, [(i, i ^ step) for i in range(count)])
        step *= 2
    return block


def halving_sum(block, axis, dim):
    count = lax.axis_size(axis)
    at = lax.axis_index(axis)
    step = count // 2
    while step >= 1:
        half = block.shape[dim] // 2
        low = lax.slice_in_dim(block, 0, half, axis=dim)
        high = lax.slice_in_dim(block, half, None, axis=dim)
        upper = (at // step) % 2 == 1
        kept = jnp.where(upper, high, low)
        sent = jnp.where(upper, low, high)
        block = kept + lax.ppermute(sent, axis, [(i, i ^ step) for i in range(count)])
        step //= 2
    return block


def attend_block(keep_ref, query_ref, tkey_ref, tvalue_ref, ikey_ref, ivalue_ref, out_ref, *, scale):
    query = query_ref[...]
    contract = (((1,), (1,)), ((), ()))
    text_scores = (
        lax.dot_general(query, tkey_ref[...], contract, preferred_element_type=jnp.float32) * scale
    )
    text_scores = jnp.where(keep_ref[...] > 0.5, text_scores, -1e30)
    img_scores = (
        lax.dot_general(query, ikey_ref[...], contract, preferred_element_type=jnp.float32) * scale
    )
    peak = jnp.maximum(
        jnp.max(text_scores, -1, keepdims=True), jnp.max(img_scores, -1, keepdims=True)
    )
    text_weights = jnp.exp(text_scores - peak)
    img_weights = jnp.exp(img_scores - peak)
    summed = jnp.sum(text_weights, -1, keepdims=True) + jnp.sum(img_weights, -1, keepdims=True)
    mixed_v = jnp.dot(
        text_weights.astype(jnp.bfloat16), tvalue_ref[...], preferred_element_type=jnp.float32
    ) + jnp.dot(img_weights.astype(jnp.bfloat16), ivalue_ref[...], preferred_element_type=jnp.float32)
    out_ref[...] = (mixed_v / summed).astype(out_ref.dtype)


def attention(keep, queries, text_kv, img_kv, head_dim, q_tile):
    rows = queries.shape[0]
    text_total = text_kv.shape[0]
    img_total = img_kv.shape[0]
    heads = queries.shape[1] // head_dim
    return pl.pallas_call(
        functools.partial(attend_block, scale=head_dim ** (-0.5)),
        grid=(heads, rows // q_tile),
        in_specs=[
            pl.BlockSpec((1, text_total), lambda h, i: (0, 0)),
            pl.BlockSpec((q_tile, head_dim), lambda h, i: (i, h)),
            pl.BlockSpec((text_total, head_dim), lambda h, i: (0, h)),
            pl.BlockSpec((text_total, head_dim), lambda h, i: (0, h + heads)),
            pl.BlockSpec((img_total, head_dim), lambda h, i: (0, h)),
            pl.BlockSpec((img_total, head_dim), lambda h, i: (0, h + heads)),
        ],
        out_specs=pl.BlockSpec((q_tile, head_dim), lambda h, i: (i, h)),
        out_shape=jax.ShapeDtypeStruct(queries.shape, jnp.bfloat16),
    )(keep, queries, text_kv, text_kv, img_kv, img_kv)


def bit_of(value, step):
    return (value // step) % 2


def doubling_gather(block, axis, dim, order):
    count = lax.axis_size(axis)
    at = lax.axis_index(axis)
    stacked = block[None]
    for step in order:
        other = lax.ppermute(stacked, axis, [(i, i ^ step) for i in range(count)])
        upper = bit_of(at, step) == 1
        stacked = jnp.stack([jnp.where(upper, other, stacked), jnp.where(upper, stacked, other)])
        stacked = stacked.reshape((-1,) + block.shape)
    rank = len(order)
    source = [sum(((p >> k) & 1) * order[k] for k in range(rank)) for p in range(count)]
    place = [source.index(d) for d in range(count)]
    picked = jnp.stack([stacked[p] for p in place], 0)
    moved = jnp.moveaxis(picked, 0, dim)
    shape = list(block.shape)
    shape[dim] *= count
    return moved.reshape(shape)


def halving_scatter(block, axis, dim, order):
    count = lax.axis_size(axis)
    at = lax.axis_index(axis)
    rank = len(order)
    width = block.shape[dim] // count
    pieces = [lax.slice_in_dim(block, d * width, (d + 1) * width, axis=dim) for d in range(count)]
    slots = [sum(((d // order[k]) % 2) << (rank - 1 - k) for k in range(rank)) for d in range(count)]
    arranged = [None] * count
    for d in range(count):
        arranged[slots[d]] = pieces[d]
    block = jnp.concatenate(arranged, dim)
    for step in order:
        half = block.shape[dim] // 2
        low = lax.slice_in_dim(block, 0, half, axis=dim)
        high = lax.slice_in_dim(block, half, None, axis=dim)
        upper = bit_of(at, step) == 1
        kept = jnp.where(upper, high, low)
        sent = jnp.where(upper, low, high)
        block = kept + lax.ppermute(sent, axis, [(i, i ^ step) for i in range(count)])
    return block


def transpose_devices(block):
    side = lax.axis_size("tp")
    swap = [(a * side + b, b * side + a) for a in range(side) for b in range(side)]
    return lax.ppermute(block, ("seq", "tp"), swap)


def modulate(hidden, mod_rows):
    values = hidden.astype(jnp.float32)
    mod_f = mod_rows.astype(jnp.float32)
    row_mean = jnp.mean(values, -1, keepdims=True)
    row_var = jnp.mean((values - row_mean) ** 2, -1, keepdims=True)
    normed = (values - row_mean) * lax.rsqrt(row_var + EPS)
    return (normed * (1.0 + mod_f[1]) + mod_f[0]).astype(jnp.bfloat16)


def rms_gain(values, gain_row):
    return values * lax.rsqrt(jnp.mean(values * values, -1, keepdims=True) + EPS) * gain_row


def rope_angles(row_pos, col_pos, head_dim):
    lead = head_dim // 16
    span = 7 * head_dim // 32
    freq = THETA ** (-jnp.arange(span, dtype=jnp.float32) / span)
    zero_part = jnp.zeros((row_pos.shape[0], lead), jnp.float32)
    return jnp.concatenate(
        [zero_part, row_pos[:, None] * freq[None], col_pos[:, None] * freq[None]], 1
    )


def apply_rope(values, angles):
    count, heads_n, head_dim = values.shape
    pairs = values.reshape(count, heads_n, head_dim // 2, 2)
    first = pairs[..., 0]
    second = pairs[..., 1]
    cosine = jnp.cos(angles)[:, None, :]
    sine = jnp.sin(angles)[:, None, :]
    turned = jnp.stack([first * cosine - second * sine, first * sine + second * cosine], -1)
    return turned.reshape(values.shape)


def split_heads(mixed, gain_q, gain_k, angles):
    head_dim = gain_q.shape[0]
    shaped = mixed.reshape(mixed.shape[0], 3, -1, head_dim)
    query = rms_gain(shaped[:, 0], gain_q)
    keyed = rms_gain(shaped[:, 1], gain_k)
    if angles is not None:
        query = apply_rope(query, angles)
        keyed = apply_rope(keyed, angles)
    return (
        query.astype(jnp.bfloat16),
        keyed.astype(jnp.bfloat16),
        shaped[:, 2].astype(jnp.bfloat16),
    )


def noise_level(tval):
    factor = math.exp(SHIFT_MU)
    return factor * tval / (factor * tval + 1.0 - tval)


def add_rows(normed, piece):
    flat_piece = piece.reshape(piece.shape[0], piece.shape[1] * piece.shape[2])
    return jnp.dot(normed, flat_piece, preferred_element_type=jnp.float32)


def per_device(
    img_hidden,
    txt_hidden,
    img_mod,
    txt_mod,
    img_qkv,
    txt_qkv,
    qk_gains,
    img_out_w,
    txt_out_w,
    final_mod,
    final_w,
    conv_w,
    latent,
    text_len,
    step_index,
):
    seq_count = lax.axis_size("seq")
    seq_at = lax.axis_index("seq")
    tp_at = lax.axis_index("tp")
    img_rows = img_hidden.shape[0]
    txt_rows = txt_hidden.shape[0]
    local_width = img_hidden.shape[1]
    img_full, txt_full = (
        lax.all_gather(img_hidden, "tp", axis=1, tiled=True),
        lax.all_gather(txt_hidden, "tp", axis=1, tiled=True),
    )
    full_width = img_full.shape[1]
    img_norm = modulate(img_full, img_mod)
    txt_norm = modulate(txt_full, txt_mod)
    img_weights = lax.all_gather(img_qkv, "seq", axis=0, tiled=True)
    img_mixed = add_rows(img_norm, img_weights)
    txt_norm, img_norm = lax.optimization_barrier((txt_norm, img_norm))
    txt_norm_rows = lax.all_to_all(txt_norm, "seq", 1, 0, tiled=True)
    txt_mixed = lax.psum_scatter(
        add_rows(txt_norm_rows, txt_qkv), "seq", scatter_dimension=0, tiled=True
    )
    head_dim = qk_gains.shape[1]
    grid_side = latent.shape[0] * seq_count
    token_ids = seq_at * img_rows + jnp.arange(img_rows, dtype=jnp.int32)
    row_pos = (token_ids // grid_side).astype(jnp.float32)
    col_pos = (token_ids % grid_side).astype(jnp.float32)
    angles = rope_angles(row_pos, col_pos, head_dim)
    img_query, img_key, img_value = split_heads(img_mixed, qk_gains[0], qk_gains[1], angles)
    txt_query, txt_key, txt_value = split_heads(txt_mixed, qk_gains[2], qk_gains[3], None)
    local_len = txt_rows + img_rows
    heads_local = img_query.shape[1]
    kv_width = heads_local * head_dim
    queries = jnp.concatenate([txt_query, img_query], 0).reshape(local_len, kv_width)
    img_kv = lax.all_gather(
        jnp.concatenate(
            [img_key.reshape(img_rows, kv_width), img_value.reshape(img_rows, kv_width)], 1
        ),
        "seq",
        axis=0,
        tiled=True,
    )
    text_kv = lax.all_gather(
        jnp.concatenate(
            [txt_key.reshape(txt_rows, kv_width), txt_value.reshape(txt_rows, kv_width)], 1
        ),
        "seq",
        axis=0,
        tiled=True,
    )
    img_kv, img_out_w = lax.optimization_barrier((img_kv, img_out_w))
    img_out_full = doubling_gather(img_out_w, "seq", 1, (2, 1, 4))
    limit = text_len[0]
    keep = (jnp.arange(text_kv.shape[0], dtype=jnp.int32) < limit).astype(jnp.float32)[None, :]
    attn = attention(keep, queries, text_kv, img_kv, head_dim, local_len // 3)
    txt_attn = attn[:txt_rows]
    img_attn = attn[txt_rows:]
    img_term = jnp.dot(
        img_attn,
        img_out_full,
        preferred_element_type=jnp.float32,
    )
    txt_term = jnp.dot(
        doubling_gather(txt_attn, "seq", 0, (2, 1, 4)),
        txt_out_w,
        preferred_element_type=jnp.float32,
    )
    txt_out = transpose_devices(
        halving_scatter(txt_term.astype(jnp.bfloat16).astype(jnp.float32), "tp", 0, (1, 2, 4))
    )
    img_out = lax.psum_scatter(
        img_term.astype(jnp.bfloat16), "tp", scatter_dimension=1, tiled=True
    ).astype(jnp.float32)
    img_gate = lax.dynamic_slice_in_dim(
        img_mod.astype(jnp.float32)[2], tp_at * local_width, local_width
    )
    txt_gate = lax.dynamic_slice_in_dim(
        txt_mod.astype(jnp.float32)[2], tp_at * local_width, local_width
    )
    img_next = (img_hidden.astype(jnp.float32) + img_gate * img_out).astype(jnp.bfloat16)
    text_valid = seq_at * txt_rows + jnp.arange(txt_rows, dtype=jnp.int32) < limit
    txt_base = txt_hidden.astype(jnp.float32)
    txt_next = jnp.where(text_valid[:, None], txt_base + txt_gate * txt_out, txt_base).astype(
        jnp.bfloat16
    )
    shift_row = lax.dynamic_slice_in_dim(final_mod[0], tp_at * local_width, local_width)
    scale_row = lax.dynamic_slice_in_dim(final_mod[1], tp_at * local_width, local_width)
    final_shift = shift_row.astype(jnp.float32)
    final_scale = scale_row.astype(jnp.float32)
    weight_final = final_w.astype(jnp.float32)
    values = img_next.astype(jnp.float32)
    channels = final_w.shape[1]
    final_gain = 1.0 + final_scale
    high = lax.Precision.HIGHEST
    lifted = jnp.dot(values * final_gain, weight_final, precision=high)
    consts = jnp.stack(
        [jnp.dot(final_gain, weight_final, precision=high), jnp.dot(final_shift, weight_final, precision=high)]
    )
    packed = jnp.concatenate(
        [
            jnp.concatenate([lifted, jnp.sum(values, -1)[:, None], jnp.sum(values * values, -1)[:, None]], 1),
            jnp.pad(consts, ((0, 0), (0, 2))),
        ],
        0,
    )
    packed = tree_sum(packed, "tp")
    lifted = packed[:img_rows, :channels]
    row_mean = packed[:img_rows, channels] / full_width
    row_var = packed[:img_rows, channels + 1] / full_width - row_mean * row_mean
    row_scale = lax.rsqrt(row_var + EPS)[:, None]
    patch = row_scale * (lifted - row_mean[:, None] * packed[img_rows, :channels]) + packed[
        img_rows + 1, :channels
    ]
    band_rows = latent.shape[0]
    patch_band = patch.astype(jnp.bfloat16).reshape(band_rows, grid_side * channels)
    rimmed = extended(patch_band, (("seq", 0),), 1)
    col_width = latent.shape[1] // channels
    framed = jnp.pad(rimmed.reshape(band_rows + 2, grid_side, channels), ((0, 0), (1, 1), (0, 0)))
    window = lax.dynamic_slice_in_dim(framed, tp_at * col_width, col_width + 2, 1)
    velocity = jnp.zeros((band_rows, col_width, channels), jnp.float32)
    for row_shift in range(3):
        for col_shift in range(3):
            velocity = velocity + jnp.einsum(
                "rci,io->rco",
                window[row_shift : row_shift + band_rows, col_shift : col_shift + col_width],
                conv_w[row_shift, col_shift],
                preferred_element_type=jnp.float32,
            )
    velocity_flat = velocity.reshape(band_rows, col_width * channels)
    step_f = step_index[0].astype(jnp.float32)
    t_now = 1.0 - step_f / STEPS
    t_after = 1.0 - (step_f + 1.0) / STEPS
    delta = noise_level(t_after) - noise_level(t_now)
    latent_next = latent + delta * velocity_flat
    denoised = latent - noise_level(t_now) * velocity_flat
    return (img_next, txt_next, velocity_flat, latent_next, denoised)


def solution(mesh):
    placed = (
        P(("req", "seq"), "tp"),
        P(("req", "seq"), "tp"),
        P("req", None),
        P("req", None),
        P("seq", None, "tp"),
        P("seq", None, "tp"),
        P(),
        P("tp", "seq"),
        P("tp", "seq"),
        P("req", None),
        P("tp", None),
        P(),
        P(("req", "seq"), "tp"),
        P("req"),
        P("req"),
    )
    return jax.shard_map(
        per_device,
        mesh=mesh,
        in_specs=placed,
        out_specs=(
            P(("req", "seq"), "tp"),
            P(("req", "seq"), "tp"),
            P(("req", "seq"), "tp"),
            P(("req", "seq"), "tp"),
            P(("req", "seq"), "tp"),
        ),
        check_vma=False,
    )
```

```python
import functools
import math

import jax
import jax.numpy as jnp
from jax import lax
from jax.experimental import pallas as pl
from jax.sharding import PartitionSpec as P

STEPS = 28


EPS = 1e-06
SHIFT_MU = 1.15
THETA = 10000.0


def extended(block, sides, width):
    for axis, dim in sides:
        count = lax.axis_size(axis)
        forward = [(i, i + 1) for i in range(count - 1)]
        backward = [(target, source) for source, target in forward]
        low = lax.ppermute(
            lax.slice_in_dim(block, block.shape[dim] - width, None, axis=dim), axis, forward
        )
        high = lax.ppermute(lax.slice_in_dim(block, 0, width, axis=dim), axis, backward)
        block = jnp.concatenate([low, block, high], axis=dim)
    return block


def tree_sum(block, axis):
    count = lax.axis_size(axis)
    step = 1
    while step < count:
        block = block + lax.ppermute(block, axis, [(i, i ^ step) for i in range(count)])
        step *= 2
    return block


def halving_sum(block, axis, dim):
    count = lax.axis_size(axis)
    at = lax.axis_index(axis)
    step = count // 2
    while step >= 1:
        half = block.shape[dim] // 2
        low = lax.slice_in_dim(block, 0, half, axis=dim)
        high = lax.slice_in_dim(block, half, None, axis=dim)
        upper = (at // step) % 2 == 1
        kept = jnp.where(upper, high, low)
        sent = jnp.where(upper, low, high)
        block = kept + lax.ppermute(sent, axis, [(i, i ^ step) for i in range(count)])
        step //= 2
    return block


def attend_block(keep_ref, query_ref, tkey_ref, tvalue_ref, ikey_ref, ivalue_ref, out_ref, *, scale):
    query = query_ref[...]
    contract = (((1,), (1,)), ((), ()))
    text_scores = (
        lax.dot_general(query, tkey_ref[...], contract, preferred_element_type=jnp.float32) * scale
    )
    text_scores = jnp.where(keep_ref[...] > 0.5, text_scores, -1e30)
    img_scores = (
        lax.dot_general(query, ikey_ref[...], contract, preferred_element_type=jnp.float32) * scale
    )
    peak = jnp.maximum(
        jnp.max(text_scores, -1, keepdims=True), jnp.max(img_scores, -1, keepdims=True)
    )
    text_weights = jnp.exp(text_scores - peak)
    img_weights = jnp.exp(img_scores - peak)
    summed = jnp.sum(text_weights, -1, keepdims=True) + jnp.sum(img_weights, -1, keepdims=True)
    mixed_v = jnp.dot(
        text_weights.astype(jnp.bfloat16), tvalue_ref[...], preferred_element_type=jnp.float32
    ) + jnp.dot(img_weights.astype(jnp.bfloat16), ivalue_ref[...], preferred_element_type=jnp.float32)
    out_ref[...] = (mixed_v / summed).astype(out_ref.dtype)


def attention(keep, queries, text_kv, img_kv, head_dim, q_tile):
    rows = queries.shape[0]
    text_total = text_kv.shape[0]
    img_total = img_kv.shape[0]
    heads = queries.shape[1] // head_dim
    return pl.pallas_call(
        functools.partial(attend_block, scale=head_dim ** (-0.5)),
        grid=(heads, rows // q_tile),
        in_specs=[
            pl.BlockSpec((1, text_total), lambda h, i: (0, 0)),
            pl.BlockSpec((q_tile, head_dim), lambda h, i: (i, h)),
            pl.BlockSpec((text_total, head_dim), lambda h, i: (0, h)),
            pl.BlockSpec((text_total, head_dim), lambda h, i: (0, h + heads)),
            pl.BlockSpec((img_total, head_dim), lambda h, i: (0, h)),
            pl.BlockSpec((img_total, head_dim), lambda h, i: (0, h + heads)),
        ],
        out_specs=pl.BlockSpec((q_tile, head_dim), lambda h, i: (i, h)),
        out_shape=jax.ShapeDtypeStruct(queries.shape, jnp.bfloat16),
    )(keep, queries, text_kv, text_kv, img_kv, img_kv)


def bit_of(value, step):
    return (value // step) % 2


def doubling_gather(block, axis, dim, order):
    count = lax.axis_size(axis)
    at = lax.axis_index(axis)
    stacked = block[None]
    for step in order:
        other = lax.ppermute(stacked, axis, [(i, i ^ step) for i in range(count)])
        upper = bit_of(at, step) == 1
        stacked = jnp.stack([jnp.where(upper, other, stacked), jnp.where(upper, stacked, other)])
        stacked = stacked.reshape((-1,) + block.shape)
    rank = len(order)
    source = [sum(((p >> k) & 1) * order[k] for k in range(rank)) for p in range(count)]
    place = [source.index(d) for d in range(count)]
    picked = jnp.stack([stacked[p] for p in place], 0)
    moved = jnp.moveaxis(picked, 0, dim)
    shape = list(block.shape)
    shape[dim] *= count
    return moved.reshape(shape)


def halving_scatter(block, axis, dim, order):
    count = lax.axis_size(axis)
    at = lax.axis_index(axis)
    rank = len(order)
    width = block.shape[dim] // count
    pieces = [lax.slice_in_dim(block, d * width, (d + 1) * width, axis=dim) for d in range(count)]
    slots = [sum(((d // order[k]) % 2) << (rank - 1 - k) for k in range(rank)) for d in range(count)]
    arranged = [None] * count
    for d in range(count):
        arranged[slots[d]] = pieces[d]
    block = jnp.concatenate(arranged, dim)
    for step in order:
        half = block.shape[dim] // 2
        low = lax.slice_in_dim(block, 0, half, axis=dim)
        high = lax.slice_in_dim(block, half, None, axis=dim)
        upper = bit_of(at, step) == 1
        kept = jnp.where(upper, high, low)
        sent = jnp.where(upper, low, high)
        block = kept + lax.ppermute(sent, axis, [(i, i ^ step) for i in range(count)])
    return block


def transpose_devices(block):
    side = lax.axis_size("tp")
    swap = [(a * side + b, b * side + a) for a in range(side) for b in range(side)]
    return lax.ppermute(block, ("seq", "tp"), swap)


def modulate(hidden, mod_rows):
    values = hidden.astype(jnp.float32)
    mod_f = mod_rows.astype(jnp.float32)
    row_mean = jnp.mean(values, -1, keepdims=True)
    row_var = jnp.mean((values - row_mean) ** 2, -1, keepdims=True)
    normed = (values - row_mean) * lax.rsqrt(row_var + EPS)
    return (normed * (1.0 + mod_f[1]) + mod_f[0]).astype(jnp.bfloat16)


def rms_gain(values, gain_row):
    return values * lax.rsqrt(jnp.mean(values * values, -1, keepdims=True) + EPS) * gain_row


def rope_angles(row_pos, col_pos, head_dim):
    lead = head_dim // 16
    span = 7 * head_dim // 32
    freq = THETA ** (-jnp.arange(span, dtype=jnp.float32) / span)
    zero_part = jnp.zeros((row_pos.shape[0], lead), jnp.float32)
    return jnp.concatenate(
        [zero_part, row_pos[:, None] * freq[None], col_pos[:, None] * freq[None]], 1
    )


def apply_rope(values, angles):
    count, heads_n, head_dim = values.shape
    pairs = values.reshape(count, heads_n, head_dim // 2, 2)
    first = pairs[..., 0]
    second = pairs[..., 1]
    cosine = jnp.cos(angles)[:, None, :]
    sine = jnp.sin(angles)[:, None, :]
    turned = jnp.stack([first * cosine - second * sine, first * sine + second * cosine], -1)
    return turned.reshape(values.shape)


def split_heads(mixed, gain_q, gain_k, angles):
    head_dim = gain_q.shape[0]
    shaped = mixed.reshape(mixed.shape[0], 3, -1, head_dim)
    query = rms_gain(shaped[:, 0], gain_q)
    keyed = rms_gain(shaped[:, 1], gain_k)
    if angles is not None:
        query = apply_rope(query, angles)
        keyed = apply_rope(keyed, angles)
    return (
        query.astype(jnp.bfloat16),
        keyed.astype(jnp.bfloat16),
        shaped[:, 2].astype(jnp.bfloat16),
    )


def noise_level(tval):
    factor = math.exp(SHIFT_MU)
    return factor * tval / (factor * tval + 1.0 - tval)


def add_rows(normed, piece):
    flat_piece = piece.reshape(piece.shape[0], piece.shape[1] * piece.shape[2])
    return jnp.dot(normed, flat_piece, preferred_element_type=jnp.float32)


def per_device(
    img_hidden,
    txt_hidden,
    img_mod,
    txt_mod,
    img_qkv,
    txt_qkv,
    qk_gains,
    img_out_w,
    txt_out_w,
    final_mod,
    final_w,
    conv_w,
    latent,
    text_len,
    step_index,
):
    seq_count = lax.axis_size("seq")
    seq_at = lax.axis_index("seq")
    tp_at = lax.axis_index("tp")
    img_rows = img_hidden.shape[0]
    txt_rows = txt_hidden.shape[0]
    local_width = img_hidden.shape[1]
    img_full, txt_full = (
        lax.all_gather(img_hidden, "tp", axis=1, tiled=True),
        lax.all_gather(txt_hidden, "tp", axis=1, tiled=True),
    )
    full_width = img_full.shape[1]
    img_norm = modulate(img_full, img_mod)
    txt_norm = modulate(txt_full, txt_mod)
    img_weights = lax.all_gather(img_qkv, "seq", axis=0, tiled=True)
    img_weights, img_out_w = lax.optimization_barrier((img_weights, img_out_w))
    img_out_full = lax.all_gather(img_out_w, "seq", axis=1, tiled=True)
    img_mixed = add_rows(img_norm, img_weights)
    txt_norm, img_norm = lax.optimization_barrier((txt_norm, img_norm))
    txt_norm_rows = lax.all_to_all(txt_norm, "seq", 1, 0, tiled=True)
    txt_mixed = halving_scatter(add_rows(txt_norm_rows, txt_qkv), "seq", 0, (4, 1, 2))
    head_dim = qk_gains.shape[1]
    grid_side = latent.shape[0] * seq_count
    token_ids = seq_at * img_rows + jnp.arange(img_rows, dtype=jnp.int32)
    row_pos = (token_ids // grid_side).astype(jnp.float32)
    col_pos = (token_ids % grid_side).astype(jnp.float32)
    angles = rope_angles(row_pos, col_pos, head_dim)
    img_query, img_key, img_value = split_heads(img_mixed, qk_gains[0], qk_gains[1], angles)
    txt_query, txt_key, txt_value = split_heads(txt_mixed, qk_gains[2], qk_gains[3], None)
    local_len = txt_rows + img_rows
    heads_local = img_query.shape[1]
    kv_width = heads_local * head_dim
    queries = jnp.concatenate([txt_query, img_query], 0).reshape(local_len, kv_width)
    img_kv = lax.all_gather(
        jnp.concatenate(
            [img_key.reshape(img_rows, kv_width), img_value.reshape(img_rows, kv_width)], 1
        ),
        "seq",
        axis=0,
        tiled=True,
    )
    text_kv = lax.all_gather(
        jnp.concatenate(
            [txt_key.reshape(txt_rows, kv_width), txt_value.reshape(txt_rows, kv_width)], 1
        ),
        "seq",
        axis=0,
        tiled=True,
    )
    limit = text_len[0]
    keep = (jnp.arange(text_kv.shape[0], dtype=jnp.int32) < limit).astype(jnp.float32)[None, :]
    attn = attention(keep, queries, text_kv, img_kv, head_dim, local_len // 3)
    txt_attn = attn[:txt_rows]
    img_attn = attn[txt_rows:]
    img_term = jnp.dot(
        img_attn,
        img_out_full,
        preferred_element_type=jnp.float32,
    )
    txt_term = jnp.dot(
        doubling_gather(txt_attn, "seq", 0, (2, 1, 4)),
        txt_out_w,
        preferred_element_type=jnp.float32,
    )
    txt_out = transpose_devices(
        halving_scatter(txt_term.astype(jnp.bfloat16).astype(jnp.float32), "tp", 0, (1, 2, 4))
    )
    img_out = lax.psum_scatter(
        img_term.astype(jnp.bfloat16), "tp", scatter_dimension=1, tiled=True
    ).astype(jnp.float32)
    img_gate = lax.dynamic_slice_in_dim(
        img_mod.astype(jnp.float32)[2], tp_at * local_width, local_width
    )
    txt_gate = lax.dynamic_slice_in_dim(
        txt_mod.astype(jnp.float32)[2], tp_at * local_width, local_width
    )
    img_next = (img_hidden.astype(jnp.float32) + img_gate * img_out).astype(jnp.bfloat16)
    text_valid = seq_at * txt_rows + jnp.arange(txt_rows, dtype=jnp.int32) < limit
    txt_base = txt_hidden.astype(jnp.float32)
    txt_next = jnp.where(text_valid[:, None], txt_base + txt_gate * txt_out, txt_base).astype(
        jnp.bfloat16
    )
    shift_row = lax.dynamic_slice_in_dim(final_mod[0], tp_at * local_width, local_width)
    scale_row = lax.dynamic_slice_in_dim(final_mod[1], tp_at * local_width, local_width)
    final_shift = shift_row.astype(jnp.float32)
    final_scale = scale_row.astype(jnp.float32)
    weight_final = final_w.astype(jnp.float32)
    values = img_next.astype(jnp.float32)
    channels = final_w.shape[1]
    final_gain = 1.0 + final_scale
    high = lax.Precision.HIGHEST
    lifted = jnp.dot(values * final_gain, weight_final, precision=high)
    consts = jnp.stack(
        [jnp.dot(final_gain, weight_final, precision=high), jnp.dot(final_shift, weight_final, precision=high)]
    )
    packed = jnp.concatenate(
        [
            jnp.concatenate([lifted, jnp.sum(values, -1)[:, None], jnp.sum(values * values, -1)[:, None]], 1),
            jnp.pad(consts, ((0, 0), (0, 2))),
        ],
        0,
    )
    packed = tree_sum(packed, "tp")
    lifted = packed[:img_rows, :channels]
    row_mean = packed[:img_rows, channels] / full_width
    row_var = packed[:img_rows, channels + 1] / full_width - row_mean * row_mean
    row_scale = lax.rsqrt(row_var + EPS)[:, None]
    patch = row_scale * (lifted - row_mean[:, None] * packed[img_rows, :channels]) + packed[
        img_rows + 1, :channels
    ]
    band_rows = latent.shape[0]
    patch_band = patch.astype(jnp.bfloat16).reshape(band_rows, grid_side * channels)
    rimmed = extended(patch_band, (("seq", 0),), 1)
    col_width = latent.shape[1] // channels
    framed = jnp.pad(rimmed.reshape(band_rows + 2, grid_side, channels), ((0, 0), (1, 1), (0, 0)))
    window = lax.dynamic_slice_in_dim(framed, tp_at * col_width, col_width + 2, 1)
    velocity = jnp.zeros((band_rows, col_width, channels), jnp.float32)
    for row_shift in range(3):
        for col_shift in range(3):
            velocity = velocity + jnp.einsum(
                "rci,io->rco",
                window[row_shift : row_shift + band_rows, col_shift : col_shift + col_width],
                conv_w[row_shift, col_shift],
                preferred_element_type=jnp.float32,
            )
    velocity_flat = velocity.reshape(band_rows, col_width * channels)
    step_f = step_index[0].astype(jnp.float32)
    t_now = 1.0 - step_f / STEPS
    t_after = 1.0 - (step_f + 1.0) / STEPS
    delta = noise_level(t_after) - noise_level(t_now)
    latent_next = latent + delta * velocity_flat
    denoised = latent - noise_level(t_now) * velocity_flat
    return (img_next, txt_next, velocity_flat, latent_next, denoised)


def solution(mesh):
    placed = (
        P(("req", "seq"), "tp"),
        P(("req", "seq"), "tp"),
        P("req", None),
        P("req", None),
        P("seq", None, "tp"),
        P("seq", None, "tp"),
        P(),
        P("tp", "seq"),
        P("tp", "seq"),
        P("req", None),
        P("tp", None),
        P(),
        P(("req", "seq"), "tp"),
        P("req"),
        P("req"),
    )
    return jax.shard_map(
        per_device,
        mesh=mesh,
        in_specs=placed,
        out_specs=(
            P(("req", "seq"), "tp"),
            P(("req", "seq"), "tp"),
            P(("req", "seq"), "tp"),
            P(("req", "seq"), "tp"),
            P(("req", "seq"), "tp"),
        ),
        check_vma=False,
    )
```

```python
import functools
import math

import jax
import jax.numpy as jnp
from jax import lax
from jax.experimental import pallas as pl
from jax.sharding import PartitionSpec as P

STEPS = 28


EPS = 1e-06
SHIFT_MU = 1.15
THETA = 10000.0


def extended(block, sides, width):
    for axis, dim in sides:
        count = lax.axis_size(axis)
        forward = [(i, i + 1) for i in range(count - 1)]
        backward = [(target, source) for source, target in forward]
        low = lax.ppermute(
            lax.slice_in_dim(block, block.shape[dim] - width, None, axis=dim), axis, forward
        )
        high = lax.ppermute(lax.slice_in_dim(block, 0, width, axis=dim), axis, backward)
        block = jnp.concatenate([low, block, high], axis=dim)
    return block


def tree_sum(block, axis):
    count = lax.axis_size(axis)
    step = 1
    while step < count:
        block = block + lax.ppermute(block, axis, [(i, i ^ step) for i in range(count)])
        step *= 2
    return block


def halving_sum(block, axis, dim):
    count = lax.axis_size(axis)
    at = lax.axis_index(axis)
    step = count // 2
    while step >= 1:
        half = block.shape[dim] // 2
        low = lax.slice_in_dim(block, 0, half, axis=dim)
        high = lax.slice_in_dim(block, half, None, axis=dim)
        upper = (at // step) % 2 == 1
        kept = jnp.where(upper, high, low)
        sent = jnp.where(upper, low, high)
        block = kept + lax.ppermute(sent, axis, [(i, i ^ step) for i in range(count)])
        step //= 2
    return block


def attend_block(keep_ref, query_ref, tkey_ref, tvalue_ref, ikey_ref, ivalue_ref, out_ref, *, scale):
    query = query_ref[...]
    contract = (((1,), (1,)), ((), ()))
    text_scores = (
        lax.dot_general(query, tkey_ref[...], contract, preferred_element_type=jnp.float32) * scale
    )
    text_scores = jnp.where(keep_ref[...] > 0.5, text_scores, -1e30)
    img_scores = (
        lax.dot_general(query, ikey_ref[...], contract, preferred_element_type=jnp.float32) * scale
    )
    peak = jnp.maximum(
        jnp.max(text_scores, -1, keepdims=True), jnp.max(img_scores, -1, keepdims=True)
    )
    text_weights = jnp.exp(text_scores - peak)
    img_weights = jnp.exp(img_scores - peak)
    summed = jnp.sum(text_weights, -1, keepdims=True) + jnp.sum(img_weights, -1, keepdims=True)
    mixed_v = jnp.dot(
        text_weights.astype(jnp.bfloat16), tvalue_ref[...], preferred_element_type=jnp.float32
    ) + jnp.dot(img_weights.astype(jnp.bfloat16), ivalue_ref[...], preferred_element_type=jnp.float32)
    out_ref[...] = (mixed_v / summed).astype(out_ref.dtype)


def attention(keep, queries, text_kv, img_kv, head_dim, q_tile):
    rows = queries.shape[0]
    text_total = text_kv.shape[0]
    img_total = img_kv.shape[0]
    heads = queries.shape[1] // head_dim
    return pl.pallas_call(
        functools.partial(attend_block, scale=head_dim ** (-0.5)),
        grid=(heads, rows // q_tile),
        in_specs=[
            pl.BlockSpec((1, text_total), lambda h, i: (0, 0)),
            pl.BlockSpec((q_tile, head_dim), lambda h, i: (i, h)),
            pl.BlockSpec((text_total, head_dim), lambda h, i: (0, h)),
            pl.BlockSpec((text_total, head_dim), lambda h, i: (0, h + heads)),
            pl.BlockSpec((img_total, head_dim), lambda h, i: (0, h)),
            pl.BlockSpec((img_total, head_dim), lambda h, i: (0, h + heads)),
        ],
        out_specs=pl.BlockSpec((q_tile, head_dim), lambda h, i: (i, h)),
        out_shape=jax.ShapeDtypeStruct(queries.shape, jnp.bfloat16),
    )(keep, queries, text_kv, text_kv, img_kv, img_kv)


def bit_of(value, step):
    return (value // step) % 2


def doubling_gather(block, axis, dim, order):
    count = lax.axis_size(axis)
    at = lax.axis_index(axis)
    stacked = block[None]
    for step in order:
        other = lax.ppermute(stacked, axis, [(i, i ^ step) for i in range(count)])
        upper = bit_of(at, step) == 1
        stacked = jnp.stack([jnp.where(upper, other, stacked), jnp.where(upper, stacked, other)])
        stacked = stacked.reshape((-1,) + block.shape)
    rank = len(order)
    source = [sum(((p >> k) & 1) * order[k] for k in range(rank)) for p in range(count)]
    place = [source.index(d) for d in range(count)]
    picked = jnp.stack([stacked[p] for p in place], 0)
    moved = jnp.moveaxis(picked, 0, dim)
    shape = list(block.shape)
    shape[dim] *= count
    return moved.reshape(shape)


def halving_scatter(block, axis, dim, order):
    count = lax.axis_size(axis)
    at = lax.axis_index(axis)
    rank = len(order)
    width = block.shape[dim] // count
    pieces = [lax.slice_in_dim(block, d * width, (d + 1) * width, axis=dim) for d in range(count)]
    slots = [sum(((d // order[k]) % 2) << (rank - 1 - k) for k in range(rank)) for d in range(count)]
    arranged = [None] * count
    for d in range(count):
        arranged[slots[d]] = pieces[d]
    block = jnp.concatenate(arranged, dim)
    for step in order:
        half = block.shape[dim] // 2
        low = lax.slice_in_dim(block, 0, half, axis=dim)
        high = lax.slice_in_dim(block, half, None, axis=dim)
        upper = bit_of(at, step) == 1
        kept = jnp.where(upper, high, low)
        sent = jnp.where(upper, low, high)
        block = kept + lax.ppermute(sent, axis, [(i, i ^ step) for i in range(count)])
    return block


def transpose_devices(block):
    side = lax.axis_size("tp")
    swap = [(a * side + b, b * side + a) for a in range(side) for b in range(side)]
    return lax.ppermute(block, ("seq", "tp"), swap)


def modulate(hidden, mod_rows):
    values = hidden.astype(jnp.float32)
    mod_f = mod_rows.astype(jnp.float32)
    row_mean = jnp.mean(values, -1, keepdims=True)
    row_var = jnp.mean((values - row_mean) ** 2, -1, keepdims=True)
    normed = (values - row_mean) * lax.rsqrt(row_var + EPS)
    return (normed * (1.0 + mod_f[1]) + mod_f[0]).astype(jnp.bfloat16)


def rms_gain(values, gain_row):
    return values * lax.rsqrt(jnp.mean(values * values, -1, keepdims=True) + EPS) * gain_row


def rope_angles(row_pos, col_pos, head_dim):
    lead = head_dim // 16
    span = 7 * head_dim // 32
    freq = THETA ** (-jnp.arange(span, dtype=jnp.float32) / span)
    zero_part = jnp.zeros((row_pos.shape[0], lead), jnp.float32)
    return jnp.concatenate(
        [zero_part, row_pos[:, None] * freq[None], col_pos[:, None] * freq[None]], 1
    )


def apply_rope(values, angles):
    count, heads_n, head_dim = values.shape
    pairs = values.reshape(count, heads_n, head_dim // 2, 2)
    first = pairs[..., 0]
    second = pairs[..., 1]
    cosine = jnp.cos(angles)[:, None, :]
    sine = jnp.sin(angles)[:, None, :]
    turned = jnp.stack([first * cosine - second * sine, first * sine + second * cosine], -1)
    return turned.reshape(values.shape)


def split_heads(mixed, gain_q, gain_k, angles):
    head_dim = gain_q.shape[0]
    shaped = mixed.reshape(mixed.shape[0], 3, -1, head_dim)
    query = rms_gain(shaped[:, 0], gain_q)
    keyed = rms_gain(shaped[:, 1], gain_k)
    if angles is not None:
        query = apply_rope(query, angles)
        keyed = apply_rope(keyed, angles)
    return (
        query.astype(jnp.bfloat16),
        keyed.astype(jnp.bfloat16),
        shaped[:, 2].astype(jnp.bfloat16),
    )


def noise_level(tval):
    factor = math.exp(SHIFT_MU)
    return factor * tval / (factor * tval + 1.0 - tval)


def add_rows(normed, piece):
    flat_piece = piece.reshape(piece.shape[0], piece.shape[1] * piece.shape[2])
    return jnp.dot(normed, flat_piece, preferred_element_type=jnp.float32)


def per_device(
    img_hidden,
    txt_hidden,
    img_mod,
    txt_mod,
    img_qkv,
    txt_qkv,
    qk_gains,
    img_out_w,
    txt_out_w,
    final_mod,
    final_w,
    conv_w,
    latent,
    text_len,
    step_index,
):
    seq_count = lax.axis_size("seq")
    seq_at = lax.axis_index("seq")
    tp_at = lax.axis_index("tp")
    img_rows = img_hidden.shape[0]
    txt_rows = txt_hidden.shape[0]
    local_width = img_hidden.shape[1]
    img_full, txt_full = (
        lax.all_gather(img_hidden, "tp", axis=1, tiled=True),
        lax.all_gather(txt_hidden, "tp", axis=1, tiled=True),
    )
    full_width = img_full.shape[1]
    img_norm = modulate(img_full, img_mod)
    txt_norm = modulate(txt_full, txt_mod)
    img_weights = lax.all_gather(img_qkv, "seq", axis=0, tiled=True)
    img_weights, img_out_w = lax.optimization_barrier((img_weights, img_out_w))
    img_out_full = lax.all_gather(img_out_w, "seq", axis=1, tiled=True)
    txt_norm_rows = lax.all_to_all(txt_norm, "seq", 1, 0, tiled=True)
    txt_mixed = halving_scatter(add_rows(txt_norm_rows, txt_qkv), "seq", 0, (4, 1, 2))
    head_dim = qk_gains.shape[1]
    txt_query, txt_key, txt_value = split_heads(txt_mixed, qk_gains[2], qk_gains[3], None)
    heads_local = txt_query.shape[1]
    kv_width = heads_local * head_dim
    text_kv = lax.all_gather(
        jnp.concatenate(
            [txt_key.reshape(txt_rows, kv_width), txt_value.reshape(txt_rows, kv_width)], 1
        ),
        "seq",
        axis=0,
        tiled=True,
    )
    text_kv, txt_query, img_norm = lax.optimization_barrier((text_kv, txt_query, img_norm))
    img_mixed = add_rows(img_norm, img_weights)
    head_dim = qk_gains.shape[1]
    grid_side = latent.shape[0] * seq_count
    token_ids = seq_at * img_rows + jnp.arange(img_rows, dtype=jnp.int32)
    row_pos = (token_ids // grid_side).astype(jnp.float32)
    col_pos = (token_ids % grid_side).astype(jnp.float32)
    angles = rope_angles(row_pos, col_pos, head_dim)
    img_query, img_key, img_value = split_heads(img_mixed, qk_gains[0], qk_gains[1], angles)
    local_len = txt_rows + img_rows
    heads_local = img_query.shape[1]
    kv_width = heads_local * head_dim
    queries = jnp.concatenate([txt_query, img_query], 0).reshape(local_len, kv_width)
    img_kv = lax.all_gather(
        jnp.concatenate(
            [img_key.reshape(img_rows, kv_width), img_value.reshape(img_rows, kv_width)], 1
        ),
        "seq",
        axis=0,
        tiled=True,
    )
    limit = text_len[0]
    keep = (jnp.arange(text_kv.shape[0], dtype=jnp.int32) < limit).astype(jnp.float32)[None, :]
    attn = attention(keep, queries, text_kv, img_kv, head_dim, local_len // 3)
    txt_attn = attn[:txt_rows]
    img_attn = attn[txt_rows:]
    img_term = jnp.dot(
        img_attn,
        img_out_full,
        preferred_element_type=jnp.float32,
    )
    txt_term = jnp.dot(
        doubling_gather(txt_attn, "seq", 0, (2, 1, 4)),
        txt_out_w,
        preferred_element_type=jnp.float32,
    )
    txt_out = transpose_devices(
        halving_scatter(txt_term.astype(jnp.bfloat16).astype(jnp.float32), "tp", 0, (1, 2, 4))
    )
    img_out = lax.psum_scatter(
        img_term.astype(jnp.bfloat16), "tp", scatter_dimension=1, tiled=True
    ).astype(jnp.float32)
    img_gate = lax.dynamic_slice_in_dim(
        img_mod.astype(jnp.float32)[2], tp_at * local_width, local_width
    )
    txt_gate = lax.dynamic_slice_in_dim(
        txt_mod.astype(jnp.float32)[2], tp_at * local_width, local_width
    )
    img_next = (img_hidden.astype(jnp.float32) + img_gate * img_out).astype(jnp.bfloat16)
    text_valid = seq_at * txt_rows + jnp.arange(txt_rows, dtype=jnp.int32) < limit
    txt_base = txt_hidden.astype(jnp.float32)
    txt_next = jnp.where(text_valid[:, None], txt_base + txt_gate * txt_out, txt_base).astype(
        jnp.bfloat16
    )
    shift_row = lax.dynamic_slice_in_dim(final_mod[0], tp_at * local_width, local_width)
    scale_row = lax.dynamic_slice_in_dim(final_mod[1], tp_at * local_width, local_width)
    final_shift = shift_row.astype(jnp.float32)
    final_scale = scale_row.astype(jnp.float32)
    weight_final = final_w.astype(jnp.float32)
    values = img_next.astype(jnp.float32)
    channels = final_w.shape[1]
    final_gain = 1.0 + final_scale
    high = lax.Precision.HIGHEST
    lifted = jnp.dot(values * final_gain, weight_final, precision=high)
    consts = jnp.stack(
        [jnp.dot(final_gain, weight_final, precision=high), jnp.dot(final_shift, weight_final, precision=high)]
    )
    packed = jnp.concatenate(
        [
            jnp.concatenate([lifted, jnp.sum(values, -1)[:, None], jnp.sum(values * values, -1)[:, None]], 1),
            jnp.pad(consts, ((0, 0), (0, 2))),
        ],
        0,
    )
    packed = tree_sum(packed, "tp")
    lifted = packed[:img_rows, :channels]
    row_mean = packed[:img_rows, channels] / full_width
    row_var = packed[:img_rows, channels + 1] / full_width - row_mean * row_mean
    row_scale = lax.rsqrt(row_var + EPS)[:, None]
    patch = row_scale * (lifted - row_mean[:, None] * packed[img_rows, :channels]) + packed[
        img_rows + 1, :channels
    ]
    band_rows = latent.shape[0]
    patch_band = patch.astype(jnp.bfloat16).reshape(band_rows, grid_side * channels)
    rimmed = extended(patch_band, (("seq", 0),), 1)
    col_width = latent.shape[1] // channels
    framed = jnp.pad(rimmed.reshape(band_rows + 2, grid_side, channels), ((0, 0), (1, 1), (0, 0)))
    window = lax.dynamic_slice_in_dim(framed, tp_at * col_width, col_width + 2, 1)
    velocity = jnp.zeros((band_rows, col_width, channels), jnp.float32)
    for row_shift in range(3):
        for col_shift in range(3):
            velocity = velocity + jnp.einsum(
                "rci,io->rco",
                window[row_shift : row_shift + band_rows, col_shift : col_shift + col_width],
                conv_w[row_shift, col_shift],
                preferred_element_type=jnp.float32,
            )
    velocity_flat = velocity.reshape(band_rows, col_width * channels)
    step_f = step_index[0].astype(jnp.float32)
    t_now = 1.0 - step_f / STEPS
    t_after = 1.0 - (step_f + 1.0) / STEPS
    delta = noise_level(t_after) - noise_level(t_now)
    latent_next = latent + delta * velocity_flat
    denoised = latent - noise_level(t_now) * velocity_flat
    return (img_next, txt_next, velocity_flat, latent_next, denoised)


def solution(mesh):
    placed = (
        P(("req", "seq"), "tp"),
        P(("req", "seq"), "tp"),
        P("req", None),
        P("req", None),
        P("seq", None, "tp"),
        P("seq", None, "tp"),
        P(),
        P("tp", "seq"),
        P("tp", "seq"),
        P("req", None),
        P("tp", None),
        P(),
        P(("req", "seq"), "tp"),
        P("req"),
        P("req"),
    )
    return jax.shard_map(
        per_device,
        mesh=mesh,
        in_specs=placed,
        out_specs=(
            P(("req", "seq"), "tp"),
            P(("req", "seq"), "tp"),
            P(("req", "seq"), "tp"),
            P(("req", "seq"), "tp"),
            P(("req", "seq"), "tp"),
        ),
        check_vma=False,
    )
```

```python
import functools
import math

import jax
import jax.numpy as jnp
from jax import lax
from jax.experimental import pallas as pl
from jax.sharding import PartitionSpec as P

STEPS = 28


EPS = 1e-06
SHIFT_MU = 1.15
THETA = 10000.0


def extended(block, sides, width):
    for axis, dim in sides:
        count = lax.axis_size(axis)
        forward = [(i, i + 1) for i in range(count - 1)]
        backward = [(target, source) for source, target in forward]
        low = lax.ppermute(
            lax.slice_in_dim(block, block.shape[dim] - width, None, axis=dim), axis, forward
        )
        high = lax.ppermute(lax.slice_in_dim(block, 0, width, axis=dim), axis, backward)
        block = jnp.concatenate([low, block, high], axis=dim)
    return block


def tree_sum(block, axis):
    count = lax.axis_size(axis)
    step = 1
    while step < count:
        block = block + lax.ppermute(block, axis, [(i, i ^ step) for i in range(count)])
        step *= 2
    return block


def halving_sum(block, axis, dim):
    count = lax.axis_size(axis)
    at = lax.axis_index(axis)
    step = count // 2
    while step >= 1:
        half = block.shape[dim] // 2
        low = lax.slice_in_dim(block, 0, half, axis=dim)
        high = lax.slice_in_dim(block, half, None, axis=dim)
        upper = (at // step) % 2 == 1
        kept = jnp.where(upper, high, low)
        sent = jnp.where(upper, low, high)
        block = kept + lax.ppermute(sent, axis, [(i, i ^ step) for i in range(count)])
        step //= 2
    return block


def attend_block(keep_ref, query_ref, tkey_ref, tvalue_ref, ikey_ref, ivalue_ref, out_ref, *, scale):
    query = query_ref[...]
    contract = (((1,), (1,)), ((), ()))
    text_scores = (
        lax.dot_general(query, tkey_ref[...], contract, preferred_element_type=jnp.float32) * scale
    )
    text_scores = jnp.where(keep_ref[...] > 0.5, text_scores, -1e30)
    img_scores = (
        lax.dot_general(query, ikey_ref[...], contract, preferred_element_type=jnp.float32) * scale
    )
    peak = jnp.maximum(
        jnp.max(text_scores, -1, keepdims=True), jnp.max(img_scores, -1, keepdims=True)
    )
    text_weights = jnp.exp(text_scores - peak)
    img_weights = jnp.exp(img_scores - peak)
    summed = jnp.sum(text_weights, -1, keepdims=True) + jnp.sum(img_weights, -1, keepdims=True)
    mixed_v = jnp.dot(
        text_weights.astype(jnp.bfloat16), tvalue_ref[...], preferred_element_type=jnp.float32
    ) + jnp.dot(img_weights.astype(jnp.bfloat16), ivalue_ref[...], preferred_element_type=jnp.float32)
    out_ref[...] = (mixed_v / summed).astype(out_ref.dtype)


def attention(keep, queries, text_kv, img_kv, head_dim, q_tile):
    rows = queries.shape[0]
    text_total = text_kv.shape[0]
    img_total = img_kv.shape[0]
    heads = queries.shape[1] // head_dim
    return pl.pallas_call(
        functools.partial(attend_block, scale=head_dim ** (-0.5)),
        grid=(heads, rows // q_tile),
        in_specs=[
            pl.BlockSpec((1, text_total), lambda h, i: (0, 0)),
            pl.BlockSpec((q_tile, head_dim), lambda h, i: (i, h)),
            pl.BlockSpec((text_total, head_dim), lambda h, i: (0, h)),
            pl.BlockSpec((text_total, head_dim), lambda h, i: (0, h + heads)),
            pl.BlockSpec((img_total, head_dim), lambda h, i: (0, h)),
            pl.BlockSpec((img_total, head_dim), lambda h, i: (0, h + heads)),
        ],
        out_specs=pl.BlockSpec((q_tile, head_dim), lambda h, i: (i, h)),
        out_shape=jax.ShapeDtypeStruct(queries.shape, jnp.bfloat16),
    )(keep, queries, text_kv, text_kv, img_kv, img_kv)


def bit_of(value, step):
    return (value // step) % 2


def doubling_gather(block, axis, dim, order):
    count = lax.axis_size(axis)
    at = lax.axis_index(axis)
    stacked = block[None]
    for step in order:
        other = lax.ppermute(stacked, axis, [(i, i ^ step) for i in range(count)])
        upper = bit_of(at, step) == 1
        stacked = jnp.stack([jnp.where(upper, other, stacked), jnp.where(upper, stacked, other)])
        stacked = stacked.reshape((-1,) + block.shape)
    rank = len(order)
    source = [sum(((p >> k) & 1) * order[k] for k in range(rank)) for p in range(count)]
    place = [source.index(d) for d in range(count)]
    picked = jnp.stack([stacked[p] for p in place], 0)
    moved = jnp.moveaxis(picked, 0, dim)
    shape = list(block.shape)
    shape[dim] *= count
    return moved.reshape(shape)


def halving_scatter(block, axis, dim, order):
    count = lax.axis_size(axis)
    at = lax.axis_index(axis)
    rank = len(order)
    width = block.shape[dim] // count
    pieces = [lax.slice_in_dim(block, d * width, (d + 1) * width, axis=dim) for d in range(count)]
    slots = [sum(((d // order[k]) % 2) << (rank - 1 - k) for k in range(rank)) for d in range(count)]
    arranged = [None] * count
    for d in range(count):
        arranged[slots[d]] = pieces[d]
    block = jnp.concatenate(arranged, dim)
    for step in order:
        half = block.shape[dim] // 2
        low = lax.slice_in_dim(block, 0, half, axis=dim)
        high = lax.slice_in_dim(block, half, None, axis=dim)
        upper = bit_of(at, step) == 1
        kept = jnp.where(upper, high, low)
        sent = jnp.where(upper, low, high)
        block = kept + lax.ppermute(sent, axis, [(i, i ^ step) for i in range(count)])
    return block


def transpose_devices(block):
    side = lax.axis_size("tp")
    swap = [(a * side + b, b * side + a) for a in range(side) for b in range(side)]
    return lax.ppermute(block, ("seq", "tp"), swap)


def direct_sum(block, axis):
    count = lax.axis_size(axis)
    at = lax.axis_index(axis)
    received = [block] + [
        lax.ppermute(block, axis, [(i, (i + shift) % count) for i in range(count)])
        for shift in range(1, count)
    ]
    stacked = jnp.stack(received)
    total = None
    for source in range(count):
        piece = lax.dynamic_index_in_dim(stacked, (at - source) % count, 0, keepdims=False)
        total = piece if total is None else total + piece
    return total


def modulate(hidden, mod_rows):
    values = hidden.astype(jnp.float32)
    mod_f = mod_rows.astype(jnp.float32)
    row_mean = jnp.mean(values, -1, keepdims=True)
    row_var = jnp.mean((values - row_mean) ** 2, -1, keepdims=True)
    normed = (values - row_mean) * lax.rsqrt(row_var + EPS)
    return (normed * (1.0 + mod_f[1]) + mod_f[0]).astype(jnp.bfloat16)


def rms_gain(values, gain_row):
    return values * lax.rsqrt(jnp.mean(values * values, -1, keepdims=True) + EPS) * gain_row


def rope_angles(row_pos, col_pos, head_dim):
    lead = head_dim // 16
    span = 7 * head_dim // 32
    freq = THETA ** (-jnp.arange(span, dtype=jnp.float32) / span)
    zero_part = jnp.zeros((row_pos.shape[0], lead), jnp.float32)
    return jnp.concatenate(
        [zero_part, row_pos[:, None] * freq[None], col_pos[:, None] * freq[None]], 1
    )


def apply_rope(values, angles):
    count, heads_n, head_dim = values.shape
    pairs = values.reshape(count, heads_n, head_dim // 2, 2)
    first = pairs[..., 0]
    second = pairs[..., 1]
    cosine = jnp.cos(angles)[:, None, :]
    sine = jnp.sin(angles)[:, None, :]
    turned = jnp.stack([first * cosine - second * sine, first * sine + second * cosine], -1)
    return turned.reshape(values.shape)


def split_heads(mixed, gain_q, gain_k, angles):
    head_dim = gain_q.shape[0]
    shaped = mixed.reshape(mixed.shape[0], 3, -1, head_dim)
    query = rms_gain(shaped[:, 0], gain_q)
    keyed = rms_gain(shaped[:, 1], gain_k)
    if angles is not None:
        query = apply_rope(query, angles)
        keyed = apply_rope(keyed, angles)
    return (
        query.astype(jnp.bfloat16),
        keyed.astype(jnp.bfloat16),
        shaped[:, 2].astype(jnp.bfloat16),
    )


def noise_level(tval):
    factor = math.exp(SHIFT_MU)
    return factor * tval / (factor * tval + 1.0 - tval)


def add_rows(normed, piece):
    flat_piece = piece.reshape(piece.shape[0], piece.shape[1] * piece.shape[2])
    return jnp.dot(normed, flat_piece, preferred_element_type=jnp.float32)


def per_device(
    img_hidden,
    txt_hidden,
    img_mod,
    txt_mod,
    img_qkv,
    txt_qkv,
    qk_gains,
    img_out_w,
    txt_out_w,
    final_mod,
    final_w,
    conv_w,
    latent,
    text_len,
    step_index,
):
    seq_count = lax.axis_size("seq")
    seq_at = lax.axis_index("seq")
    tp_at = lax.axis_index("tp")
    img_rows = img_hidden.shape[0]
    txt_rows = txt_hidden.shape[0]
    local_width = img_hidden.shape[1]
    img_full, txt_full = (
        lax.all_gather(img_hidden, "tp", axis=1, tiled=True),
        lax.all_gather(txt_hidden, "tp", axis=1, tiled=True),
    )
    full_width = img_full.shape[1]
    img_norm = modulate(img_full, img_mod)
    txt_norm = modulate(txt_full, txt_mod)
    img_weights = lax.all_gather(img_qkv, "seq", axis=0, tiled=True)
    img_weights, img_out_w = lax.optimization_barrier((img_weights, img_out_w))
    img_out_full = lax.all_gather(img_out_w, "seq", axis=1, tiled=True)
    img_mixed = add_rows(img_norm, img_weights)
    txt_norm, img_norm = lax.optimization_barrier((txt_norm, img_norm))
    txt_norm_rows = lax.all_to_all(txt_norm, "seq", 1, 0, tiled=True)
    txt_mixed = lax.psum_scatter(
        add_rows(txt_norm_rows, txt_qkv), "seq", scatter_dimension=0, tiled=True
    )
    head_dim = qk_gains.shape[1]
    grid_side = latent.shape[0] * seq_count
    token_ids = seq_at * img_rows + jnp.arange(img_rows, dtype=jnp.int32)
    row_pos = (token_ids // grid_side).astype(jnp.float32)
    col_pos = (token_ids % grid_side).astype(jnp.float32)
    angles = rope_angles(row_pos, col_pos, head_dim)
    img_query, img_key, img_value = split_heads(img_mixed, qk_gains[0], qk_gains[1], angles)
    txt_query, txt_key, txt_value = split_heads(txt_mixed, qk_gains[2], qk_gains[3], None)
    local_len = txt_rows + img_rows
    heads_local = img_query.shape[1]
    kv_width = heads_local * head_dim
    queries = jnp.concatenate([txt_query, img_query], 0).reshape(local_len, kv_width)
    img_kv = lax.all_gather(
        jnp.concatenate(
            [img_key.reshape(img_rows, kv_width), img_value.reshape(img_rows, kv_width)], 1
        ),
        "seq",
        axis=0,
        tiled=True,
    )
    text_kv = lax.all_gather(
        jnp.concatenate(
            [txt_key.reshape(txt_rows, kv_width), txt_value.reshape(txt_rows, kv_width)], 1
        ),
        "seq",
        axis=0,
        tiled=True,
    )
    limit = text_len[0]
    keep = (jnp.arange(text_kv.shape[0], dtype=jnp.int32) < limit).astype(jnp.float32)[None, :]
    attn = attention(keep, queries, text_kv, img_kv, head_dim, local_len // 3)
    txt_attn = attn[:txt_rows]
    img_attn = attn[txt_rows:]
    img_term = jnp.dot(
        img_attn,
        img_out_full,
        preferred_element_type=jnp.float32,
    )
    txt_term = jnp.dot(
        doubling_gather(txt_attn, "seq", 0, (2, 1, 4)),
        txt_out_w,
        preferred_element_type=jnp.float32,
    )
    txt_out = transpose_devices(
        halving_scatter(txt_term.astype(jnp.bfloat16).astype(jnp.float32), "tp", 0, (1, 2, 4))
    )
    img_out = lax.psum_scatter(
        img_term.astype(jnp.bfloat16), "tp", scatter_dimension=1, tiled=True
    ).astype(jnp.float32)
    img_gate = lax.dynamic_slice_in_dim(
        img_mod.astype(jnp.float32)[2], tp_at * local_width, local_width
    )
    txt_gate = lax.dynamic_slice_in_dim(
        txt_mod.astype(jnp.float32)[2], tp_at * local_width, local_width
    )
    img_next = (img_hidden.astype(jnp.float32) + img_gate * img_out).astype(jnp.bfloat16)
    text_valid = seq_at * txt_rows + jnp.arange(txt_rows, dtype=jnp.int32) < limit
    txt_base = txt_hidden.astype(jnp.float32)
    txt_next = jnp.where(text_valid[:, None], txt_base + txt_gate * txt_out, txt_base).astype(
        jnp.bfloat16
    )
    shift_row = lax.dynamic_slice_in_dim(final_mod[0], tp_at * local_width, local_width)
    scale_row = lax.dynamic_slice_in_dim(final_mod[1], tp_at * local_width, local_width)
    final_shift = shift_row.astype(jnp.float32)
    final_scale = scale_row.astype(jnp.float32)
    weight_final = final_w.astype(jnp.float32)
    values = img_next.astype(jnp.float32)
    channels = final_w.shape[1]
    final_gain = 1.0 + final_scale
    high = lax.Precision.HIGHEST
    lifted = jnp.dot(values * final_gain, weight_final, precision=high)
    consts = jnp.stack(
        [jnp.dot(final_gain, weight_final, precision=high), jnp.dot(final_shift, weight_final, precision=high)]
    )
    packed = jnp.concatenate(
        [
            jnp.concatenate([lifted, jnp.sum(values, -1)[:, None], jnp.sum(values * values, -1)[:, None]], 1),
            jnp.pad(consts, ((0, 0), (0, 2))),
        ],
        0,
    )
    packed = direct_sum(packed, "tp")
    lifted = packed[:img_rows, :channels]
    row_mean = packed[:img_rows, channels] / full_width
    row_var = packed[:img_rows, channels + 1] / full_width - row_mean * row_mean
    row_scale = lax.rsqrt(row_var + EPS)[:, None]
    patch = row_scale * (lifted - row_mean[:, None] * packed[img_rows, :channels]) + packed[
        img_rows + 1, :channels
    ]
    band_rows = latent.shape[0]
    patch_band = patch.astype(jnp.bfloat16).reshape(band_rows, grid_side * channels)
    rimmed = extended(patch_band, (("seq", 0),), 1)
    col_width = latent.shape[1] // channels
    framed = jnp.pad(rimmed.reshape(band_rows + 2, grid_side, channels), ((0, 0), (1, 1), (0, 0)))
    window = lax.dynamic_slice_in_dim(framed, tp_at * col_width, col_width + 2, 1)
    velocity = jnp.zeros((band_rows, col_width, channels), jnp.float32)
    for row_shift in range(3):
        for col_shift in range(3):
            velocity = velocity + jnp.einsum(
                "rci,io->rco",
                window[row_shift : row_shift + band_rows, col_shift : col_shift + col_width],
                conv_w[row_shift, col_shift],
                preferred_element_type=jnp.float32,
            )
    velocity_flat = velocity.reshape(band_rows, col_width * channels)
    step_f = step_index[0].astype(jnp.float32)
    t_now = 1.0 - step_f / STEPS
    t_after = 1.0 - (step_f + 1.0) / STEPS
    delta = noise_level(t_after) - noise_level(t_now)
    latent_next = latent + delta * velocity_flat
    denoised = latent - noise_level(t_now) * velocity_flat
    return (img_next, txt_next, velocity_flat, latent_next, denoised)


def solution(mesh):
    placed = (
        P(("req", "seq"), "tp"),
        P(("req", "seq"), "tp"),
        P("req", None),
        P("req", None),
        P("seq", None, "tp"),
        P("seq", None, "tp"),
        P(),
        P("tp", "seq"),
        P("tp", "seq"),
        P("req", None),
        P("tp", None),
        P(),
        P(("req", "seq"), "tp"),
        P("req"),
        P("req"),
    )
    return jax.shard_map(
        per_device,
        mesh=mesh,
        in_specs=placed,
        out_specs=(
            P(("req", "seq"), "tp"),
            P(("req", "seq"), "tp"),
            P(("req", "seq"), "tp"),
            P(("req", "seq"), "tp"),
            P(("req", "seq"), "tp"),
        ),
        check_vma=False,
    )
```

```python
import functools
import math

import jax
import jax.numpy as jnp
from jax import lax
from jax.experimental import pallas as pl
from jax.sharding import PartitionSpec as P

STEPS = 28


EPS = 1e-06
SHIFT_MU = 1.15
THETA = 10000.0


def extended(block, sides, width):
    for axis, dim in sides:
        count = lax.axis_size(axis)
        forward = [(i, i + 1) for i in range(count - 1)]
        backward = [(target, source) for source, target in forward]
        low = lax.ppermute(
            lax.slice_in_dim(block, block.shape[dim] - width, None, axis=dim), axis, forward
        )
        high = lax.ppermute(lax.slice_in_dim(block, 0, width, axis=dim), axis, backward)
        block = jnp.concatenate([low, block, high], axis=dim)
    return block


def tree_sum(block, axis):
    count = lax.axis_size(axis)
    step = 1
    while step < count:
        block = block + lax.ppermute(block, axis, [(i, i ^ step) for i in range(count)])
        step *= 2
    return block


def halving_sum(block, axis, dim):
    count = lax.axis_size(axis)
    at = lax.axis_index(axis)
    step = count // 2
    while step >= 1:
        half = block.shape[dim] // 2
        low = lax.slice_in_dim(block, 0, half, axis=dim)
        high = lax.slice_in_dim(block, half, None, axis=dim)
        upper = (at // step) % 2 == 1
        kept = jnp.where(upper, high, low)
        sent = jnp.where(upper, low, high)
        block = kept + lax.ppermute(sent, axis, [(i, i ^ step) for i in range(count)])
        step //= 2
    return block


def attend_block(keep_ref, query_ref, tkey_ref, tvalue_ref, ikey_ref, ivalue_ref, out_ref, *, scale):
    query = query_ref[...]
    contract = (((1,), (1,)), ((), ()))
    text_scores = (
        lax.dot_general(query, tkey_ref[...], contract, preferred_element_type=jnp.float32) * scale
    )
    text_scores = jnp.where(keep_ref[...] > 0.5, text_scores, -1e30)
    img_scores = (
        lax.dot_general(query, ikey_ref[...], contract, preferred_element_type=jnp.float32) * scale
    )
    peak = jnp.maximum(
        jnp.max(text_scores, -1, keepdims=True), jnp.max(img_scores, -1, keepdims=True)
    )
    text_weights = jnp.exp(text_scores - peak)
    img_weights = jnp.exp(img_scores - peak)
    summed = jnp.sum(text_weights, -1, keepdims=True) + jnp.sum(img_weights, -1, keepdims=True)
    mixed_v = jnp.dot(
        text_weights.astype(jnp.bfloat16), tvalue_ref[...], preferred_element_type=jnp.float32
    ) + jnp.dot(img_weights.astype(jnp.bfloat16), ivalue_ref[...], preferred_element_type=jnp.float32)
    out_ref[...] = (mixed_v / summed).astype(out_ref.dtype)


def attention(keep, queries, text_kv, img_kv, head_dim, q_tile):
    rows = queries.shape[0]
    text_total = text_kv.shape[0]
    img_total = img_kv.shape[0]
    heads = queries.shape[1] // head_dim
    return pl.pallas_call(
        functools.partial(attend_block, scale=head_dim ** (-0.5)),
        grid=(heads, rows // q_tile),
        in_specs=[
            pl.BlockSpec((1, text_total), lambda h, i: (0, 0)),
            pl.BlockSpec((q_tile, head_dim), lambda h, i: (i, h)),
            pl.BlockSpec((text_total, head_dim), lambda h, i: (0, h)),
            pl.BlockSpec((text_total, head_dim), lambda h, i: (0, h + heads)),
            pl.BlockSpec((img_total, head_dim), lambda h, i: (0, h)),
            pl.BlockSpec((img_total, head_dim), lambda h, i: (0, h + heads)),
        ],
        out_specs=pl.BlockSpec((q_tile, head_dim), lambda h, i: (i, h)),
        out_shape=jax.ShapeDtypeStruct(queries.shape, jnp.bfloat16),
    )(keep, queries, text_kv, text_kv, img_kv, img_kv)


def bit_of(value, step):
    return (value // step) % 2


def doubling_gather(block, axis, dim, order):
    count = lax.axis_size(axis)
    at = lax.axis_index(axis)
    stacked = block[None]
    for step in order:
        other = lax.ppermute(stacked, axis, [(i, i ^ step) for i in range(count)])
        upper = bit_of(at, step) == 1
        stacked = jnp.stack([jnp.where(upper, other, stacked), jnp.where(upper, stacked, other)])
        stacked = stacked.reshape((-1,) + block.shape)
    rank = len(order)
    source = [sum(((p >> k) & 1) * order[k] for k in range(rank)) for p in range(count)]
    place = [source.index(d) for d in range(count)]
    picked = jnp.stack([stacked[p] for p in place], 0)
    moved = jnp.moveaxis(picked, 0, dim)
    shape = list(block.shape)
    shape[dim] *= count
    return moved.reshape(shape)


def halving_scatter(block, axis, dim, order):
    count = lax.axis_size(axis)
    at = lax.axis_index(axis)
    rank = len(order)
    width = block.shape[dim] // count
    pieces = [lax.slice_in_dim(block, d * width, (d + 1) * width, axis=dim) for d in range(count)]
    slots = [sum(((d // order[k]) % 2) << (rank - 1 - k) for k in range(rank)) for d in range(count)]
    arranged = [None] * count
    for d in range(count):
        arranged[slots[d]] = pieces[d]
    block = jnp.concatenate(arranged, dim)
    for step in order:
        half = block.shape[dim] // 2
        low = lax.slice_in_dim(block, 0, half, axis=dim)
        high = lax.slice_in_dim(block, half, None, axis=dim)
        upper = bit_of(at, step) == 1
        kept = jnp.where(upper, high, low)
        sent = jnp.where(upper, low, high)
        block = kept + lax.ppermute(sent, axis, [(i, i ^ step) for i in range(count)])
    return block


def transpose_devices(block):
    side = lax.axis_size("tp")
    swap = [(a * side + b, b * side + a) for a in range(side) for b in range(side)]
    return lax.ppermute(block, ("seq", "tp"), swap)


def modulate(hidden, mod_rows):
    values = hidden.astype(jnp.float32)
    mod_f = mod_rows.astype(jnp.float32)
    row_mean = jnp.mean(values, -1, keepdims=True)
    row_var = jnp.mean((values - row_mean) ** 2, -1, keepdims=True)
    normed = (values - row_mean) * lax.rsqrt(row_var + EPS)
    return (normed * (1.0 + mod_f[1]) + mod_f[0]).astype(jnp.bfloat16)


def rms_gain(values, gain_row):
    return values * lax.rsqrt(jnp.mean(values * values, -1, keepdims=True) + EPS) * gain_row


def rope_angles(row_pos, col_pos, head_dim):
    lead = head_dim // 16
    span = 7 * head_dim // 32
    freq = THETA ** (-jnp.arange(span, dtype=jnp.float32) / span)
    zero_part = jnp.zeros((row_pos.shape[0], lead), jnp.float32)
    return jnp.concatenate(
        [zero_part, row_pos[:, None] * freq[None], col_pos[:, None] * freq[None]], 1
    )


def apply_rope(values, angles):
    count, heads_n, head_dim = values.shape
    pairs = values.reshape(count, heads_n, head_dim // 2, 2)
    first = pairs[..., 0]
    second = pairs[..., 1]
    cosine = jnp.cos(angles)[:, None, :]
    sine = jnp.sin(angles)[:, None, :]
    turned = jnp.stack([first * cosine - second * sine, first * sine + second * cosine], -1)
    return turned.reshape(values.shape)


def split_heads(mixed, gain_q, gain_k, angles):
    head_dim = gain_q.shape[0]
    shaped = mixed.reshape(mixed.shape[0], 3, -1, head_dim)
    query = rms_gain(shaped[:, 0], gain_q)
    keyed = rms_gain(shaped[:, 1], gain_k)
    if angles is not None:
        query = apply_rope(query, angles)
        keyed = apply_rope(keyed, angles)
    return (
        query.astype(jnp.bfloat16),
        keyed.astype(jnp.bfloat16),
        shaped[:, 2].astype(jnp.bfloat16),
    )


def noise_level(tval):
    factor = math.exp(SHIFT_MU)
    return factor * tval / (factor * tval + 1.0 - tval)


def add_rows(normed, piece):
    flat_piece = piece.reshape(piece.shape[0], piece.shape[1] * piece.shape[2])
    return jnp.dot(normed, flat_piece, preferred_element_type=jnp.float32)


def per_device(
    img_hidden,
    txt_hidden,
    img_mod,
    txt_mod,
    img_qkv,
    txt_qkv,
    qk_gains,
    img_out_w,
    txt_out_w,
    final_mod,
    final_w,
    conv_w,
    latent,
    text_len,
    step_index,
):
    seq_count = lax.axis_size("seq")
    seq_at = lax.axis_index("seq")
    tp_at = lax.axis_index("tp")
    img_rows = img_hidden.shape[0]
    txt_rows = txt_hidden.shape[0]
    local_width = img_hidden.shape[1]
    img_full, txt_full = (
        lax.all_gather(img_hidden, "tp", axis=1, tiled=True),
        lax.all_gather(txt_hidden, "tp", axis=1, tiled=True),
    )
    full_width = img_full.shape[1]
    img_norm = modulate(img_full, img_mod)
    txt_norm = modulate(txt_full, txt_mod)
    img_weights = lax.all_gather(img_qkv, "seq", axis=0, tiled=True)
    img_weights, img_out_w = lax.optimization_barrier((img_weights, img_out_w))
    img_out_full = lax.all_gather(img_out_w, "seq", axis=1, tiled=True)
    img_mixed = add_rows(img_norm, img_weights)
    txt_norm, img_norm = lax.optimization_barrier((txt_norm, img_norm))
    txt_norm_rows = lax.all_to_all(txt_norm, "seq", 1, 0, tiled=True)
    txt_mixed = lax.psum_scatter(
        add_rows(txt_norm_rows, txt_qkv).astype(jnp.bfloat16), "seq", scatter_dimension=0, tiled=True
    ).astype(jnp.float32)
    head_dim = qk_gains.shape[1]
    grid_side = latent.shape[0] * seq_count
    token_ids = seq_at * img_rows + jnp.arange(img_rows, dtype=jnp.int32)
    row_pos = (token_ids // grid_side).astype(jnp.float32)
    col_pos = (token_ids % grid_side).astype(jnp.float32)
    angles = rope_angles(row_pos, col_pos, head_dim)
    img_query, img_key, img_value = split_heads(img_mixed, qk_gains[0], qk_gains[1], angles)
    txt_query, txt_key, txt_value = split_heads(txt_mixed, qk_gains[2], qk_gains[3], None)
    local_len = txt_rows + img_rows
    heads_local = img_query.shape[1]
    kv_width = heads_local * head_dim
    queries = jnp.concatenate([txt_query, img_query], 0).reshape(local_len, kv_width)
    img_kv = lax.all_gather(
        jnp.concatenate(
            [img_key.reshape(img_rows, kv_width), img_value.reshape(img_rows, kv_width)], 1
        ),
        "seq",
        axis=0,
        tiled=True,
    )
    text_kv = lax.all_gather(
        jnp.concatenate(
            [txt_key.reshape(txt_rows, kv_width), txt_value.reshape(txt_rows, kv_width)], 1
        ),
        "seq",
        axis=0,
        tiled=True,
    )
    limit = text_len[0]
    keep = (jnp.arange(text_kv.shape[0], dtype=jnp.int32) < limit).astype(jnp.float32)[None, :]
    attn = attention(keep, queries, text_kv, img_kv, head_dim, local_len // 3)
    txt_attn = attn[:txt_rows]
    img_attn = attn[txt_rows:]
    img_term = jnp.dot(
        img_attn,
        img_out_full,
        preferred_element_type=jnp.float32,
    )
    txt_term = jnp.dot(
        doubling_gather(txt_attn, "seq", 0, (2, 1, 4)),
        txt_out_w,
        preferred_element_type=jnp.float32,
    )
    txt_out = transpose_devices(
        halving_scatter(txt_term.astype(jnp.bfloat16).astype(jnp.float32), "tp", 0, (1, 2, 4))
    )
    img_out = lax.psum_scatter(
        img_term.astype(jnp.bfloat16), "tp", scatter_dimension=1, tiled=True
    ).astype(jnp.float32)
    img_gate = lax.dynamic_slice_in_dim(
        img_mod.astype(jnp.float32)[2], tp_at * local_width, local_width
    )
    txt_gate = lax.dynamic_slice_in_dim(
        txt_mod.astype(jnp.float32)[2], tp_at * local_width, local_width
    )
    img_next = (img_hidden.astype(jnp.float32) + img_gate * img_out).astype(jnp.bfloat16)
    text_valid = seq_at * txt_rows + jnp.arange(txt_rows, dtype=jnp.int32) < limit
    txt_base = txt_hidden.astype(jnp.float32)
    txt_next = jnp.where(text_valid[:, None], txt_base + txt_gate * txt_out, txt_base).astype(
        jnp.bfloat16
    )
    shift_row = lax.dynamic_slice_in_dim(final_mod[0], tp_at * local_width, local_width)
    scale_row = lax.dynamic_slice_in_dim(final_mod[1], tp_at * local_width, local_width)
    final_shift = shift_row.astype(jnp.float32)
    final_scale = scale_row.astype(jnp.float32)
    weight_final = final_w.astype(jnp.float32)
    values = img_next.astype(jnp.float32)
    channels = final_w.shape[1]
    final_gain = 1.0 + final_scale
    high = lax.Precision.HIGHEST
    lifted = jnp.dot(values * final_gain, weight_final, precision=high)
    consts = jnp.stack(
        [jnp.dot(final_gain, weight_final, precision=high), jnp.dot(final_shift, weight_final, precision=high)]
    )
    packed = jnp.concatenate(
        [
            jnp.concatenate([lifted, jnp.sum(values, -1)[:, None], jnp.sum(values * values, -1)[:, None]], 1),
            jnp.pad(consts, ((0, 0), (0, 2))),
        ],
        0,
    )
    packed = tree_sum(packed, "tp")
    lifted = packed[:img_rows, :channels]
    row_mean = packed[:img_rows, channels] / full_width
    row_var = packed[:img_rows, channels + 1] / full_width - row_mean * row_mean
    row_scale = lax.rsqrt(row_var + EPS)[:, None]
    patch = row_scale * (lifted - row_mean[:, None] * packed[img_rows, :channels]) + packed[
        img_rows + 1, :channels
    ]
    band_rows = latent.shape[0]
    patch_band = patch.astype(jnp.bfloat16).reshape(band_rows, grid_side * channels)
    rimmed = extended(patch_band, (("seq", 0),), 1)
    col_width = latent.shape[1] // channels
    framed = jnp.pad(rimmed.reshape(band_rows + 2, grid_side, channels), ((0, 0), (1, 1), (0, 0)))
    window = lax.dynamic_slice_in_dim(framed, tp_at * col_width, col_width + 2, 1)
    velocity = jnp.zeros((band_rows, col_width, channels), jnp.float32)
    for row_shift in range(3):
        for col_shift in range(3):
            velocity = velocity + jnp.einsum(
                "rci,io->rco",
                window[row_shift : row_shift + band_rows, col_shift : col_shift + col_width],
                conv_w[row_shift, col_shift],
                preferred_element_type=jnp.float32,
            )
    velocity_flat = velocity.reshape(band_rows, col_width * channels)
    step_f = step_index[0].astype(jnp.float32)
    t_now = 1.0 - step_f / STEPS
    t_after = 1.0 - (step_f + 1.0) / STEPS
    delta = noise_level(t_after) - noise_level(t_now)
    latent_next = latent + delta * velocity_flat
    denoised = latent - noise_level(t_now) * velocity_flat
    return (img_next, txt_next, velocity_flat, latent_next, denoised)


def solution(mesh):
    placed = (
        P(("req", "seq"), "tp"),
        P(("req", "seq"), "tp"),
        P("req", None),
        P("req", None),
        P("seq", None, "tp"),
        P("seq", None, "tp"),
        P(),
        P("tp", "seq"),
        P("tp", "seq"),
        P("req", None),
        P("tp", None),
        P(),
        P(("req", "seq"), "tp"),
        P("req"),
        P("req"),
    )
    return jax.shard_map(
        per_device,
        mesh=mesh,
        in_specs=placed,
        out_specs=(
            P(("req", "seq"), "tp"),
            P(("req", "seq"), "tp"),
            P(("req", "seq"), "tp"),
            P(("req", "seq"), "tp"),
            P(("req", "seq"), "tp"),
        ),
        check_vma=False,
    )
```

```python
import functools
import math

import jax
import jax.numpy as jnp
from jax import lax
from jax.experimental import pallas as pl
from jax.sharding import PartitionSpec as P

STEPS = 28


EPS = 1e-06
SHIFT_MU = 1.15
THETA = 10000.0


def extended(block, sides, width):
    for axis, dim in sides:
        count = lax.axis_size(axis)
        forward = [(i, i + 1) for i in range(count - 1)]
        backward = [(target, source) for source, target in forward]
        low = lax.ppermute(
            lax.slice_in_dim(block, block.shape[dim] - width, None, axis=dim), axis, forward
        )
        high = lax.ppermute(lax.slice_in_dim(block, 0, width, axis=dim), axis, backward)
        block = jnp.concatenate([low, block, high], axis=dim)
    return block


def tree_sum(block, axis):
    count = lax.axis_size(axis)
    step = 1
    while step < count:
        block = block + lax.ppermute(block, axis, [(i, i ^ step) for i in range(count)])
        step *= 2
    return block


def halving_sum(block, axis, dim):
    count = lax.axis_size(axis)
    at = lax.axis_index(axis)
    step = count // 2
    while step >= 1:
        half = block.shape[dim] // 2
        low = lax.slice_in_dim(block, 0, half, axis=dim)
        high = lax.slice_in_dim(block, half, None, axis=dim)
        upper = (at // step) % 2 == 1
        kept = jnp.where(upper, high, low)
        sent = jnp.where(upper, low, high)
        block = kept + lax.ppermute(sent, axis, [(i, i ^ step) for i in range(count)])
        step //= 2
    return block


def attend_block(keep_ref, query_ref, tkey_ref, tvalue_ref, ikey_ref, ivalue_ref, out_ref, *, scale):
    query = query_ref[...]
    contract = (((1,), (1,)), ((), ()))
    text_scores = (
        lax.dot_general(query, tkey_ref[...], contract, preferred_element_type=jnp.float32) * scale
    )
    text_scores = jnp.where(keep_ref[...] > 0.5, text_scores, -1e30)
    img_scores = (
        lax.dot_general(query, ikey_ref[...], contract, preferred_element_type=jnp.float32) * scale
    )
    peak = jnp.maximum(
        jnp.max(text_scores, -1, keepdims=True), jnp.max(img_scores, -1, keepdims=True)
    )
    text_weights = jnp.exp(text_scores - peak)
    img_weights = jnp.exp(img_scores - peak)
    summed = jnp.sum(text_weights, -1, keepdims=True) + jnp.sum(img_weights, -1, keepdims=True)
    mixed_v = jnp.dot(
        text_weights.astype(jnp.bfloat16), tvalue_ref[...], preferred_element_type=jnp.float32
    ) + jnp.dot(img_weights.astype(jnp.bfloat16), ivalue_ref[...], preferred_element_type=jnp.float32)
    out_ref[...] = (mixed_v / summed).astype(out_ref.dtype)


def attention(keep, queries, text_kv, img_kv, head_dim, q_tile):
    rows = queries.shape[0]
    text_total = text_kv.shape[0]
    img_total = img_kv.shape[0]
    heads = queries.shape[1] // head_dim
    return pl.pallas_call(
        functools.partial(attend_block, scale=head_dim ** (-0.5)),
        grid=(heads, rows // q_tile),
        in_specs=[
            pl.BlockSpec((1, text_total), lambda h, i: (0, 0)),
            pl.BlockSpec((q_tile, head_dim), lambda h, i: (i, h)),
            pl.BlockSpec((text_total, head_dim), lambda h, i: (0, h)),
            pl.BlockSpec((text_total, head_dim), lambda h, i: (0, h + heads)),
            pl.BlockSpec((img_total, head_dim), lambda h, i: (0, h)),
            pl.BlockSpec((img_total, head_dim), lambda h, i: (0, h + heads)),
        ],
        out_specs=pl.BlockSpec((q_tile, head_dim), lambda h, i: (i, h)),
        out_shape=jax.ShapeDtypeStruct(queries.shape, jnp.bfloat16),
    )(keep, queries, text_kv, text_kv, img_kv, img_kv)


def bit_of(value, step):
    return (value // step) % 2


def doubling_gather(block, axis, dim, order):
    count = lax.axis_size(axis)
    at = lax.axis_index(axis)
    stacked = block[None]
    for step in order:
        other = lax.ppermute(stacked, axis, [(i, i ^ step) for i in range(count)])
        upper = bit_of(at, step) == 1
        stacked = jnp.stack([jnp.where(upper, other, stacked), jnp.where(upper, stacked, other)])
        stacked = stacked.reshape((-1,) + block.shape)
    rank = len(order)
    source = [sum(((p >> k) & 1) * order[k] for k in range(rank)) for p in range(count)]
    place = [source.index(d) for d in range(count)]
    picked = jnp.stack([stacked[p] for p in place], 0)
    moved = jnp.moveaxis(picked, 0, dim)
    shape = list(block.shape)
    shape[dim] *= count
    return moved.reshape(shape)


def halving_scatter(block, axis, dim, order):
    count = lax.axis_size(axis)
    at = lax.axis_index(axis)
    rank = len(order)
    width = block.shape[dim] // count
    pieces = [lax.slice_in_dim(block, d * width, (d + 1) * width, axis=dim) for d in range(count)]
    slots = [sum(((d // order[k]) % 2) << (rank - 1 - k) for k in range(rank)) for d in range(count)]
    arranged = [None] * count
    for d in range(count):
        arranged[slots[d]] = pieces[d]
    block = jnp.concatenate(arranged, dim)
    for step in order:
        half = block.shape[dim] // 2
        low = lax.slice_in_dim(block, 0, half, axis=dim)
        high = lax.slice_in_dim(block, half, None, axis=dim)
        upper = bit_of(at, step) == 1
        kept = jnp.where(upper, high, low)
        sent = jnp.where(upper, low, high)
        moved = lax.ppermute(sent.astype(jnp.bfloat16), axis, [(i, i ^ step) for i in range(count)])
        block = kept + moved.astype(block.dtype)
    return block


def transpose_devices(block):
    side = lax.axis_size("tp")
    swap = [(a * side + b, b * side + a) for a in range(side) for b in range(side)]
    return lax.ppermute(block, ("seq", "tp"), swap)


def modulate(hidden, mod_rows):
    values = hidden.astype(jnp.float32)
    mod_f = mod_rows.astype(jnp.float32)
    row_mean = jnp.mean(values, -1, keepdims=True)
    row_var = jnp.mean((values - row_mean) ** 2, -1, keepdims=True)
    normed = (values - row_mean) * lax.rsqrt(row_var + EPS)
    return (normed * (1.0 + mod_f[1]) + mod_f[0]).astype(jnp.bfloat16)


def rms_gain(values, gain_row):
    return values * lax.rsqrt(jnp.mean(values * values, -1, keepdims=True) + EPS) * gain_row


def rope_angles(row_pos, col_pos, head_dim):
    lead = head_dim // 16
    span = 7 * head_dim // 32
    freq = THETA ** (-jnp.arange(span, dtype=jnp.float32) / span)
    zero_part = jnp.zeros((row_pos.shape[0], lead), jnp.float32)
    return jnp.concatenate(
        [zero_part, row_pos[:, None] * freq[None], col_pos[:, None] * freq[None]], 1
    )


def apply_rope(values, angles):
    count, heads_n, head_dim = values.shape
    pairs = values.reshape(count, heads_n, head_dim // 2, 2)
    first = pairs[..., 0]
    second = pairs[..., 1]
    cosine = jnp.cos(angles)[:, None, :]
    sine = jnp.sin(angles)[:, None, :]
    turned = jnp.stack([first * cosine - second * sine, first * sine + second * cosine], -1)
    return turned.reshape(values.shape)


def split_heads(mixed, gain_q, gain_k, angles):
    head_dim = gain_q.shape[0]
    shaped = mixed.reshape(mixed.shape[0], 3, -1, head_dim)
    query = rms_gain(shaped[:, 0], gain_q)
    keyed = rms_gain(shaped[:, 1], gain_k)
    if angles is not None:
        query = apply_rope(query, angles)
        keyed = apply_rope(keyed, angles)
    return (
        query.astype(jnp.bfloat16),
        keyed.astype(jnp.bfloat16),
        shaped[:, 2].astype(jnp.bfloat16),
    )


def noise_level(tval):
    factor = math.exp(SHIFT_MU)
    return factor * tval / (factor * tval + 1.0 - tval)


def add_rows(normed, piece):
    flat_piece = piece.reshape(piece.shape[0], piece.shape[1] * piece.shape[2])
    return jnp.dot(normed, flat_piece, preferred_element_type=jnp.float32)


def per_device(
    img_hidden,
    txt_hidden,
    img_mod,
    txt_mod,
    img_qkv,
    txt_qkv,
    qk_gains,
    img_out_w,
    txt_out_w,
    final_mod,
    final_w,
    conv_w,
    latent,
    text_len,
    step_index,
):
    seq_count = lax.axis_size("seq")
    seq_at = lax.axis_index("seq")
    tp_at = lax.axis_index("tp")
    img_rows = img_hidden.shape[0]
    txt_rows = txt_hidden.shape[0]
    local_width = img_hidden.shape[1]
    img_full, txt_full = (
        lax.all_gather(img_hidden, "tp", axis=1, tiled=True),
        lax.all_gather(txt_hidden, "tp", axis=1, tiled=True),
    )
    full_width = img_full.shape[1]
    img_norm = modulate(img_full, img_mod)
    txt_norm = modulate(txt_full, txt_mod)
    img_weights = lax.all_gather(img_qkv, "seq", axis=0, tiled=True)
    img_weights, img_out_w = lax.optimization_barrier((img_weights, img_out_w))
    img_out_full = lax.all_gather(img_out_w, "seq", axis=1, tiled=True)
    img_mixed = add_rows(img_norm, img_weights)
    txt_norm, img_norm = lax.optimization_barrier((txt_norm, img_norm))
    txt_norm_rows = lax.all_to_all(txt_norm, "seq", 1, 0, tiled=True)
    txt_mixed = lax.psum_scatter(
        add_rows(txt_norm_rows, txt_qkv).astype(jnp.bfloat16), "seq", scatter_dimension=0, tiled=True
    ).astype(jnp.float32)
    head_dim = qk_gains.shape[1]
    grid_side = latent.shape[0] * seq_count
    token_ids = seq_at * img_rows + jnp.arange(img_rows, dtype=jnp.int32)
    row_pos = (token_ids // grid_side).astype(jnp.float32)
    col_pos = (token_ids % grid_side).astype(jnp.float32)
    angles = rope_angles(row_pos, col_pos, head_dim)
    img_query, img_key, img_value = split_heads(img_mixed, qk_gains[0], qk_gains[1], angles)
    txt_query, txt_key, txt_value = split_heads(txt_mixed, qk_gains[2], qk_gains[3], None)
    local_len = txt_rows + img_rows
    heads_local = img_query.shape[1]
    kv_width = heads_local * head_dim
    queries = jnp.concatenate([txt_query, img_query], 0).reshape(local_len, kv_width)
    img_kv = lax.all_gather(
        jnp.concatenate(
            [img_key.reshape(img_rows, kv_width), img_value.reshape(img_rows, kv_width)], 1
        ),
        "seq",
        axis=0,
        tiled=True,
    )
    text_kv = lax.all_gather(
        jnp.concatenate(
            [txt_key.reshape(txt_rows, kv_width), txt_value.reshape(txt_rows, kv_width)], 1
        ),
        "seq",
        axis=0,
        tiled=True,
    )
    limit = text_len[0]
    keep = (jnp.arange(text_kv.shape[0], dtype=jnp.int32) < limit).astype(jnp.float32)[None, :]
    attn = attention(keep, queries, text_kv, img_kv, head_dim, local_len // 3)
    txt_attn = attn[:txt_rows]
    img_attn = attn[txt_rows:]
    img_term = jnp.dot(
        img_attn,
        img_out_full,
        preferred_element_type=jnp.float32,
    )
    txt_term = jnp.dot(
        doubling_gather(txt_attn, "seq", 0, (2, 1, 4)),
        txt_out_w,
        preferred_element_type=jnp.float32,
    )
    txt_out = transpose_devices(
        halving_scatter(txt_term.astype(jnp.bfloat16).astype(jnp.float32), "tp", 0, (1, 2, 4))
    )
    img_out = lax.psum_scatter(
        img_term.astype(jnp.bfloat16), "tp", scatter_dimension=1, tiled=True
    ).astype(jnp.float32)
    img_gate = lax.dynamic_slice_in_dim(
        img_mod.astype(jnp.float32)[2], tp_at * local_width, local_width
    )
    txt_gate = lax.dynamic_slice_in_dim(
        txt_mod.astype(jnp.float32)[2], tp_at * local_width, local_width
    )
    img_next = (img_hidden.astype(jnp.float32) + img_gate * img_out).astype(jnp.bfloat16)
    text_valid = seq_at * txt_rows + jnp.arange(txt_rows, dtype=jnp.int32) < limit
    txt_base = txt_hidden.astype(jnp.float32)
    txt_next = jnp.where(text_valid[:, None], txt_base + txt_gate * txt_out, txt_base).astype(
        jnp.bfloat16
    )
    shift_row = lax.dynamic_slice_in_dim(final_mod[0], tp_at * local_width, local_width)
    scale_row = lax.dynamic_slice_in_dim(final_mod[1], tp_at * local_width, local_width)
    final_shift = shift_row.astype(jnp.float32)
    final_scale = scale_row.astype(jnp.float32)
    weight_final = final_w.astype(jnp.float32)
    values = img_next.astype(jnp.float32)
    channels = final_w.shape[1]
    final_gain = 1.0 + final_scale
    high = lax.Precision.HIGHEST
    lifted = jnp.dot(values * final_gain, weight_final, precision=high)
    consts = jnp.stack(
        [jnp.dot(final_gain, weight_final, precision=high), jnp.dot(final_shift, weight_final, precision=high)]
    )
    packed = jnp.concatenate(
        [
            jnp.concatenate([lifted, jnp.sum(values, -1)[:, None], jnp.sum(values * values, -1)[:, None]], 1),
            jnp.pad(consts, ((0, 0), (0, 2))),
        ],
        0,
    )
    packed = tree_sum(packed, "tp")
    lifted = packed[:img_rows, :channels]
    row_mean = packed[:img_rows, channels] / full_width
    row_var = packed[:img_rows, channels + 1] / full_width - row_mean * row_mean
    row_scale = lax.rsqrt(row_var + EPS)[:, None]
    patch = row_scale * (lifted - row_mean[:, None] * packed[img_rows, :channels]) + packed[
        img_rows + 1, :channels
    ]
    band_rows = latent.shape[0]
    patch_band = patch.astype(jnp.bfloat16).reshape(band_rows, grid_side * channels)
    rimmed = extended(patch_band, (("seq", 0),), 1)
    col_width = latent.shape[1] // channels
    framed = jnp.pad(rimmed.reshape(band_rows + 2, grid_side, channels), ((0, 0), (1, 1), (0, 0)))
    window = lax.dynamic_slice_in_dim(framed, tp_at * col_width, col_width + 2, 1)
    velocity = jnp.zeros((band_rows, col_width, channels), jnp.float32)
    for row_shift in range(3):
        for col_shift in range(3):
            velocity = velocity + jnp.einsum(
                "rci,io->rco",
                window[row_shift : row_shift + band_rows, col_shift : col_shift + col_width],
                conv_w[row_shift, col_shift],
                preferred_element_type=jnp.float32,
            )
    velocity_flat = velocity.reshape(band_rows, col_width * channels)
    step_f = step_index[0].astype(jnp.float32)
    t_now = 1.0 - step_f / STEPS
    t_after = 1.0 - (step_f + 1.0) / STEPS
    delta = noise_level(t_after) - noise_level(t_now)
    latent_next = latent + delta * velocity_flat
    denoised = latent - noise_level(t_now) * velocity_flat
    return (img_next, txt_next, velocity_flat, latent_next, denoised)


def solution(mesh):
    placed = (
        P(("req", "seq"), "tp"),
        P(("req", "seq"), "tp"),
        P("req", None),
        P("req", None),
        P("seq", None, "tp"),
        P("seq", None, "tp"),
        P(),
        P("tp", "seq"),
        P("tp", "seq"),
        P("req", None),
        P("tp", None),
        P(),
        P(("req", "seq"), "tp"),
        P("req"),
        P("req"),
    )
    return jax.shard_map(
        per_device,
        mesh=mesh,
        in_specs=placed,
        out_specs=(
            P(("req", "seq"), "tp"),
            P(("req", "seq"), "tp"),
            P(("req", "seq"), "tp"),
            P(("req", "seq"), "tp"),
            P(("req", "seq"), "tp"),
        ),
        check_vma=False,
    )
```

```python
import functools
import math

import jax
import jax.numpy as jnp
from jax import lax
from jax.experimental import pallas as pl
from jax.sharding import PartitionSpec as P

STEPS = 28


EPS = 1e-06
SHIFT_MU = 1.15
THETA = 10000.0


def extended(block, sides, width):
    for axis, dim in sides:
        count = lax.axis_size(axis)
        forward = [(i, i + 1) for i in range(count - 1)]
        backward = [(target, source) for source, target in forward]
        low = lax.ppermute(
            lax.slice_in_dim(block, block.shape[dim] - width, None, axis=dim), axis, forward
        )
        high = lax.ppermute(lax.slice_in_dim(block, 0, width, axis=dim), axis, backward)
        block = jnp.concatenate([low, block, high], axis=dim)
    return block


def tree_sum(block, axis):
    count = lax.axis_size(axis)
    step = 1
    while step < count:
        block = block + lax.ppermute(block, axis, [(i, i ^ step) for i in range(count)])
        step *= 2
    return block


def halving_sum(block, axis, dim):
    count = lax.axis_size(axis)
    at = lax.axis_index(axis)
    step = count // 2
    while step >= 1:
        half = block.shape[dim] // 2
        low = lax.slice_in_dim(block, 0, half, axis=dim)
        high = lax.slice_in_dim(block, half, None, axis=dim)
        upper = (at // step) % 2 == 1
        kept = jnp.where(upper, high, low)
        sent = jnp.where(upper, low, high)
        block = kept + lax.ppermute(sent, axis, [(i, i ^ step) for i in range(count)])
        step //= 2
    return block


def attend_block(keep_ref, query_ref, tkey_ref, tvalue_ref, ikey_ref, ivalue_ref, out_ref, *, scale):
    query = query_ref[...]
    contract = (((1,), (1,)), ((), ()))
    text_scores = (
        lax.dot_general(query, tkey_ref[...], contract, preferred_element_type=jnp.float32) * scale
    )
    text_scores = jnp.where(keep_ref[...] > 0.5, text_scores, -1e30)
    img_scores = (
        lax.dot_general(query, ikey_ref[...], contract, preferred_element_type=jnp.float32) * scale
    )
    peak = jnp.maximum(
        jnp.max(text_scores, -1, keepdims=True), jnp.max(img_scores, -1, keepdims=True)
    )
    text_weights = jnp.exp(text_scores - peak)
    img_weights = jnp.exp(img_scores - peak)
    summed = jnp.sum(text_weights, -1, keepdims=True) + jnp.sum(img_weights, -1, keepdims=True)
    mixed_v = jnp.dot(
        text_weights.astype(jnp.bfloat16), tvalue_ref[...], preferred_element_type=jnp.float32
    ) + jnp.dot(img_weights.astype(jnp.bfloat16), ivalue_ref[...], preferred_element_type=jnp.float32)
    out_ref[...] = (mixed_v / summed).astype(out_ref.dtype)


def attention(keep, queries, text_kv, img_kv, head_dim, q_tile):
    rows = queries.shape[0]
    text_total = text_kv.shape[0]
    img_total = img_kv.shape[0]
    heads = queries.shape[1] // head_dim
    return pl.pallas_call(
        functools.partial(attend_block, scale=head_dim ** (-0.5)),
        grid=(heads, rows // q_tile),
        in_specs=[
            pl.BlockSpec((1, text_total), lambda h, i: (0, 0)),
            pl.BlockSpec((q_tile, head_dim), lambda h, i: (i, h)),
            pl.BlockSpec((text_total, head_dim), lambda h, i: (0, h)),
            pl.BlockSpec((text_total, head_dim), lambda h, i: (0, h + heads)),
            pl.BlockSpec((img_total, head_dim), lambda h, i: (0, h)),
            pl.BlockSpec((img_total, head_dim), lambda h, i: (0, h + heads)),
        ],
        out_specs=pl.BlockSpec((q_tile, head_dim), lambda h, i: (i, h)),
        out_shape=jax.ShapeDtypeStruct(queries.shape, jnp.bfloat16),
    )(keep, queries, text_kv, text_kv, img_kv, img_kv)


def bit_of(value, step):
    return (value // step) % 2


def doubling_gather(block, axis, dim, order):
    count = lax.axis_size(axis)
    at = lax.axis_index(axis)
    stacked = block[None]
    for step in order:
        other = lax.ppermute(stacked, axis, [(i, i ^ step) for i in range(count)])
        upper = bit_of(at, step) == 1
        stacked = jnp.stack([jnp.where(upper, other, stacked), jnp.where(upper, stacked, other)])
        stacked = stacked.reshape((-1,) + block.shape)
    rank = len(order)
    source = [sum(((p >> k) & 1) * order[k] for k in range(rank)) for p in range(count)]
    place = [source.index(d) for d in range(count)]
    picked = jnp.stack([stacked[p] for p in place], 0)
    moved = jnp.moveaxis(picked, 0, dim)
    shape = list(block.shape)
    shape[dim] *= count
    return moved.reshape(shape)


def halving_scatter(block, axis, dim, order):
    count = lax.axis_size(axis)
    at = lax.axis_index(axis)
    rank = len(order)
    width = block.shape[dim] // count
    pieces = [lax.slice_in_dim(block, d * width, (d + 1) * width, axis=dim) for d in range(count)]
    slots = [sum(((d // order[k]) % 2) << (rank - 1 - k) for k in range(rank)) for d in range(count)]
    arranged = [None] * count
    for d in range(count):
        arranged[slots[d]] = pieces[d]
    block = jnp.concatenate(arranged, dim)
    for step in order:
        half = block.shape[dim] // 2
        low = lax.slice_in_dim(block, 0, half, axis=dim)
        high = lax.slice_in_dim(block, half, None, axis=dim)
        upper = bit_of(at, step) == 1
        kept = jnp.where(upper, high, low)
        sent = jnp.where(upper, low, high)
        moved = lax.ppermute(sent.astype(jnp.bfloat16), axis, [(i, i ^ step) for i in range(count)])
        block = kept + moved.astype(block.dtype)
    return block


def transpose_devices(block):
    side = lax.axis_size("tp")
    swap = [(a * side + b, b * side + a) for a in range(side) for b in range(side)]
    return lax.ppermute(block, ("seq", "tp"), swap)


def modulate(hidden, mod_rows):
    values = hidden.astype(jnp.float32)
    mod_f = mod_rows.astype(jnp.float32)
    row_mean = jnp.mean(values, -1, keepdims=True)
    row_var = jnp.mean((values - row_mean) ** 2, -1, keepdims=True)
    normed = (values - row_mean) * lax.rsqrt(row_var + EPS)
    return (normed * (1.0 + mod_f[1]) + mod_f[0]).astype(jnp.bfloat16)


def rms_gain(values, gain_row):
    return values * lax.rsqrt(jnp.mean(values * values, -1, keepdims=True) + EPS) * gain_row


def rope_angles(row_pos, col_pos, head_dim):
    lead = head_dim // 16
    span = 7 * head_dim // 32
    freq = THETA ** (-jnp.arange(span, dtype=jnp.float32) / span)
    zero_part = jnp.zeros((row_pos.shape[0], lead), jnp.float32)
    return jnp.concatenate(
        [zero_part, row_pos[:, None] * freq[None], col_pos[:, None] * freq[None]], 1
    )


def apply_rope(values, angles):
    count, heads_n, head_dim = values.shape
    pairs = values.reshape(count, heads_n, head_dim // 2, 2)
    first = pairs[..., 0]
    second = pairs[..., 1]
    cosine = jnp.cos(angles)[:, None, :]
    sine = jnp.sin(angles)[:, None, :]
    turned = jnp.stack([first * cosine - second * sine, first * sine + second * cosine], -1)
    return turned.reshape(values.shape)


def split_heads(mixed, gain_q, gain_k, angles):
    head_dim = gain_q.shape[0]
    shaped = mixed.reshape(mixed.shape[0], 3, -1, head_dim)
    query = rms_gain(shaped[:, 0], gain_q)
    keyed = rms_gain(shaped[:, 1], gain_k)
    if angles is not None:
        query = apply_rope(query, angles)
        keyed = apply_rope(keyed, angles)
    return (
        query.astype(jnp.bfloat16),
        keyed.astype(jnp.bfloat16),
        shaped[:, 2].astype(jnp.bfloat16),
    )


def noise_level(tval):
    factor = math.exp(SHIFT_MU)
    return factor * tval / (factor * tval + 1.0 - tval)


def add_rows(normed, piece):
    flat_piece = piece.reshape(piece.shape[0], piece.shape[1] * piece.shape[2])
    return jnp.dot(normed, flat_piece, preferred_element_type=jnp.float32)


def per_device(
    img_hidden,
    txt_hidden,
    img_mod,
    txt_mod,
    img_qkv,
    txt_qkv,
    qk_gains,
    img_out_w,
    txt_out_w,
    final_mod,
    final_w,
    conv_w,
    latent,
    text_len,
    step_index,
):
    seq_count = lax.axis_size("seq")
    seq_at = lax.axis_index("seq")
    tp_at = lax.axis_index("tp")
    img_rows = img_hidden.shape[0]
    txt_rows = txt_hidden.shape[0]
    local_width = img_hidden.shape[1]
    img_full, txt_full = (
        lax.all_gather(img_hidden, "tp", axis=1, tiled=True),
        lax.all_gather(txt_hidden, "tp", axis=1, tiled=True),
    )
    full_width = img_full.shape[1]
    img_norm = modulate(img_full, img_mod)
    txt_norm = modulate(txt_full, txt_mod)
    img_weights = lax.all_gather(img_qkv, "seq", axis=0, tiled=True)
    img_weights, img_out_w = lax.optimization_barrier((img_weights, img_out_w))
    img_out_full = lax.all_gather(img_out_w, "seq", axis=1, tiled=True)
    img_mixed = add_rows(img_norm, img_weights)
    txt_norm, img_norm = lax.optimization_barrier((txt_norm, img_norm))
    txt_norm_rows = lax.all_to_all(txt_norm, "seq", 1, 0, tiled=True)
    txt_mixed = lax.psum_scatter(
        add_rows(txt_norm_rows, txt_qkv).astype(jnp.bfloat16), "seq", scatter_dimension=0, tiled=True
    ).astype(jnp.float32)
    head_dim = qk_gains.shape[1]
    grid_side = latent.shape[0] * seq_count
    token_ids = seq_at * img_rows + jnp.arange(img_rows, dtype=jnp.int32)
    row_pos = (token_ids // grid_side).astype(jnp.float32)
    col_pos = (token_ids % grid_side).astype(jnp.float32)
    angles = rope_angles(row_pos, col_pos, head_dim)
    img_query, img_key, img_value = split_heads(img_mixed, qk_gains[0], qk_gains[1], angles)
    txt_query, txt_key, txt_value = split_heads(txt_mixed, qk_gains[2], qk_gains[3], None)
    local_len = txt_rows + img_rows
    heads_local = img_query.shape[1]
    kv_width = heads_local * head_dim
    queries = jnp.concatenate([txt_query, img_query], 0).reshape(local_len, kv_width)
    img_kv = lax.all_gather(
        jnp.concatenate(
            [img_key.reshape(img_rows, kv_width), img_value.reshape(img_rows, kv_width)], 1
        ),
        "seq",
        axis=0,
        tiled=True,
    )
    text_kv = lax.all_gather(
        jnp.concatenate(
            [txt_key.reshape(txt_rows, kv_width), txt_value.reshape(txt_rows, kv_width)], 1
        ),
        "seq",
        axis=0,
        tiled=True,
    )
    limit = text_len[0]
    keep = (jnp.arange(text_kv.shape[0], dtype=jnp.int32) < limit).astype(jnp.float32)[None, :]
    attn = attention(keep, queries, text_kv, img_kv, head_dim, local_len // 3)
    txt_attn = attn[:txt_rows]
    img_attn = attn[txt_rows:]
    img_term = jnp.dot(
        img_attn,
        img_out_full,
        preferred_element_type=jnp.float32,
    )
    txt_term = jnp.dot(
        doubling_gather(txt_attn, "seq", 0, (2, 1, 4)),
        txt_out_w,
        preferred_element_type=jnp.float32,
    )
    txt_out = transpose_devices(
        halving_scatter(txt_term.astype(jnp.bfloat16).astype(jnp.float32), "tp", 0, (1, 2, 4)).astype(
            jnp.bfloat16
        )
    ).astype(jnp.float32)
    img_out = lax.psum_scatter(
        img_term.astype(jnp.bfloat16), "tp", scatter_dimension=1, tiled=True
    ).astype(jnp.float32)
    img_gate = lax.dynamic_slice_in_dim(
        img_mod.astype(jnp.float32)[2], tp_at * local_width, local_width
    )
    txt_gate = lax.dynamic_slice_in_dim(
        txt_mod.astype(jnp.float32)[2], tp_at * local_width, local_width
    )
    img_next = (img_hidden.astype(jnp.float32) + img_gate * img_out).astype(jnp.bfloat16)
    text_valid = seq_at * txt_rows + jnp.arange(txt_rows, dtype=jnp.int32) < limit
    txt_base = txt_hidden.astype(jnp.float32)
    txt_next = jnp.where(text_valid[:, None], txt_base + txt_gate * txt_out, txt_base).astype(
        jnp.bfloat16
    )
    shift_row = lax.dynamic_slice_in_dim(final_mod[0], tp_at * local_width, local_width)
    scale_row = lax.dynamic_slice_in_dim(final_mod[1], tp_at * local_width, local_width)
    final_shift = shift_row.astype(jnp.float32)
    final_scale = scale_row.astype(jnp.float32)
    weight_final = final_w.astype(jnp.float32)
    values = img_next.astype(jnp.float32)
    channels = final_w.shape[1]
    final_gain = 1.0 + final_scale
    high = lax.Precision.HIGHEST
    lifted = jnp.dot(values * final_gain, weight_final, precision=high)
    consts = jnp.stack(
        [jnp.dot(final_gain, weight_final, precision=high), jnp.dot(final_shift, weight_final, precision=high)]
    )
    packed = jnp.concatenate(
        [
            jnp.concatenate([lifted, jnp.sum(values, -1)[:, None], jnp.sum(values * values, -1)[:, None]], 1),
            jnp.pad(consts, ((0, 0), (0, 2))),
        ],
        0,
    )
    packed = tree_sum(packed, "tp")
    lifted = packed[:img_rows, :channels]
    row_mean = packed[:img_rows, channels] / full_width
    row_var = packed[:img_rows, channels + 1] / full_width - row_mean * row_mean
    row_scale = lax.rsqrt(row_var + EPS)[:, None]
    patch = row_scale * (lifted - row_mean[:, None] * packed[img_rows, :channels]) + packed[
        img_rows + 1, :channels
    ]
    band_rows = latent.shape[0]
    patch_band = patch.astype(jnp.bfloat16).reshape(band_rows, grid_side * channels)
    rimmed = extended(patch_band, (("seq", 0),), 1)
    col_width = latent.shape[1] // channels
    framed = jnp.pad(rimmed.reshape(band_rows + 2, grid_side, channels), ((0, 0), (1, 1), (0, 0)))
    window = lax.dynamic_slice_in_dim(framed, tp_at * col_width, col_width + 2, 1)
    velocity = jnp.zeros((band_rows, col_width, channels), jnp.float32)
    for row_shift in range(3):
        for col_shift in range(3):
            velocity = velocity + jnp.einsum(
                "rci,io->rco",
                window[row_shift : row_shift + band_rows, col_shift : col_shift + col_width],
                conv_w[row_shift, col_shift],
                preferred_element_type=jnp.float32,
            )
    velocity_flat = velocity.reshape(band_rows, col_width * channels)
    step_f = step_index[0].astype(jnp.float32)
    t_now = 1.0 - step_f / STEPS
    t_after = 1.0 - (step_f + 1.0) / STEPS
    delta = noise_level(t_after) - noise_level(t_now)
    latent_next = latent + delta * velocity_flat
    denoised = latent - noise_level(t_now) * velocity_flat
    return (img_next, txt_next, velocity_flat, latent_next, denoised)


def solution(mesh):
    placed = (
        P(("req", "seq"), "tp"),
        P(("req", "seq"), "tp"),
        P("req", None),
        P("req", None),
        P("seq", None, "tp"),
        P("seq", None, "tp"),
        P(),
        P("tp", "seq"),
        P("tp", "seq"),
        P("req", None),
        P("tp", None),
        P(),
        P(("req", "seq"), "tp"),
        P("req"),
        P("req"),
    )
    return jax.shard_map(
        per_device,
        mesh=mesh,
        in_specs=placed,
        out_specs=(
            P(("req", "seq"), "tp"),
            P(("req", "seq"), "tp"),
            P(("req", "seq"), "tp"),
            P(("req", "seq"), "tp"),
            P(("req", "seq"), "tp"),
        ),
        check_vma=False,
    )
```
